128 devices in a mesh: lon: 8 (over x, core), lat: 16 (over y, z).
Axes of the slice: x: 4, y: 4, z: 4, core: 2. Of those that a mesh axis runs over, the one named last changes fastest.
Arguments:
- tracers: float32 [2, 20, 1024, 3072], P(None, None, 'lat', 'lon'), may hold values from -6 to 6
- east_velocity: bfloat16 [20, 1024, 3072], P(None, 'lat', 'lon'), may hold values from -3 to 3
- north_velocity: bfloat16 [20, 1024, 3072], P(None, 'lat', 'lon'), may hold values from -3 to 3
- vertical_diffusivity: bfloat16 [20, 1024, 3072], P(None, 'lat', 'lon'), may hold values from 0.049804688 to 5
- depth_levels: int32 [1024, 3072], P('lat', 'lon'), may hold values from 0 to 20
- ocean_blocks: int32 [32, 16], P('lat', 'lon'), may hold values 0 or 1
- forcing: float32 [1024, 3072], P('lat', 'lon'), may hold values from -6 to 6
- surface_coupling: float32 [1024, 3072], P('lat', 'lon'), may hold values from 0.1 to 2
Outputs:
- new_tracers: float32 [2, 20, 1024, 3072], P(None, None, 'lat', 'lon')
- surface_solution: float32 [1024, 3072], P('lat', 'lon')
The draws below stay inside these ranges and needn't reach their ends.
All inputs are finite; a program needn't handle non-finite values. No bound on the sum of `ocean_blocks` on one device may be relied on, other than what follows from the above.
Results may differ from the reference program's by a relative error of at most 0.0003.
Values sent between devices are 32-bit elements; how exact they have to be, the bound alone decides.
No kernel may reach another device: no remote copies, remote signals or barrier semaphores. Data moves between devices by JAX's collectives and lax.ppermute only.
A program may use at most 192 MiB of HBM per device.

```python
import math
import jax
import jax.numpy as jnp
from jax import lax

LEV = 20
NTRA = 2
ITERS = 3
NX = 3072
NY = 1024
NBX = 16
NBY = 32


def plant(values, rng, low, top_value):
    longest = values.shape.index(max(values.shape))
    spots = []
    for shift in (0, 1):
        where = [jax.random.randint(jax.random.fold_in(rng, axis), (), 0, length) for axis, length in enumerate(values.shape)]
        where[longest] = (where[longest] + shift) % values.shape[longest]
        spots.append(tuple(where))
    return values.at[spots[0]].set(low).at[spots[1]].set(top_value)


def shard_levels(rng, dims, cuts, smallest, largest):
    level, own = 1.0, jax.random.fold_in(rng, 6)
    for position, parts in cuts:
        steps = jnp.exp(jax.random.uniform(jax.random.fold_in(own, position), (parts,), jnp.float32, smallest / len(cuts), largest / len(cuts)))
        level = level * jnp.repeat(steps, dims[position] // parts).reshape([-1 if axis == position else 1 for axis in range(len(dims))])
    return level


def normal_values(key, extent, deviation, bound, shards=(), held_as=jnp.bfloat16):
    values = deviation * jax.random.normal(key, extent, jnp.float32)
    if shards:
        values = values * shard_levels(key, extent, shards, -0.22, 0.18)
    return jnp.clip(values, -bound, bound).astype(held_as)


def setup_inputs(seed: int = 0) -> dict:
    splits = jax.random.split(jax.random.key(seed), 9)
    return {
        "tracers": normal_values(splits[0], (NTRA, LEV, NY, NX), 1.0, 6.0, ((2, 16), (3, 8)), jnp.float32),
        "east_velocity": normal_values(splits[1], (LEV, NY, NX), 0.5, 3.0, ((1, 16), (2, 8))),
        "north_velocity": normal_values(splits[2], (LEV, NY, NX), 0.5, 3.0, ((1, 16), (2, 8))),
        "vertical_diffusivity": jnp.clip(jnp.exp(math.log(5.0) - 4.609084 * jax.random.uniform(splits[3], (LEV, NY, NX), jnp.float32) ** shard_levels(splits[3], (LEV, NY, NX), ((1, 16), (2, 8)), -0.2, 0.2)), 0.049804688, 5.0).astype(jnp.bfloat16),
        "depth_levels": plant(jax.random.randint(splits[4], (NY, NX), 0, LEV + 1), jax.random.fold_in(splits[4], 1), 0, LEV).astype(jnp.int32),
        "ocean_blocks": plant((jax.random.randint(splits[5], (NBY, NBX), 0, 4) < 3).astype(jnp.int32), jax.random.fold_in(splits[5], 1), 0, 1),
        "forcing": normal_values(splits[6], (NY, NX), 1.0, 6.0, ((0, 16), (1, 8)), jnp.float32),
        "surface_coupling": jnp.clip(jnp.exp(math.log(2.0) - 2.9957323 * jax.random.uniform(splits[7], (NY, NX), jnp.float32) ** shard_levels(splits[7], (NY, NX), ((0, 16), (1, 8)), -0.2, 0.2)), 0.1, 2.0),
    }


advection_rate = 0.25
biharmonic_rate = 0.01
corner_weight = 0.5


def window(array, shift_row, shift_col):
    inner_height = array.shape[-2] - 2
    inner_width = array.shape[-1] - 2
    return array[..., shift_row:shift_row + inner_height, shift_col:shift_col + inner_width]


def masked_laplacian(values, wet_mask):
    centre = window(values, 1, 1)
    running = jnp.zeros_like(centre)
    for shift_row, shift_col in ((0, 1), (2, 1), (1, 0), (1, 2)):
        running = running + window(wet_mask, shift_row, shift_col) * (window(values, shift_row, shift_col) - centre)
    return window(wet_mask, 1, 1) * running


def face_flux(speed_one, speed_two, tracer_one, tracer_two, wet_one, wet_two):
    return 0.5 * (speed_one + speed_two) * 0.5 * (tracer_one + tracer_two) * wet_one * wet_two


def baroclinic(padded):
    tracer = padded[0:2]
    wet_mask = padded[2]
    inner_tracer = tracer[..., 1:-1, 1:-1]
    inner_mask = wet_mask[..., 1:-1, 1:-1]
    east_speed = padded[3][..., 1:-1, 1:-1]
    north_speed = padded[4][..., 1:-1, 1:-1]
    lap_one = masked_laplacian(tracer, wet_mask)
    lap_two = masked_laplacian(lap_one, inner_mask)
    centre = window(inner_tracer, 1, 1)
    wet_centre = window(inner_mask, 1, 1)
    east_flux = face_flux(window(east_speed, 1, 1), window(east_speed, 1, 2), centre, window(inner_tracer, 1, 2), wet_centre, window(inner_mask, 1, 2))
    west_flux = face_flux(window(east_speed, 1, 0), window(east_speed, 1, 1), window(inner_tracer, 1, 0), centre, window(inner_mask, 1, 0), wet_centre)
    north_flux = face_flux(window(north_speed, 1, 1), window(north_speed, 2, 1), centre, window(inner_tracer, 2, 1), wet_centre, window(inner_mask, 2, 1))
    south_flux = face_flux(window(north_speed, 0, 1), window(north_speed, 1, 1), window(inner_tracer, 0, 1), centre, window(inner_mask, 0, 1), wet_centre)
    divergence = east_flux - west_flux + north_flux - south_flux
    return wet_centre * (centre - advection_rate * divergence - biharmonic_rate * lap_two)


def vertical_mix(values, wet_mask, diffusivity):
    level_count = wet_mask.shape[0]
    zeros_plane = jnp.zeros_like(wet_mask[0])
    coupling = [zeros_plane] + [diffusivity[k] * wet_mask[k] * wet_mask[k - 1] for k in range(1, level_count)] + [zeros_plane]
    upper_ratio = []
    reduced = []
    for k in range(level_count):
        diagonal = 1.0 + coupling[k] + coupling[k + 1]
        if k == 0:
            divisor = diagonal
            source = values[:, 0]
        else:
            divisor = diagonal + coupling[k] * upper_ratio[k - 1]
            source = values[:, k] + coupling[k] * reduced[k - 1]
        upper_ratio.append(-coupling[k + 1] / divisor)
        reduced.append(source / divisor)
    result = [reduced[-1]]
    for k in range(level_count - 2, -1, -1):
        result.insert(0, reduced[k] - upper_ratio[k] * result[0])
    return jnp.stack(result, axis=1)


def nine_point(padded, wet_surface, centre_weight):
    centre = window(padded, 1, 1)
    edges = window(padded, 0, 1) + window(padded, 2, 1) + window(padded, 1, 0) + window(padded, 1, 2)
    corners = window(padded, 0, 0) + window(padded, 0, 2) + window(padded, 2, 0) + window(padded, 2, 2)
    return wet_surface * (centre_weight * centre - edges - corner_weight * corners)


def fold_pad(array, margin, fold_signs):
    widened = jnp.concatenate([array[..., -margin:], array, array[..., :margin]], axis=-1)
    southern = jnp.zeros(widened.shape[:-2] + (margin, widened.shape[-1]), widened.dtype)
    northern = jnp.flip(widened[..., -margin:, :], axis=(-2, -1)) * fold_signs
    return jnp.concatenate([southern, widened, northern], axis=-2)


def reference(tracers, east_velocity, north_velocity, vertical_diffusivity, depth_levels, ocean_blocks, forcing, surface_coupling):
    ocean_cells = jnp.repeat(jnp.repeat(ocean_blocks, NY // NBY, axis=0), NX // NBX, axis=1).astype(jnp.float32)
    fold_signs = jnp.array([1.0, 1.0, 1.0, -1.0, -1.0], jnp.float32).reshape(5, 1, 1)

    def level_update(k):
        tracer_level = lax.dynamic_index_in_dim(tracers, k, 1, keepdims=False)
        wet_level = jnp.where(k < depth_levels, ocean_cells, jnp.zeros_like(ocean_cells))
        east_level = lax.dynamic_index_in_dim(east_velocity, k, 0, keepdims=False).astype(jnp.float32)
        north_level = lax.dynamic_index_in_dim(north_velocity, k, 0, keepdims=False).astype(jnp.float32)
        stacked = jnp.concatenate([tracer_level, wet_level[None], east_level[None], north_level[None]], axis=0)
        return baroclinic(fold_pad(stacked, 2, fold_signs)), wet_level

    provisional, wet_mask = lax.map(level_update, jnp.arange(LEV, dtype=jnp.int32))
    provisional = jnp.moveaxis(provisional, 0, 1)
    new_tracers = vertical_mix(provisional, wet_mask, vertical_diffusivity.astype(jnp.float32))
    wet_surface = wet_mask[0]
    surface_source = wet_surface * (forcing + jnp.mean(new_tracers[0] - new_tracers[1], axis=0))
    centre_weight = 6.0 + surface_coupling

    def apply_operator(surface_field):
        return nine_point(fold_pad(surface_field, 1, 1.0), wet_surface, centre_weight)

    solution = jnp.zeros_like(surface_source)
    residual = surface_source
    precond = wet_surface * residual / centre_weight
    direction = precond
    resid_dot = jnp.sum(residual * precond)
    for iteration in range(ITERS):
        operator_image = apply_operator(direction)
        step_size = resid_dot / jnp.sum(direction * operator_image)
        solution = solution + step_size * direction
        if iteration + 1 < ITERS:
            residual = residual - step_size * operator_image
            precond = wet_surface * residual / centre_weight
            dot_next = jnp.sum(residual * precond)
            direction = precond + (dot_next / resid_dot) * direction
            resid_dot = dot_next
    return new_tracers, solution
```

```python
import jax
import jax.numpy as jnp
from jax import lax
from jax.sharding import PartitionSpec as P

ITERS = 3


advection_rate = 0.25
biharmonic_rate = 0.01
corner_weight = 0.5


def extended_2(block, sides, width, periodic):
    for axis, dim in sides:
        count = lax.axis_size(axis)
        forward = [(i, i + 1) for i in range(count - 1)]
        if periodic:
            forward.append((count - 1, 0))
        backward = [(target, source) for source, target in forward]
        low = lax.ppermute(
            lax.slice_in_dim(block, block.shape[dim] - width, None, axis=dim), axis, forward
        )
        high = lax.ppermute(lax.slice_in_dim(block, 0, width, axis=dim), axis, backward)
        block = jnp.concatenate([low, block, high], axis=dim)
    return block


def from_partner(block, axis, stride):
    count = lax.axis_size(axis)
    route = []
    for low in range(count):
        high = low | 1 << stride
        if high != low and high < count:
            route += [(low, high), (high, low)]
    return lax.ppermute(block, axis, route)


def passed_along(value, axis, steps):
    count = lax.axis_size(axis)
    pairs = [(source, (source + steps) % count) for source in range(count)]
    return lax.ppermute(value, axis, pairs)


def shifted(shard, axis, by):
    count = lax.axis_size(axis)
    pairs = [(i, i + by) for i in range(count) if 0 <= i + by < count]
    return lax.ppermute(shard, axis, pairs)


def window(array, shift_row, shift_col):
    inner_height = array.shape[-2] - 2
    inner_width = array.shape[-1] - 2
    return array[..., shift_row : shift_row + inner_height, shift_col : shift_col + inner_width]


def masked_laplacian(values, wet_mask):
    centre = window(values, 1, 1)
    running = jnp.zeros_like(centre)
    for shift_row, shift_col in ((0, 1), (2, 1), (1, 0), (1, 2)):
        running = running + window(wet_mask, shift_row, shift_col) * (
            window(values, shift_row, shift_col) - centre
        )
    return window(wet_mask, 1, 1) * running


def face_flux(speed_one, speed_two, tracer_one, tracer_two, wet_one, wet_two):
    return 0.5 * (speed_one + speed_two) * 0.5 * (tracer_one + tracer_two) * wet_one * wet_two


def baroclinic(padded):
    tracer = padded[0:2]
    wet_mask = padded[2]
    inner_tracer = tracer[..., 1:-1, 1:-1]
    inner_mask = wet_mask[..., 1:-1, 1:-1]
    east_speed = padded[3][..., 1:-1, 1:-1]
    north_speed = padded[4][..., 1:-1, 1:-1]
    lap_one = masked_laplacian(tracer, wet_mask)
    lap_two = masked_laplacian(lap_one, inner_mask)
    centre = window(inner_tracer, 1, 1)
    wet_centre = window(inner_mask, 1, 1)
    east_flux = face_flux(
        window(east_speed, 1, 1),
        window(east_speed, 1, 2),
        centre,
        window(inner_tracer, 1, 2),
        wet_centre,
        window(inner_mask, 1, 2),
    )
    west_flux = face_flux(
        window(east_speed, 1, 0),
        window(east_speed, 1, 1),
        window(inner_tracer, 1, 0),
        centre,
        window(inner_mask, 1, 0),
        wet_centre,
    )
    north_flux = face_flux(
        window(north_speed, 1, 1),
        window(north_speed, 2, 1),
        centre,
        window(inner_tracer, 2, 1),
        wet_centre,
        window(inner_mask, 2, 1),
    )
    south_flux = face_flux(
        window(north_speed, 0, 1),
        window(north_speed, 1, 1),
        window(inner_tracer, 0, 1),
        centre,
        window(inner_mask, 0, 1),
        wet_centre,
    )
    divergence = east_flux - west_flux + north_flux - south_flux
    return wet_centre * (centre - advection_rate * divergence - biharmonic_rate * lap_two)


def vertical_mix(values, wet_mask, diffusivity):
    level_count = wet_mask.shape[0]
    zeros_plane = jnp.zeros_like(wet_mask[0])
    coupling = (
        [zeros_plane]
        + [diffusivity[k] * wet_mask[k] * wet_mask[k - 1] for k in range(1, level_count)]
        + [zeros_plane]
    )
    upper_ratio = []
    reduced = []
    for k in range(level_count):
        diagonal = 1.0 + coupling[k] + coupling[k + 1]
        if k == 0:
            divisor = diagonal
            source = values[:, 0]
        else:
            divisor = diagonal + coupling[k] * upper_ratio[k - 1]
            source = values[:, k] + coupling[k] * reduced[k - 1]
        upper_ratio.append(-coupling[k + 1] / divisor)
        reduced.append(source / divisor)
    result = [reduced[-1]]
    for k in range(level_count - 2, -1, -1):
        result.insert(0, reduced[k] - upper_ratio[k] * result[0])
    return jnp.stack(result, axis=1)


def nine_point(padded, wet_surface, centre_weight):
    centre = window(padded, 1, 1)
    edges = (
        window(padded, 0, 1) + window(padded, 2, 1) + window(padded, 1, 0) + window(padded, 1, 2)
    )
    corners = (
        window(padded, 0, 0) + window(padded, 0, 2) + window(padded, 2, 0) + window(padded, 2, 2)
    )
    return wet_surface * (centre_weight * centre - edges - corner_weight * corners)


def clinic_extend(stacked, fold_signs):
    row_count = stacked.shape[2]
    widened = extended_2(stacked, (("lon", 3),), 2, True)
    extended = extended_2(widened, (("lat", 2),), 2, False)
    top_rows = widened[:, :, row_count - 2 :, :]
    for bit in range(lax.axis_size("lon").bit_length() - 1):
        top_rows = from_partner(top_rows, "lon", bit)
    northern = jnp.flip(top_rows, axis=(2, 3)) * fold_signs
    at_top = lax.axis_index("lat") == lax.axis_size("lat") - 1
    ghost_rows = jnp.where(at_top, northern, extended[:, :, row_count + 2 :, :])
    return jnp.concatenate([extended[:, :, : row_count + 2, :], ghost_rows], axis=2)


def strip_pad(surface_field):
    lon_index = lax.axis_index("lon")
    lon_count = lax.axis_size("lon")
    first_row = surface_field[0:1, :]
    last_row = surface_field[-1:, :]
    following = passed_along(first_row, "lon", -1)
    following_far = shifted(following, "lat", -1)
    preceding = passed_along(last_row, "lon", 1)
    preceding_far = shifted(preceding, "lat", 1)
    above_row = jnp.where(lon_index == lon_count - 1, following_far, following)
    below_row = jnp.where(lon_index == 0, preceding_far, preceding)
    top_strip = jnp.logical_and(
        lon_index == lon_count - 1, lax.axis_index("lat") == lax.axis_size("lat") - 1
    )
    above_row = jnp.where(top_strip, jnp.flip(last_row, axis=1), above_row)
    extended = jnp.concatenate([below_row, surface_field, above_row], axis=0)
    return jnp.concatenate([extended[:, -1:], extended, extended[:, :1]], axis=1)


def butterfly_sum(value):
    for axis in ("lon", "lat"):
        count = lax.axis_size(axis)
        bit = 1
        while bit < count:
            value = value + lax.ppermute(value, axis, [(i, i ^ bit) for i in range(count)])
            bit <<= 1
    return value


def residual_total(residual, precond):
    return butterfly_sum(jnp.sum(residual * precond))


def solve(surface_source, wet_surface, centre_weight, padder):

    def precondition(residual):
        return wet_surface * residual / centre_weight

    solution = jnp.zeros_like(surface_source)
    residual = surface_source
    precond = precondition(residual)
    direction = precond
    resid_dot = None
    for iteration in range(ITERS):
        operator_image = nine_point(padder(direction), wet_surface, centre_weight)
        curvature = jnp.sum(direction * operator_image)
        if resid_dot is None:
            both = butterfly_sum(jnp.stack([jnp.sum(residual * precond), curvature]))
            resid_dot, curvature = both[0], both[1]
        else:
            curvature = butterfly_sum(curvature)
        step_size = resid_dot / curvature
        solution = solution + step_size * direction
        if iteration + 1 < ITERS:
            residual = residual - step_size * operator_image
            precond = precondition(residual)
            dot_next = residual_total(residual, precond)
            direction = precond + dot_next / resid_dot * direction
            resid_dot = dot_next
    return solution


def shards(
    tracers,
    east_velocity,
    north_velocity,
    vertical_diffusivity,
    depth_levels,
    ocean_blocks,
    forcing,
    surface_coupling,
):
    level_count = tracers.shape[1]
    row_count = tracers.shape[2]
    col_count = tracers.shape[3]
    ocean_cells = jnp.repeat(
        jnp.repeat(ocean_blocks, row_count // ocean_blocks.shape[0], axis=0),
        col_count // ocean_blocks.shape[1],
        axis=1,
    ).astype(jnp.float32)
    level_index = lax.broadcasted_iota(jnp.int32, (level_count, row_count, col_count), 0)
    wet_mask = jnp.where(
        level_index < depth_levels[None], ocean_cells[None], jnp.zeros_like(ocean_cells)[None]
    )
    east_float = east_velocity.astype(jnp.float32)
    north_float = north_velocity.astype(jnp.float32)
    stacked = jnp.concatenate(
        [tracers, wet_mask[None], east_float[None], north_float[None]], axis=0
    )
    fold_signs = jnp.array([1.0, 1.0, 1.0, -1.0, -1.0], jnp.float32).reshape(5, 1, 1, 1)
    padded = clinic_extend(stacked, fold_signs)
    provisional = baroclinic(padded)
    new_tracers = vertical_mix(provisional, wet_mask, vertical_diffusivity.astype(jnp.float32))
    wet_surface = wet_mask[0]
    surface_source = wet_surface * (forcing + jnp.mean(new_tracers[0] - new_tracers[1], axis=0))
    centre_weight = 6.0 + surface_coupling
    relaid = lax.all_to_all(
        jnp.stack([surface_source, wet_surface, centre_weight]),
        "lon",
        split_axis=1,
        concat_axis=2,
        tiled=True,
    )
    strip_solution = solve(relaid[0], relaid[1], relaid[2], strip_pad)
    solution = lax.all_to_all(strip_solution, "lon", split_axis=1, concat_axis=0, tiled=True)
    return (new_tracers, solution)


def solution(mesh):
    placed = (
        P(None, None, "lat", "lon"),
        P(None, "lat", "lon"),
        P(None, "lat", "lon"),
        P(None, "lat", "lon"),
        P("lat", "lon"),
        P("lat", "lon"),
        P("lat", "lon"),
        P("lat", "lon"),
    )
    return jax.shard_map(
        shards,
        mesh=mesh,
        in_specs=placed,
        out_specs=(P(None, None, "lat", "lon"), P("lat", "lon")),
        check_vma=False,
    )
```

```python
import jax
import jax.numpy as jnp
from jax import lax
from jax.sharding import PartitionSpec as P
from jax.experimental import pallas as pl
from jax.experimental.pallas import tpu as pltpu

ITERS = 3


advection_rate = 0.25
biharmonic_rate = 0.01
corner_weight = 0.5


def extended_2(block, sides, width, periodic):
    for axis, dim in sides:
        count = lax.axis_size(axis)
        forward = [(i, i + 1) for i in range(count - 1)]
        if periodic:
            forward.append((count - 1, 0))
        backward = [(target, source) for source, target in forward]
        low = lax.ppermute(
            lax.slice_in_dim(block, block.shape[dim] - width, None, axis=dim), axis, forward
        )
        high = lax.ppermute(lax.slice_in_dim(block, 0, width, axis=dim), axis, backward)
        block = jnp.concatenate([low, block, high], axis=dim)
    return block


def from_partner(block, axis, stride):
    count = lax.axis_size(axis)
    route = []
    for low in range(count):
        high = low | 1 << stride
        if high != low and high < count:
            route += [(low, high), (high, low)]
    return lax.ppermute(block, axis, route)


def passed_along(value, axis, steps):
    count = lax.axis_size(axis)
    pairs = [(source, (source + steps) % count) for source in range(count)]
    return lax.ppermute(value, axis, pairs)


def shifted(shard, axis, by):
    count = lax.axis_size(axis)
    pairs = [(i, i + by) for i in range(count) if 0 <= i + by < count]
    return lax.ppermute(shard, axis, pairs)


def window(array, shift_row, shift_col):
    inner_height = array.shape[-2] - 2
    inner_width = array.shape[-1] - 2
    return array[..., shift_row : shift_row + inner_height, shift_col : shift_col + inner_width]


def masked_laplacian(values, wet_mask):
    centre = window(values, 1, 1)
    running = jnp.zeros_like(centre)
    for shift_row, shift_col in ((0, 1), (2, 1), (1, 0), (1, 2)):
        running = running + window(wet_mask, shift_row, shift_col) * (
            window(values, shift_row, shift_col) - centre
        )
    return window(wet_mask, 1, 1) * running


def face_flux(speed_one, speed_two, tracer_one, tracer_two, wet_one, wet_two):
    return 0.5 * (speed_one + speed_two) * 0.5 * (tracer_one + tracer_two) * wet_one * wet_two


def baroclinic(padded):
    tracer = padded[0:2]
    wet_mask = padded[2]
    inner_tracer = tracer[..., 1:-1, 1:-1]
    inner_mask = wet_mask[..., 1:-1, 1:-1]
    east_speed = padded[3][..., 1:-1, 1:-1]
    north_speed = padded[4][..., 1:-1, 1:-1]
    lap_one = masked_laplacian(tracer, wet_mask)
    lap_two = masked_laplacian(lap_one, inner_mask)
    centre = window(inner_tracer, 1, 1)
    wet_centre = window(inner_mask, 1, 1)
    east_flux = face_flux(
        window(east_speed, 1, 1),
        window(east_speed, 1, 2),
        centre,
        window(inner_tracer, 1, 2),
        wet_centre,
        window(inner_mask, 1, 2),
    )
    west_flux = face_flux(
        window(east_speed, 1, 0),
        window(east_speed, 1, 1),
        window(inner_tracer, 1, 0),
        centre,
        window(inner_mask, 1, 0),
        wet_centre,
    )
    north_flux = face_flux(
        window(north_speed, 1, 1),
        window(north_speed, 2, 1),
        centre,
        window(inner_tracer, 2, 1),
        wet_centre,
        window(inner_mask, 2, 1),
    )
    south_flux = face_flux(
        window(north_speed, 0, 1),
        window(north_speed, 1, 1),
        window(inner_tracer, 0, 1),
        centre,
        window(inner_mask, 0, 1),
        wet_centre,
    )
    divergence = east_flux - west_flux + north_flux - south_flux
    return wet_centre * (centre - advection_rate * divergence - biharmonic_rate * lap_two)


def mix_kernel(values_ref, wet_ref, diff_ref, out_ref, ratio_ref):
    level_count = wet_ref.shape[0]
    tracer_count = values_ref.shape[0]

    def coupling(k):
        return diff_ref[k].astype(jnp.float32) * wet_ref[k] * wet_ref[k - 1]

    below = coupling(1)
    upper = None
    reduced = [None] * tracer_count
    for k in range(level_count):
        above = below
        below = coupling(k + 1) if k + 1 < level_count else None
        if k == 0:
            diagonal = 1.0 + below
            divisor = diagonal
        elif below is None:
            diagonal = 1.0 + above
            divisor = diagonal + above * upper
        else:
            diagonal = 1.0 + above + below
            divisor = diagonal + above * upper
        if below is not None:
            upper = -below / divisor
            ratio_ref[k] = upper
        for t in range(tracer_count):
            if k == 0:
                source = values_ref[t, 0]
            else:
                source = values_ref[t, k] + above * reduced[t]
            reduced[t] = source / divisor
            out_ref[t, k] = reduced[t]
    result = reduced
    for k in range(level_count - 2, -1, -1):
        ratio = ratio_ref[k]
        for t in range(tracer_count):
            result[t] = out_ref[t, k] - ratio * result[t]
            out_ref[t, k] = result[t]


def vertical_mix(values, wet_mask, diffusivity):
    tracer_count, level_count, row_count, col_count = values.shape
    rows = 16 if row_count % 16 == 0 else row_count
    return pl.pallas_call(
        mix_kernel,
        grid=(row_count // rows,),
        in_specs=[
            pl.BlockSpec((tracer_count, level_count, rows, col_count), lambda i: (0, 0, i, 0)),
            pl.BlockSpec((level_count, rows, col_count), lambda i: (0, i, 0)),
            pl.BlockSpec((level_count, rows, col_count), lambda i: (0, i, 0)),
        ],
        out_specs=pl.BlockSpec((tracer_count, level_count, rows, col_count), lambda i: (0, 0, i, 0)),
        out_shape=jax.ShapeDtypeStruct(values.shape, jnp.float32),
        scratch_shapes=[pltpu.VMEM((level_count - 1, rows, col_count), jnp.float32)],
    )(values, wet_mask, diffusivity)


def nine_point(padded, wet_surface, centre_weight):
    centre = window(padded, 1, 1)
    edges = (
        window(padded, 0, 1) + window(padded, 2, 1) + window(padded, 1, 0) + window(padded, 1, 2)
    )
    corners = (
        window(padded, 0, 0) + window(padded, 0, 2) + window(padded, 2, 0) + window(padded, 2, 2)
    )
    return wet_surface * (centre_weight * centre - edges - corner_weight * corners)


def clinic_extend(stacked, fold_signs):
    row_count = stacked.shape[2]
    widened = extended_2(stacked, (("lon", 3),), 2, True)
    extended = extended_2(widened, (("lat", 2),), 2, False)
    top_rows = widened[:, :, row_count - 2 :, :]
    for bit in range(lax.axis_size("lon").bit_length() - 1):
        top_rows = from_partner(top_rows, "lon", bit)
    northern = jnp.flip(top_rows, axis=(2, 3)) * fold_signs
    at_top = lax.axis_index("lat") == lax.axis_size("lat") - 1
    ghost_rows = jnp.where(at_top, northern, extended[:, :, row_count + 2 :, :])
    return jnp.concatenate([extended[:, :, : row_count + 2, :], ghost_rows], axis=2)


def strip_pad(surface_field):
    lon_index = lax.axis_index("lon")
    lon_count = lax.axis_size("lon")
    first_row = surface_field[0:1, :]
    last_row = surface_field[-1:, :]
    following = passed_along(first_row, "lon", -1)
    following_far = shifted(following, "lat", -1)
    preceding = passed_along(last_row, "lon", 1)
    preceding_far = shifted(preceding, "lat", 1)
    above_row = jnp.where(lon_index == lon_count - 1, following_far, following)
    below_row = jnp.where(lon_index == 0, preceding_far, preceding)
    top_strip = jnp.logical_and(
        lon_index == lon_count - 1, lax.axis_index("lat") == lax.axis_size("lat") - 1
    )
    above_row = jnp.where(top_strip, jnp.flip(last_row, axis=1), above_row)
    extended = jnp.concatenate([below_row, surface_field, above_row], axis=0)
    return jnp.concatenate([extended[:, -1:], extended, extended[:, :1]], axis=1)


def butterfly_sum(value):
    for axis in ("lon", "lat"):
        count = lax.axis_size(axis)
        bit = 1
        while bit < count:
            value = value + lax.ppermute(value, axis, [(i, i ^ bit) for i in range(count)])
            bit <<= 1
    return value


def residual_total(residual, precond):
    return butterfly_sum(jnp.sum(residual * precond))


def solve(surface_source, wet_surface, centre_weight, padder):

    def precondition(residual):
        return wet_surface * residual / centre_weight

    solution = jnp.zeros_like(surface_source)
    residual = surface_source
    precond = precondition(residual)
    direction = precond
    resid_dot = None
    for iteration in range(ITERS):
        operator_image = nine_point(padder(direction), wet_surface, centre_weight)
        curvature = jnp.sum(direction * operator_image)
        if resid_dot is None:
            both = butterfly_sum(jnp.stack([jnp.sum(residual * precond), curvature]))
            resid_dot, curvature = both[0], both[1]
        else:
            curvature = butterfly_sum(curvature)
        step_size = resid_dot / curvature
        solution = solution + step_size * direction
        if iteration + 1 < ITERS:
            residual = residual - step_size * operator_image
            precond = precondition(residual)
            dot_next = residual_total(residual, precond)
            direction = precond + dot_next / resid_dot * direction
            resid_dot = dot_next
    return solution


def shards(
    tracers,
    east_velocity,
    north_velocity,
    vertical_diffusivity,
    depth_levels,
    ocean_blocks,
    forcing,
    surface_coupling,
):
    level_count = tracers.shape[1]
    row_count = tracers.shape[2]
    col_count = tracers.shape[3]
    ocean_cells = jnp.repeat(
        jnp.repeat(ocean_blocks, row_count // ocean_blocks.shape[0], axis=0),
        col_count // ocean_blocks.shape[1],
        axis=1,
    ).astype(jnp.float32)
    level_index = lax.broadcasted_iota(jnp.int32, (level_count, row_count, col_count), 0)
    wet_mask = jnp.where(
        level_index < depth_levels[None], ocean_cells[None], jnp.zeros_like(ocean_cells)[None]
    )
    east_float = east_velocity.astype(jnp.float32)
    north_float = north_velocity.astype(jnp.float32)
    stacked = jnp.concatenate(
        [tracers, wet_mask[None], east_float[None], north_float[None]], axis=0
    )
    fold_signs = jnp.array([1.0, 1.0, 1.0, -1.0, -1.0], jnp.float32).reshape(5, 1, 1, 1)
    padded = clinic_extend(stacked, fold_signs)
    provisional = baroclinic(padded)
    new_tracers = vertical_mix(provisional, wet_mask, vertical_diffusivity)
    wet_surface = wet_mask[0]
    surface_source = wet_surface * (forcing + jnp.mean(new_tracers[0] - new_tracers[1], axis=0))
    centre_weight = 6.0 + surface_coupling
    relaid = lax.all_to_all(
        jnp.stack([surface_source, wet_surface, centre_weight]),
        "lon",
        split_axis=1,
        concat_axis=2,
        tiled=True,
    )
    strip_solution = solve(relaid[0], relaid[1], relaid[2], strip_pad)
    solution = lax.all_to_all(strip_solution, "lon", split_axis=1, concat_axis=0, tiled=True)
    return (new_tracers, solution)


def solution(mesh):
    placed = (
        P(None, None, "lat", "lon"),
        P(None, "lat", "lon"),
        P(None, "lat", "lon"),
        P(None, "lat", "lon"),
        P("lat", "lon"),
        P("lat", "lon"),
        P("lat", "lon"),
        P("lat", "lon"),
    )
    return jax.shard_map(
        shards,
        mesh=mesh,
        in_specs=placed,
        out_specs=(P(None, None, "lat", "lon"), P("lat", "lon")),
        check_vma=False,
    )
```

```python
import jax
import jax.numpy as jnp
from jax import lax
from jax.sharding import PartitionSpec as P
from jax.experimental import pallas as pl
from jax.experimental.pallas import tpu as pltpu

ITERS = 3


advection_rate = 0.25
biharmonic_rate = 0.01
corner_weight = 0.5


def extended_2(block, sides, width, periodic):
    for axis, dim in sides:
        count = lax.axis_size(axis)
        forward = [(i, i + 1) for i in range(count - 1)]
        if periodic:
            forward.append((count - 1, 0))
        backward = [(target, source) for source, target in forward]
        low = lax.ppermute(
            lax.slice_in_dim(block, block.shape[dim] - width, None, axis=dim), axis, forward
        )
        high = lax.ppermute(lax.slice_in_dim(block, 0, width, axis=dim), axis, backward)
        block = jnp.concatenate([low, block, high], axis=dim)
    return block


def from_partner(block, axis, stride):
    count = lax.axis_size(axis)
    route = []
    for low in range(count):
        high = low | 1 << stride
        if high != low and high < count:
            route += [(low, high), (high, low)]
    return lax.ppermute(block, axis, route)


def passed_along(value, axis, steps):
    count = lax.axis_size(axis)
    pairs = [(source, (source + steps) % count) for source in range(count)]
    return lax.ppermute(value, axis, pairs)


def shifted(shard, axis, by):
    count = lax.axis_size(axis)
    pairs = [(i, i + by) for i in range(count) if 0 <= i + by < count]
    return lax.ppermute(shard, axis, pairs)


def window(array, shift_row, shift_col):
    inner_height = array.shape[-2] - 2
    inner_width = array.shape[-1] - 2
    return array[..., shift_row : shift_row + inner_height, shift_col : shift_col + inner_width]


def masked_laplacian(values, wet_mask):
    centre = window(values, 1, 1)
    running = jnp.zeros_like(centre)
    for shift_row, shift_col in ((0, 1), (2, 1), (1, 0), (1, 2)):
        running = running + window(wet_mask, shift_row, shift_col) * (
            window(values, shift_row, shift_col) - centre
        )
    return window(wet_mask, 1, 1) * running


def face_flux(speed_one, speed_two, tracer_one, tracer_two, wet_one, wet_two):
    return 0.5 * (speed_one + speed_two) * 0.5 * (tracer_one + tracer_two) * wet_one * wet_two


def baroclinic(padded):
    tracer = padded[0:2]
    wet_mask = padded[2]
    inner_tracer = tracer[..., 1:-1, 1:-1]
    inner_mask = wet_mask[..., 1:-1, 1:-1]
    east_speed = padded[3][..., 1:-1, 1:-1]
    north_speed = padded[4][..., 1:-1, 1:-1]
    lap_one = masked_laplacian(tracer, wet_mask)
    lap_two = masked_laplacian(lap_one, inner_mask)
    centre = window(inner_tracer, 1, 1)
    wet_centre = window(inner_mask, 1, 1)
    east_flux = face_flux(
        window(east_speed, 1, 1),
        window(east_speed, 1, 2),
        centre,
        window(inner_tracer, 1, 2),
        wet_centre,
        window(inner_mask, 1, 2),
    )
    west_flux = face_flux(
        window(east_speed, 1, 0),
        window(east_speed, 1, 1),
        window(inner_tracer, 1, 0),
        centre,
        window(inner_mask, 1, 0),
        wet_centre,
    )
    north_flux = face_flux(
        window(north_speed, 1, 1),
        window(north_speed, 2, 1),
        centre,
        window(inner_tracer, 2, 1),
        wet_centre,
        window(inner_mask, 2, 1),
    )
    south_flux = face_flux(
        window(north_speed, 0, 1),
        window(north_speed, 1, 1),
        window(inner_tracer, 0, 1),
        centre,
        window(inner_mask, 0, 1),
        wet_centre,
    )
    divergence = east_flux - west_flux + north_flux - south_flux
    return wet_centre * (centre - advection_rate * divergence - biharmonic_rate * lap_two)


def mix_kernel(values_ref, wet_ref, diff_ref, out_ref, ratio_ref):
    level_count = wet_ref.shape[0]
    tracer_count = values_ref.shape[0]

    def coupling(k):
        return diff_ref[k].astype(jnp.float32) * wet_ref[k] * wet_ref[k - 1]

    below = coupling(1)
    upper = None
    reduced = [None] * tracer_count
    for k in range(level_count):
        above = below
        below = coupling(k + 1) if k + 1 < level_count else None
        if k == 0:
            diagonal = 1.0 + below
            divisor = diagonal
        elif below is None:
            diagonal = 1.0 + above
            divisor = diagonal + above * upper
        else:
            diagonal = 1.0 + above + below
            divisor = diagonal + above * upper
        if below is not None:
            upper = -below / divisor
            ratio_ref[k] = upper
        for t in range(tracer_count):
            if k == 0:
                source = values_ref[t, 0]
            else:
                source = values_ref[t, k] + above * reduced[t]
            reduced[t] = source / divisor
            out_ref[t, k] = reduced[t]
    result = reduced
    for k in range(level_count - 2, -1, -1):
        ratio = ratio_ref[k]
        for t in range(tracer_count):
            result[t] = out_ref[t, k] - ratio * result[t]
            out_ref[t, k] = result[t]


def vertical_mix(values, wet_mask, diffusivity):
    tracer_count, level_count, row_count, col_count = values.shape
    rows = 16 if row_count % 16 == 0 else row_count
    return pl.pallas_call(
        mix_kernel,
        grid=(row_count // rows,),
        in_specs=[
            pl.BlockSpec((tracer_count, level_count, rows, col_count), lambda i: (0, 0, i, 0)),
            pl.BlockSpec((level_count, rows, col_count), lambda i: (0, i, 0)),
            pl.BlockSpec((level_count, rows, col_count), lambda i: (0, i, 0)),
        ],
        out_specs=pl.BlockSpec((tracer_count, level_count, rows, col_count), lambda i: (0, 0, i, 0)),
        out_shape=jax.ShapeDtypeStruct(values.shape, jnp.float32),
        scratch_shapes=[pltpu.VMEM((level_count - 1, rows, col_count), jnp.float32)],
    )(values, wet_mask, diffusivity)


def nine_point(padded, wet_surface, centre_weight):
    centre = window(padded, 1, 1)
    edges = (
        window(padded, 0, 1) + window(padded, 2, 1) + window(padded, 1, 0) + window(padded, 1, 2)
    )
    corners = (
        window(padded, 0, 0) + window(padded, 0, 2) + window(padded, 2, 0) + window(padded, 2, 2)
    )
    return wet_surface * (centre_weight * centre - edges - corner_weight * corners)


def clinic_extend(stacked, fold_signs):
    row_count = stacked.shape[2]
    widened = extended_2(stacked, (("lon", 3),), 2, True)
    extended = extended_2(widened, (("lat", 2),), 2, False)
    top_rows = widened[:, :, row_count - 2 :, :]
    for bit in range(lax.axis_size("lon").bit_length() - 1):
        top_rows = from_partner(top_rows, "lon", bit)
    northern = jnp.flip(top_rows, axis=(2, 3)) * fold_signs
    at_top = lax.axis_index("lat") == lax.axis_size("lat") - 1
    ghost_rows = jnp.where(at_top, northern, extended[:, :, row_count + 2 :, :])
    return jnp.concatenate([extended[:, :, : row_count + 2, :], ghost_rows], axis=2)


def strip_pad(surface_field):
    lon_index = lax.axis_index("lon")
    lon_count = lax.axis_size("lon")
    first_row = surface_field[0:1, :]
    last_row = surface_field[-1:, :]
    following = passed_along(first_row, "lon", -1)
    following_far = shifted(following, "lat", -1)
    preceding = passed_along(last_row, "lon", 1)
    preceding_far = shifted(preceding, "lat", 1)
    above_row = jnp.where(lon_index == lon_count - 1, following_far, following)
    below_row = jnp.where(lon_index == 0, preceding_far, preceding)
    top_strip = jnp.logical_and(
        lon_index == lon_count - 1, lax.axis_index("lat") == lax.axis_size("lat") - 1
    )
    above_row = jnp.where(top_strip, jnp.flip(last_row, axis=1), above_row)
    extended = jnp.concatenate([below_row, surface_field, above_row], axis=0)
    return jnp.concatenate([extended[:, -1:], extended, extended[:, :1]], axis=1)


def butterfly_sum(value):
    for axis in ("lon", "lat"):
        count = lax.axis_size(axis)
        bit = 1
        while bit < count:
            value = value + lax.ppermute(value, axis, [(i, i ^ bit) for i in range(count)])
            bit <<= 1
    return value


def solve(surface_source, wet_surface, centre_weight, padder):

    def precondition(residual):
        return wet_surface * residual / centre_weight

    def apply_operator(field):
        return nine_point(padder(field), wet_surface, centre_weight)

    solution = jnp.zeros_like(surface_source)
    residual = surface_source
    precond = precondition(residual)
    direction = precond
    operator_image = apply_operator(direction)
    totals = butterfly_sum(
        jnp.stack([jnp.sum(residual * precond), jnp.sum(direction * operator_image)])
    )
    resid_dot, curvature = totals[0], totals[1]
    for iteration in range(ITERS):
        step_size = resid_dot / curvature
        solution = solution + step_size * direction
        if iteration + 1 < ITERS:
            residual = residual - step_size * operator_image
            precond = precondition(residual)
            precond_image = apply_operator(precond)
            totals = butterfly_sum(
                jnp.stack(
                    [
                        jnp.sum(residual * precond),
                        jnp.sum(precond * precond_image),
                        jnp.sum(precond * operator_image),
                    ]
                )
            )
            dot_next = totals[0]
            ratio = dot_next / resid_dot
            direction = precond + ratio * direction
            curvature = totals[1] + 2.0 * ratio * totals[2] + ratio * ratio * curvature
            operator_image = precond_image + ratio * operator_image
            resid_dot = dot_next
    return solution


def shards(
    tracers,
    east_velocity,
    north_velocity,
    vertical_diffusivity,
    depth_levels,
    ocean_blocks,
    forcing,
    surface_coupling,
):
    level_count = tracers.shape[1]
    row_count = tracers.shape[2]
    col_count = tracers.shape[3]
    ocean_cells = jnp.repeat(
        jnp.repeat(ocean_blocks, row_count // ocean_blocks.shape[0], axis=0),
        col_count // ocean_blocks.shape[1],
        axis=1,
    ).astype(jnp.float32)
    level_index = lax.broadcasted_iota(jnp.int32, (level_count, row_count, col_count), 0)
    wet_mask = jnp.where(
        level_index < depth_levels[None], ocean_cells[None], jnp.zeros_like(ocean_cells)[None]
    )
    east_float = east_velocity.astype(jnp.float32)
    north_float = north_velocity.astype(jnp.float32)
    stacked = jnp.concatenate(
        [tracers, wet_mask[None], east_float[None], north_float[None]], axis=0
    )
    fold_signs = jnp.array([1.0, 1.0, 1.0, -1.0, -1.0], jnp.float32).reshape(5, 1, 1, 1)
    padded = clinic_extend(stacked, fold_signs)
    provisional = baroclinic(padded)
    new_tracers = vertical_mix(provisional, wet_mask, vertical_diffusivity)
    wet_surface = wet_mask[0]
    surface_source = wet_surface * (forcing + jnp.mean(new_tracers[0] - new_tracers[1], axis=0))
    centre_weight = 6.0 + surface_coupling
    relaid = lax.all_to_all(
        jnp.stack([surface_source, wet_surface, centre_weight]),
        "lon",
        split_axis=1,
        concat_axis=2,
        tiled=True,
    )
    strip_solution = solve(relaid[0], relaid[1], relaid[2], strip_pad)
    solution = lax.all_to_all(strip_solution, "lon", split_axis=1, concat_axis=0, tiled=True)
    return (new_tracers, solution)


def solution(mesh):
    placed = (
        P(None, None, "lat", "lon"),
        P(None, "lat", "lon"),
        P(None, "lat", "lon"),
        P(None, "lat", "lon"),
        P("lat", "lon"),
        P("lat", "lon"),
        P("lat", "lon"),
        P("lat", "lon"),
    )
    return jax.shard_map(
        shards,
        mesh=mesh,
        in_specs=placed,
        out_specs=(P(None, None, "lat", "lon"), P("lat", "lon")),
        check_vma=False,
    )
```

```python
import jax
import jax.numpy as jnp
from jax import lax
from jax.sharding import PartitionSpec as P
from jax.experimental import pallas as pl
from jax.experimental.pallas import tpu as pltpu

ITERS = 3


advection_rate = 0.25
biharmonic_rate = 0.01
corner_weight = 0.5


def extended_2(block, sides, width, periodic):
    for axis, dim in sides:
        count = lax.axis_size(axis)
        forward = [(i, i + 1) for i in range(count - 1)]
        if periodic:
            forward.append((count - 1, 0))
        backward = [(target, source) for source, target in forward]
        low = lax.ppermute(
            lax.slice_in_dim(block, block.shape[dim] - width, None, axis=dim), axis, forward
        )
        high = lax.ppermute(lax.slice_in_dim(block, 0, width, axis=dim), axis, backward)
        block = jnp.concatenate([low, block, high], axis=dim)
    return block


def from_partner(block, axis, stride):
    count = lax.axis_size(axis)
    route = []
    for low in range(count):
        high = low | 1 << stride
        if high != low and high < count:
            route += [(low, high), (high, low)]
    return lax.ppermute(block, axis, route)


def passed_along(value, axis, steps):
    count = lax.axis_size(axis)
    pairs = [(source, (source + steps) % count) for source in range(count)]
    return lax.ppermute(value, axis, pairs)


def shifted(shard, axis, by):
    count = lax.axis_size(axis)
    pairs = [(i, i + by) for i in range(count) if 0 <= i + by < count]
    return lax.ppermute(shard, axis, pairs)


def window(array, shift_row, shift_col):
    inner_height = array.shape[-2] - 2
    inner_width = array.shape[-1] - 2
    return array[..., shift_row : shift_row + inner_height, shift_col : shift_col + inner_width]


def masked_laplacian(values, wet_mask):
    centre = window(values, 1, 1)
    running = jnp.zeros_like(centre)
    for shift_row, shift_col in ((0, 1), (2, 1), (1, 0), (1, 2)):
        running = running + window(wet_mask, shift_row, shift_col) * (
            window(values, shift_row, shift_col) - centre
        )
    return window(wet_mask, 1, 1) * running


def face_flux(speed_one, speed_two, tracer_one, tracer_two, wet_one, wet_two):
    return 0.5 * (speed_one + speed_two) * 0.5 * (tracer_one + tracer_two) * wet_one * wet_two


def baroclinic(padded):
    tracer = padded[0:2]
    wet_mask = padded[2]
    inner_tracer = tracer[..., 1:-1, 1:-1]
    inner_mask = wet_mask[..., 1:-1, 1:-1]
    east_speed = padded[3][..., 1:-1, 1:-1]
    north_speed = padded[4][..., 1:-1, 1:-1]
    lap_one = masked_laplacian(tracer, wet_mask)
    lap_two = masked_laplacian(lap_one, inner_mask)
    centre = window(inner_tracer, 1, 1)
    wet_centre = window(inner_mask, 1, 1)
    east_flux = face_flux(
        window(east_speed, 1, 1),
        window(east_speed, 1, 2),
        centre,
        window(inner_tracer, 1, 2),
        wet_centre,
        window(inner_mask, 1, 2),
    )
    west_flux = face_flux(
        window(east_speed, 1, 0),
        window(east_speed, 1, 1),
        window(inner_tracer, 1, 0),
        centre,
        window(inner_mask, 1, 0),
        wet_centre,
    )
    north_flux = face_flux(
        window(north_speed, 1, 1),
        window(north_speed, 2, 1),
        centre,
        window(inner_tracer, 2, 1),
        wet_centre,
        window(inner_mask, 2, 1),
    )
    south_flux = face_flux(
        window(north_speed, 0, 1),
        window(north_speed, 1, 1),
        window(inner_tracer, 0, 1),
        centre,
        window(inner_mask, 0, 1),
        wet_centre,
    )
    divergence = east_flux - west_flux + north_flux - south_flux
    return wet_centre * (centre - advection_rate * divergence - biharmonic_rate * lap_two)


def stencil_kernel(ext_ref, out_ref):
    height, width = ext_ref.shape[2], ext_ref.shape[3]
    row_count, col_count = out_ref.shape[2], out_ref.shape[3]

    def south(x):
        return pltpu.roll(x, 1, 0)

    def north(x):
        return pltpu.roll(x, height - 1, 0)

    def west(x):
        return pltpu.roll(x, 1, 1)

    def east(x):
        return pltpu.roll(x, width - 1, 1)

    shifts = (south, north, west, east)
    wet = ext_ref[2, 0]
    wet_near = [shift(wet) for shift in shifts]

    def laplacian(values):
        running = None
        for shift, wet_n in zip(shifts, wet_near):
            term = wet_n * (shift(values) - values)
            running = term if running is None else running + term
        return wet * running

    east_speed = ext_ref[3, 0]
    north_speed = ext_ref[4, 0]
    east_mean = 0.5 * (east_speed + east(east_speed))
    north_mean = 0.5 * (north_speed + north(north_speed))
    for t in range(out_ref.shape[0]):
        tracer = ext_ref[t, 0]
        lap_two = laplacian(laplacian(tracer))
        east_flux = east_mean * 0.5 * (tracer + east(tracer)) * wet * wet_near[3]
        north_flux = north_mean * 0.5 * (tracer + north(tracer)) * wet * wet_near[1]
        divergence = east_flux - west(east_flux) + north_flux - south(north_flux)
        result = wet * (tracer - advection_rate * divergence - biharmonic_rate * lap_two)
        out_ref[t, 0] = result[:row_count, :col_count]


def wrapped_layout(padded):
    rows = padded.shape[2] - 4
    cols = padded.shape[3] - 4
    height = -(-(rows + 4) // 8) * 8
    width = -(-(cols + 4) // 128) * 128
    lead = padded.shape[:2]
    by_rows = jnp.concatenate(
        [
            padded[:, :, 2 : rows + 4],
            jnp.zeros(lead + (height - rows - 4, padded.shape[3]), padded.dtype),
            padded[:, :, 0:2],
        ],
        axis=2,
    )
    return jnp.concatenate(
        [
            by_rows[..., 2 : cols + 4],
            jnp.zeros(lead + (height, width - cols - 4), padded.dtype),
            by_rows[..., 0:2],
        ],
        axis=3,
    )


def baroclinic_kernel(padded):
    tracer_count = 2
    level_count = padded.shape[1]
    rows = padded.shape[2] - 4
    cols = padded.shape[3] - 4
    ext = wrapped_layout(padded)
    height, width = ext.shape[2], ext.shape[3]
    return pl.pallas_call(
        stencil_kernel,
        grid=(level_count,),
        in_specs=[pl.BlockSpec((ext.shape[0], 1, height, width), lambda k: (0, k, 0, 0))],
        out_specs=pl.BlockSpec((tracer_count, 1, rows, cols), lambda k: (0, k, 0, 0)),
        out_shape=jax.ShapeDtypeStruct((tracer_count, level_count, rows, cols), jnp.float32),
    )(ext)


def mix_kernel(values_ref, wet_ref, diff_ref, out_ref, ratio_ref):
    level_count = wet_ref.shape[0]
    tracer_count = values_ref.shape[0]

    def coupling(k):
        return diff_ref[k].astype(jnp.float32) * wet_ref[k] * wet_ref[k - 1]

    below = coupling(1)
    upper = None
    reduced = [None] * tracer_count
    for k in range(level_count):
        above = below
        below = coupling(k + 1) if k + 1 < level_count else None
        if k == 0:
            diagonal = 1.0 + below
            divisor = diagonal
        elif below is None:
            diagonal = 1.0 + above
            divisor = diagonal + above * upper
        else:
            diagonal = 1.0 + above + below
            divisor = diagonal + above * upper
        if below is not None:
            upper = -below / divisor
            ratio_ref[k] = upper
        for t in range(tracer_count):
            if k == 0:
                source = values_ref[t, 0]
            else:
                source = values_ref[t, k] + above * reduced[t]
            reduced[t] = source / divisor
            out_ref[t, k] = reduced[t]
    result = reduced
    for k in range(level_count - 2, -1, -1):
        ratio = ratio_ref[k]
        for t in range(tracer_count):
            result[t] = out_ref[t, k] - ratio * result[t]
            out_ref[t, k] = result[t]


def vertical_mix(values, wet_mask, diffusivity):
    tracer_count, level_count, row_count, col_count = values.shape
    rows = 16 if row_count % 16 == 0 else row_count
    return pl.pallas_call(
        mix_kernel,
        grid=(row_count // rows,),
        in_specs=[
            pl.BlockSpec((tracer_count, level_count, rows, col_count), lambda i: (0, 0, i, 0)),
            pl.BlockSpec((level_count, rows, col_count), lambda i: (0, i, 0)),
            pl.BlockSpec((level_count, rows, col_count), lambda i: (0, i, 0)),
        ],
        out_specs=pl.BlockSpec((tracer_count, level_count, rows, col_count), lambda i: (0, 0, i, 0)),
        out_shape=jax.ShapeDtypeStruct(values.shape, jnp.float32),
        scratch_shapes=[pltpu.VMEM((level_count - 1, rows, col_count), jnp.float32)],
    )(values, wet_mask, diffusivity)


def nine_point(padded, wet_surface, centre_weight):
    centre = window(padded, 1, 1)
    edges = (
        window(padded, 0, 1) + window(padded, 2, 1) + window(padded, 1, 0) + window(padded, 1, 2)
    )
    corners = (
        window(padded, 0, 0) + window(padded, 0, 2) + window(padded, 2, 0) + window(padded, 2, 2)
    )
    return wet_surface * (centre_weight * centre - edges - corner_weight * corners)


def clinic_extend(stacked, fold_signs):
    row_count = stacked.shape[2]
    widened = extended_2(stacked, (("lon", 3),), 2, True)
    extended = extended_2(widened, (("lat", 2),), 2, False)
    top_rows = widened[:, :, row_count - 2 :, :]
    for bit in range(lax.axis_size("lon").bit_length() - 1):
        top_rows = from_partner(top_rows, "lon", bit)
    northern = jnp.flip(top_rows, axis=(2, 3)) * fold_signs
    at_top = lax.axis_index("lat") == lax.axis_size("lat") - 1
    ghost_rows = jnp.where(at_top, northern, extended[:, :, row_count + 2 :, :])
    return jnp.concatenate([extended[:, :, : row_count + 2, :], ghost_rows], axis=2)


def strip_pad(surface_field):
    lon_index = lax.axis_index("lon")
    lon_count = lax.axis_size("lon")
    first_row = surface_field[0:1, :]
    last_row = surface_field[-1:, :]
    following = passed_along(first_row, "lon", -1)
    following_far = shifted(following, "lat", -1)
    preceding = passed_along(last_row, "lon", 1)
    preceding_far = shifted(preceding, "lat", 1)
    above_row = jnp.where(lon_index == lon_count - 1, following_far, following)
    below_row = jnp.where(lon_index == 0, preceding_far, preceding)
    top_strip = jnp.logical_and(
        lon_index == lon_count - 1, lax.axis_index("lat") == lax.axis_size("lat") - 1
    )
    above_row = jnp.where(top_strip, jnp.flip(last_row, axis=1), above_row)
    extended = jnp.concatenate([below_row, surface_field, above_row], axis=0)
    return jnp.concatenate([extended[:, -1:], extended, extended[:, :1]], axis=1)


def butterfly_sum(value):
    for axis in ("lon", "lat"):
        count = lax.axis_size(axis)
        bit = 1
        while bit < count:
            value = value + lax.ppermute(value, axis, [(i, i ^ bit) for i in range(count)])
            bit <<= 1
    return value


def solve(surface_source, wet_surface, centre_weight, padder):

    def precondition(residual):
        return wet_surface * residual / centre_weight

    def apply_operator(field):
        return nine_point(padder(field), wet_surface, centre_weight)

    solution = jnp.zeros_like(surface_source)
    residual = surface_source
    precond = precondition(residual)
    direction = precond
    operator_image = apply_operator(direction)
    totals = butterfly_sum(
        jnp.stack([jnp.sum(residual * precond), jnp.sum(direction * operator_image)])
    )
    resid_dot, curvature = totals[0], totals[1]
    for iteration in range(ITERS):
        step_size = resid_dot / curvature
        solution = solution + step_size * direction
        if iteration + 1 < ITERS:
            residual = residual - step_size * operator_image
            precond = precondition(residual)
            precond_image = apply_operator(precond)
            totals = butterfly_sum(
                jnp.stack(
                    [
                        jnp.sum(residual * precond),
                        jnp.sum(precond * precond_image),
                        jnp.sum(precond * operator_image),
                    ]
                )
            )
            dot_next = totals[0]
            ratio = dot_next / resid_dot
            direction = precond + ratio * direction
            curvature = totals[1] + 2.0 * ratio * totals[2] + ratio * ratio * curvature
            operator_image = precond_image + ratio * operator_image
            resid_dot = dot_next
    return solution


def shards(
    tracers,
    east_velocity,
    north_velocity,
    vertical_diffusivity,
    depth_levels,
    ocean_blocks,
    forcing,
    surface_coupling,
):
    level_count = tracers.shape[1]
    row_count = tracers.shape[2]
    col_count = tracers.shape[3]
    ocean_cells = jnp.repeat(
        jnp.repeat(ocean_blocks, row_count // ocean_blocks.shape[0], axis=0),
        col_count // ocean_blocks.shape[1],
        axis=1,
    ).astype(jnp.float32)
    level_index = lax.broadcasted_iota(jnp.int32, (level_count, row_count, col_count), 0)
    wet_mask = jnp.where(
        level_index < depth_levels[None], ocean_cells[None], jnp.zeros_like(ocean_cells)[None]
    )
    east_float = east_velocity.astype(jnp.float32)
    north_float = north_velocity.astype(jnp.float32)
    stacked = jnp.concatenate(
        [tracers, wet_mask[None], east_float[None], north_float[None]], axis=0
    )
    fold_signs = jnp.array([1.0, 1.0, 1.0, -1.0, -1.0], jnp.float32).reshape(5, 1, 1, 1)
    padded = clinic_extend(stacked, fold_signs)
    provisional = baroclinic_kernel(padded)
    new_tracers = vertical_mix(provisional, wet_mask, vertical_diffusivity)
    wet_surface = wet_mask[0]
    surface_source = wet_surface * (forcing + jnp.mean(new_tracers[0] - new_tracers[1], axis=0))
    centre_weight = 6.0 + surface_coupling
    relaid = lax.all_to_all(
        jnp.stack([surface_source, wet_surface, centre_weight]),
        "lon",
        split_axis=1,
        concat_axis=2,
        tiled=True,
    )
    strip_solution = solve(relaid[0], relaid[1], relaid[2], strip_pad)
    solution = lax.all_to_all(strip_solution, "lon", split_axis=1, concat_axis=0, tiled=True)
    return (new_tracers, solution)


def solution(mesh):
    placed = (
        P(None, None, "lat", "lon"),
        P(None, "lat", "lon"),
        P(None, "lat", "lon"),
        P(None, "lat", "lon"),
        P("lat", "lon"),
        P("lat", "lon"),
        P("lat", "lon"),
        P("lat", "lon"),
    )
    return jax.shard_map(
        shards,
        mesh=mesh,
        in_specs=placed,
        out_specs=(P(None, None, "lat", "lon"), P("lat", "lon")),
        check_vma=False,
    )
```

```python
import jax
import jax.numpy as jnp
from jax import lax
from jax.sharding import PartitionSpec as P
from jax.experimental import pallas as pl
from jax.experimental.pallas import tpu as pltpu

ITERS = 3


advection_rate = 0.25
biharmonic_rate = 0.01
corner_weight = 0.5


def extended_2(block, sides, width, periodic):
    for axis, dim in sides:
        count = lax.axis_size(axis)
        forward = [(i, i + 1) for i in range(count - 1)]
        if periodic:
            forward.append((count - 1, 0))
        backward = [(target, source) for source, target in forward]
        low = lax.ppermute(
            lax.slice_in_dim(block, block.shape[dim] - width, None, axis=dim), axis, forward
        )
        high = lax.ppermute(lax.slice_in_dim(block, 0, width, axis=dim), axis, backward)
        block = jnp.concatenate([low, block, high], axis=dim)
    return block


def from_partner(block, axis, stride):
    count = lax.axis_size(axis)
    route = []
    for low in range(count):
        high = low | 1 << stride
        if high != low and high < count:
            route += [(low, high), (high, low)]
    return lax.ppermute(block, axis, route)


def passed_along(value, axis, steps):
    count = lax.axis_size(axis)
    pairs = [(source, (source + steps) % count) for source in range(count)]
    return lax.ppermute(value, axis, pairs)


def shifted(shard, axis, by):
    count = lax.axis_size(axis)
    pairs = [(i, i + by) for i in range(count) if 0 <= i + by < count]
    return lax.ppermute(shard, axis, pairs)


def window(array, shift_row, shift_col):
    inner_height = array.shape[-2] - 2
    inner_width = array.shape[-1] - 2
    return array[..., shift_row : shift_row + inner_height, shift_col : shift_col + inner_width]


def masked_laplacian(values, wet_mask):
    centre = window(values, 1, 1)
    running = jnp.zeros_like(centre)
    for shift_row, shift_col in ((0, 1), (2, 1), (1, 0), (1, 2)):
        running = running + window(wet_mask, shift_row, shift_col) * (
            window(values, shift_row, shift_col) - centre
        )
    return window(wet_mask, 1, 1) * running


def face_flux(speed_one, speed_two, tracer_one, tracer_two, wet_one, wet_two):
    return 0.5 * (speed_one + speed_two) * 0.5 * (tracer_one + tracer_two) * wet_one * wet_two


def baroclinic(padded):
    tracer = padded[0:2]
    wet_mask = padded[2]
    inner_tracer = tracer[..., 1:-1, 1:-1]
    inner_mask = wet_mask[..., 1:-1, 1:-1]
    east_speed = padded[3][..., 1:-1, 1:-1]
    north_speed = padded[4][..., 1:-1, 1:-1]
    lap_one = masked_laplacian(tracer, wet_mask)
    lap_two = masked_laplacian(lap_one, inner_mask)
    centre = window(inner_tracer, 1, 1)
    wet_centre = window(inner_mask, 1, 1)
    east_flux = face_flux(
        window(east_speed, 1, 1),
        window(east_speed, 1, 2),
        centre,
        window(inner_tracer, 1, 2),
        wet_centre,
        window(inner_mask, 1, 2),
    )
    west_flux = face_flux(
        window(east_speed, 1, 0),
        window(east_speed, 1, 1),
        window(inner_tracer, 1, 0),
        centre,
        window(inner_mask, 1, 0),
        wet_centre,
    )
    north_flux = face_flux(
        window(north_speed, 1, 1),
        window(north_speed, 2, 1),
        centre,
        window(inner_tracer, 2, 1),
        wet_centre,
        window(inner_mask, 2, 1),
    )
    south_flux = face_flux(
        window(north_speed, 0, 1),
        window(north_speed, 1, 1),
        window(inner_tracer, 0, 1),
        centre,
        window(inner_mask, 0, 1),
        wet_centre,
    )
    divergence = east_flux - west_flux + north_flux - south_flux
    return wet_centre * (centre - advection_rate * divergence - biharmonic_rate * lap_two)


def stencil_kernel(ext_ref, out_ref):
    height, width = ext_ref.shape[2], ext_ref.shape[3]
    row_count, col_count = out_ref.shape[2], out_ref.shape[3]

    def south(x):
        return pltpu.roll(x, 1, 0)

    def north(x):
        return pltpu.roll(x, height - 1, 0)

    def west(x):
        return pltpu.roll(x, 1, 1)

    def east(x):
        return pltpu.roll(x, width - 1, 1)

    shifts = (south, north, west, east)
    wet = ext_ref[2, 0]
    wet_near = [shift(wet) for shift in shifts]

    def laplacian(values):
        running = None
        for shift, wet_n in zip(shifts, wet_near):
            term = wet_n * (shift(values) - values)
            running = term if running is None else running + term
        return wet * running

    east_speed = ext_ref[3, 0]
    north_speed = ext_ref[4, 0]
    east_mean = 0.5 * (east_speed + east(east_speed))
    north_mean = 0.5 * (north_speed + north(north_speed))
    for t in range(out_ref.shape[0]):
        tracer = ext_ref[t, 0]
        lap_two = laplacian(laplacian(tracer))
        east_flux = east_mean * 0.5 * (tracer + east(tracer)) * wet * wet_near[3]
        north_flux = north_mean * 0.5 * (tracer + north(tracer)) * wet * wet_near[1]
        divergence = east_flux - west(east_flux) + north_flux - south(north_flux)
        result = wet * (tracer - advection_rate * divergence - biharmonic_rate * lap_two)
        out_ref[t, 0] = result[:row_count, :col_count]


def wrapped_layout(padded):
    rows = padded.shape[2] - 4
    cols = padded.shape[3] - 4
    height = -(-(rows + 4) // 8) * 8
    width = -(-(cols + 4) // 128) * 128
    lead = padded.shape[:2]
    by_rows = jnp.concatenate(
        [
            padded[:, :, 2 : rows + 4],
            jnp.zeros(lead + (height - rows - 4, padded.shape[3]), padded.dtype),
            padded[:, :, 0:2],
        ],
        axis=2,
    )
    return jnp.concatenate(
        [
            by_rows[..., 2 : cols + 4],
            jnp.zeros(lead + (height, width - cols - 4), padded.dtype),
            by_rows[..., 0:2],
        ],
        axis=3,
    )


def stencil_call(ext, rows, cols):
    tracer_count = 2
    level_count = ext.shape[1]
    height, width = ext.shape[2], ext.shape[3]
    return pl.pallas_call(
        stencil_kernel,
        grid=(level_count,),
        in_specs=[pl.BlockSpec((ext.shape[0], 1, height, width), lambda k: (0, k, 0, 0))],
        out_specs=pl.BlockSpec((tracer_count, 1, rows, cols), lambda k: (0, k, 0, 0)),
        out_shape=jax.ShapeDtypeStruct((tracer_count, level_count, rows, cols), jnp.float32),
    )(ext)


def mix_kernel(values_ref, wet_ref, diff_ref, out_ref, ratio_ref):
    level_count = wet_ref.shape[0]
    tracer_count = values_ref.shape[0]

    def coupling(k):
        return diff_ref[k].astype(jnp.float32) * wet_ref[k] * wet_ref[k - 1]

    below = coupling(1)
    upper = None
    reduced = [None] * tracer_count
    for k in range(level_count):
        above = below
        below = coupling(k + 1) if k + 1 < level_count else None
        if k == 0:
            diagonal = 1.0 + below
            divisor = diagonal
        elif below is None:
            diagonal = 1.0 + above
            divisor = diagonal + above * upper
        else:
            diagonal = 1.0 + above + below
            divisor = diagonal + above * upper
        if below is not None:
            upper = -below / divisor
            ratio_ref[k] = upper
        for t in range(tracer_count):
            if k == 0:
                source = values_ref[t, 0]
            else:
                source = values_ref[t, k] + above * reduced[t]
            reduced[t] = source / divisor
            out_ref[t, k] = reduced[t]
    result = reduced
    for k in range(level_count - 2, -1, -1):
        ratio = ratio_ref[k]
        for t in range(tracer_count):
            result[t] = out_ref[t, k] - ratio * result[t]
            out_ref[t, k] = result[t]


def vertical_mix(values, wet_mask, diffusivity):
    tracer_count, level_count, row_count, col_count = values.shape
    rows = 16 if row_count % 16 == 0 else row_count
    return pl.pallas_call(
        mix_kernel,
        grid=(row_count // rows,),
        in_specs=[
            pl.BlockSpec((tracer_count, level_count, rows, col_count), lambda i: (0, 0, i, 0)),
            pl.BlockSpec((level_count, rows, col_count), lambda i: (0, i, 0)),
            pl.BlockSpec((level_count, rows, col_count), lambda i: (0, i, 0)),
        ],
        out_specs=pl.BlockSpec((tracer_count, level_count, rows, col_count), lambda i: (0, 0, i, 0)),
        out_shape=jax.ShapeDtypeStruct(values.shape, jnp.float32),
        scratch_shapes=[pltpu.VMEM((level_count - 1, rows, col_count), jnp.float32)],
    )(values, wet_mask, diffusivity)


def nine_point(padded, wet_surface, centre_weight):
    centre = window(padded, 1, 1)
    edges = (
        window(padded, 0, 1) + window(padded, 2, 1) + window(padded, 1, 0) + window(padded, 1, 2)
    )
    corners = (
        window(padded, 0, 0) + window(padded, 0, 2) + window(padded, 2, 0) + window(padded, 2, 2)
    )
    return wet_surface * (centre_weight * centre - edges - corner_weight * corners)


def wrapped_extend(stacked, fold_signs):
    rows, cols = stacked.shape[2], stacked.shape[3]
    height = -(-(rows + 4) // 8) * 8
    width = -(-(cols + 4) // 128) * 128
    lead = stacked.shape[:2]
    lon_count = lax.axis_size("lon")
    lat_count = lax.axis_size("lat")
    east_halo = lax.ppermute(
        stacked[..., :2], "lon", [(i, (i - 1) % lon_count) for i in range(lon_count)]
    )
    west_halo = lax.ppermute(
        stacked[..., cols - 2 :], "lon", [(i, (i + 1) % lon_count) for i in range(lon_count)]
    )
    widened = jnp.concatenate(
        [stacked, east_halo, jnp.zeros(lead + (rows, width - cols - 4), stacked.dtype), west_halo],
        axis=3,
    )
    north_rows = lax.ppermute(widened[:, :, :2], "lat", [(j, j - 1) for j in range(1, lat_count)])
    south_rows = lax.ppermute(
        widened[:, :, rows - 2 :], "lat", [(j, j + 1) for j in range(lat_count - 1)]
    )
    mirrored = lax.ppermute(
        widened[:, :, rows - 2 :], "lon", [(i, lon_count - 1 - i) for i in range(lon_count)]
    )
    folded = jnp.roll(jnp.flip(mirrored, axis=(2, 3)), cols - width, axis=3) * fold_signs
    at_top = lax.axis_index("lat") == lat_count - 1
    north = jnp.where(at_top, folded, north_rows)
    return jnp.concatenate(
        [widened, north, jnp.zeros(lead + (height - rows - 4, width), stacked.dtype), south_rows],
        axis=2,
    )


def clinic_extend(stacked, fold_signs):
    row_count = stacked.shape[2]
    widened = extended_2(stacked, (("lon", 3),), 2, True)
    extended = extended_2(widened, (("lat", 2),), 2, False)
    top_rows = widened[:, :, row_count - 2 :, :]
    for bit in range(lax.axis_size("lon").bit_length() - 1):
        top_rows = from_partner(top_rows, "lon", bit)
    northern = jnp.flip(top_rows, axis=(2, 3)) * fold_signs
    at_top = lax.axis_index("lat") == lax.axis_size("lat") - 1
    ghost_rows = jnp.where(at_top, northern, extended[:, :, row_count + 2 :, :])
    return jnp.concatenate([extended[:, :, : row_count + 2, :], ghost_rows], axis=2)


def strip_pad(surface_field):
    lon_index = lax.axis_index("lon")
    lon_count = lax.axis_size("lon")
    first_row = surface_field[0:1, :]
    last_row = surface_field[-1:, :]
    following = passed_along(first_row, "lon", -1)
    following_far = shifted(following, "lat", -1)
    preceding = passed_along(last_row, "lon", 1)
    preceding_far = shifted(preceding, "lat", 1)
    above_row = jnp.where(lon_index == lon_count - 1, following_far, following)
    below_row = jnp.where(lon_index == 0, preceding_far, preceding)
    top_strip = jnp.logical_and(
        lon_index == lon_count - 1, lax.axis_index("lat") == lax.axis_size("lat") - 1
    )
    above_row = jnp.where(top_strip, jnp.flip(last_row, axis=1), above_row)
    extended = jnp.concatenate([below_row, surface_field, above_row], axis=0)
    return jnp.concatenate([extended[:, -1:], extended, extended[:, :1]], axis=1)


def butterfly_sum(value):
    for axis in ("lon", "lat"):
        count = lax.axis_size(axis)
        bit = 1
        while bit < count:
            value = value + lax.ppermute(value, axis, [(i, i ^ bit) for i in range(count)])
            bit <<= 1
    return value


def solve(surface_source, wet_surface, centre_weight, padder):

    def precondition(residual):
        return wet_surface * residual / centre_weight

    def apply_operator(field):
        return nine_point(padder(field), wet_surface, centre_weight)

    solution = jnp.zeros_like(surface_source)
    residual = surface_source
    precond = precondition(residual)
    direction = precond
    operator_image = apply_operator(direction)
    totals = butterfly_sum(
        jnp.stack([jnp.sum(residual * precond), jnp.sum(direction * operator_image)])
    )
    resid_dot, curvature = totals[0], totals[1]
    for iteration in range(ITERS):
        step_size = resid_dot / curvature
        solution = solution + step_size * direction
        if iteration + 1 < ITERS:
            residual = residual - step_size * operator_image
            precond = precondition(residual)
            precond_image = apply_operator(precond)
            totals = butterfly_sum(
                jnp.stack(
                    [
                        jnp.sum(residual * precond),
                        jnp.sum(precond * precond_image),
                        jnp.sum(precond * operator_image),
                    ]
                )
            )
            dot_next = totals[0]
            ratio = dot_next / resid_dot
            direction = precond + ratio * direction
            curvature = totals[1] + 2.0 * ratio * totals[2] + ratio * ratio * curvature
            operator_image = precond_image + ratio * operator_image
            resid_dot = dot_next
    return solution


def shards(
    tracers,
    east_velocity,
    north_velocity,
    vertical_diffusivity,
    depth_levels,
    ocean_blocks,
    forcing,
    surface_coupling,
):
    level_count = tracers.shape[1]
    row_count = tracers.shape[2]
    col_count = tracers.shape[3]
    ocean_cells = jnp.repeat(
        jnp.repeat(ocean_blocks, row_count // ocean_blocks.shape[0], axis=0),
        col_count // ocean_blocks.shape[1],
        axis=1,
    ).astype(jnp.float32)
    level_index = lax.broadcasted_iota(jnp.int32, (level_count, row_count, col_count), 0)
    wet_mask = jnp.where(
        level_index < depth_levels[None], ocean_cells[None], jnp.zeros_like(ocean_cells)[None]
    )
    east_float = east_velocity.astype(jnp.float32)
    north_float = north_velocity.astype(jnp.float32)
    stacked = jnp.concatenate(
        [tracers, wet_mask[None], east_float[None], north_float[None]], axis=0
    )
    fold_signs = jnp.array([1.0, 1.0, 1.0, -1.0, -1.0], jnp.float32).reshape(5, 1, 1, 1)
    provisional = stencil_call(wrapped_extend(stacked, fold_signs), row_count, col_count)
    new_tracers = vertical_mix(provisional, wet_mask, vertical_diffusivity)
    wet_surface = wet_mask[0]
    surface_source = wet_surface * (forcing + jnp.mean(new_tracers[0] - new_tracers[1], axis=0))
    centre_weight = 6.0 + surface_coupling
    relaid = lax.all_to_all(
        jnp.stack([surface_source, wet_surface, centre_weight]),
        "lon",
        split_axis=1,
        concat_axis=2,
        tiled=True,
    )
    strip_solution = solve(relaid[0], relaid[1], relaid[2], strip_pad)
    solution = lax.all_to_all(strip_solution, "lon", split_axis=1, concat_axis=0, tiled=True)
    return (new_tracers, solution)


def solution(mesh):
    placed = (
        P(None, None, "lat", "lon"),
        P(None, "lat", "lon"),
        P(None, "lat", "lon"),
        P(None, "lat", "lon"),
        P("lat", "lon"),
        P("lat", "lon"),
        P("lat", "lon"),
        P("lat", "lon"),
    )
    return jax.shard_map(
        shards,
        mesh=mesh,
        in_specs=placed,
        out_specs=(P(None, None, "lat", "lon"), P("lat", "lon")),
        check_vma=False,
    )
```

```python
import jax
import jax.numpy as jnp
from jax import lax
from jax.sharding import PartitionSpec as P
from jax.experimental import pallas as pl
from jax.experimental.pallas import tpu as pltpu

ITERS = 3


advection_rate = 0.25
biharmonic_rate = 0.01
corner_weight = 0.5


def extended_2(block, sides, width, periodic):
    for axis, dim in sides:
        count = lax.axis_size(axis)
        forward = [(i, i + 1) for i in range(count - 1)]
        if periodic:
            forward.append((count - 1, 0))
        backward = [(target, source) for source, target in forward]
        low = lax.ppermute(
            lax.slice_in_dim(block, block.shape[dim] - width, None, axis=dim), axis, forward
        )
        high = lax.ppermute(lax.slice_in_dim(block, 0, width, axis=dim), axis, backward)
        block = jnp.concatenate([low, block, high], axis=dim)
    return block


def from_partner(block, axis, stride):
    count = lax.axis_size(axis)
    route = []
    for low in range(count):
        high = low | 1 << stride
        if high != low and high < count:
            route += [(low, high), (high, low)]
    return lax.ppermute(block, axis, route)


def passed_along(value, axis, steps):
    count = lax.axis_size(axis)
    pairs = [(source, (source + steps) % count) for source in range(count)]
    return lax.ppermute(value, axis, pairs)


def shifted(shard, axis, by):
    count = lax.axis_size(axis)
    pairs = [(i, i + by) for i in range(count) if 0 <= i + by < count]
    return lax.ppermute(shard, axis, pairs)


def window(array, shift_row, shift_col):
    inner_height = array.shape[-2] - 2
    inner_width = array.shape[-1] - 2
    return array[..., shift_row : shift_row + inner_height, shift_col : shift_col + inner_width]


def masked_laplacian(values, wet_mask):
    centre = window(values, 1, 1)
    running = jnp.zeros_like(centre)
    for shift_row, shift_col in ((0, 1), (2, 1), (1, 0), (1, 2)):
        running = running + window(wet_mask, shift_row, shift_col) * (
            window(values, shift_row, shift_col) - centre
        )
    return window(wet_mask, 1, 1) * running


def face_flux(speed_one, speed_two, tracer_one, tracer_two, wet_one, wet_two):
    return 0.5 * (speed_one + speed_two) * 0.5 * (tracer_one + tracer_two) * wet_one * wet_two


def baroclinic(padded):
    tracer = padded[0:2]
    wet_mask = padded[2]
    inner_tracer = tracer[..., 1:-1, 1:-1]
    inner_mask = wet_mask[..., 1:-1, 1:-1]
    east_speed = padded[3][..., 1:-1, 1:-1]
    north_speed = padded[4][..., 1:-1, 1:-1]
    lap_one = masked_laplacian(tracer, wet_mask)
    lap_two = masked_laplacian(lap_one, inner_mask)
    centre = window(inner_tracer, 1, 1)
    wet_centre = window(inner_mask, 1, 1)
    east_flux = face_flux(
        window(east_speed, 1, 1),
        window(east_speed, 1, 2),
        centre,
        window(inner_tracer, 1, 2),
        wet_centre,
        window(inner_mask, 1, 2),
    )
    west_flux = face_flux(
        window(east_speed, 1, 0),
        window(east_speed, 1, 1),
        window(inner_tracer, 1, 0),
        centre,
        window(inner_mask, 1, 0),
        wet_centre,
    )
    north_flux = face_flux(
        window(north_speed, 1, 1),
        window(north_speed, 2, 1),
        centre,
        window(inner_tracer, 2, 1),
        wet_centre,
        window(inner_mask, 2, 1),
    )
    south_flux = face_flux(
        window(north_speed, 0, 1),
        window(north_speed, 1, 1),
        window(inner_tracer, 0, 1),
        centre,
        window(inner_mask, 0, 1),
        wet_centre,
    )
    divergence = east_flux - west_flux + north_flux - south_flux
    return wet_centre * (centre - advection_rate * divergence - biharmonic_rate * lap_two)


def stencil_kernel(ext_ref, out_ref):
    height, width = ext_ref.shape[2], ext_ref.shape[3]
    row_count, col_count = out_ref.shape[2], out_ref.shape[3]

    def south(x):
        return pltpu.roll(x, 1, 0)

    def north(x):
        return pltpu.roll(x, height - 1, 0)

    def west(x):
        return pltpu.roll(x, 1, 1)

    def east(x):
        return pltpu.roll(x, width - 1, 1)

    shifts = (south, north, west, east)
    wet = ext_ref[2, 0]
    wet_near = [shift(wet) for shift in shifts]

    def laplacian(values):
        running = None
        for shift, wet_n in zip(shifts, wet_near):
            term = wet_n * (shift(values) - values)
            running = term if running is None else running + term
        return wet * running

    east_speed = ext_ref[3, 0]
    north_speed = ext_ref[4, 0]
    east_mean = 0.5 * (east_speed + east(east_speed))
    north_mean = 0.5 * (north_speed + north(north_speed))
    for t in range(out_ref.shape[0]):
        tracer = ext_ref[t, 0]
        lap_two = laplacian(laplacian(tracer))
        east_flux = east_mean * 0.5 * (tracer + east(tracer)) * wet * wet_near[3]
        north_flux = north_mean * 0.5 * (tracer + north(tracer)) * wet * wet_near[1]
        divergence = east_flux - west(east_flux) + north_flux - south(north_flux)
        result = wet * (tracer - advection_rate * divergence - biharmonic_rate * lap_two)
        out_ref[t, 0] = result[:row_count, :col_count]


def wrapped_layout(padded):
    rows = padded.shape[2] - 4
    cols = padded.shape[3] - 4
    height = -(-(rows + 4) // 8) * 8
    width = -(-(cols + 4) // 128) * 128
    lead = padded.shape[:2]
    by_rows = jnp.concatenate(
        [
            padded[:, :, 2 : rows + 4],
            jnp.zeros(lead + (height - rows - 4, padded.shape[3]), padded.dtype),
            padded[:, :, 0:2],
        ],
        axis=2,
    )
    return jnp.concatenate(
        [
            by_rows[..., 2 : cols + 4],
            jnp.zeros(lead + (height, width - cols - 4), padded.dtype),
            by_rows[..., 0:2],
        ],
        axis=3,
    )


def stencil_call(ext, rows, cols):
    tracer_count = 2
    level_count = ext.shape[1]
    height, width = ext.shape[2], ext.shape[3]
    return pl.pallas_call(
        stencil_kernel,
        grid=(level_count,),
        in_specs=[pl.BlockSpec((ext.shape[0], 1, height, width), lambda k: (0, k, 0, 0))],
        out_specs=pl.BlockSpec((tracer_count, 1, rows, cols), lambda k: (0, k, 0, 0)),
        out_shape=jax.ShapeDtypeStruct((tracer_count, level_count, rows, cols), jnp.float32),
    )(ext)


def mix_kernel(values_ref, wet_ref, diff_ref, out_ref, ratio_ref):
    level_count = wet_ref.shape[0]
    tracer_count = values_ref.shape[0]

    def coupling(k):
        return diff_ref[k].astype(jnp.float32) * wet_ref[k] * wet_ref[k - 1]

    below = coupling(1)
    upper = None
    reduced = [None] * tracer_count
    for k in range(level_count):
        above = below
        below = coupling(k + 1) if k + 1 < level_count else None
        if k == 0:
            diagonal = 1.0 + below
            divisor = diagonal
        elif below is None:
            diagonal = 1.0 + above
            divisor = diagonal + above * upper
        else:
            diagonal = 1.0 + above + below
            divisor = diagonal + above * upper
        if below is not None:
            upper = -below / divisor
            ratio_ref[k] = upper
        for t in range(tracer_count):
            if k == 0:
                source = values_ref[t, 0]
            else:
                source = values_ref[t, k] + above * reduced[t]
            reduced[t] = source / divisor
            out_ref[t, k] = reduced[t]
    result = reduced
    for k in range(level_count - 2, -1, -1):
        ratio = ratio_ref[k]
        for t in range(tracer_count):
            result[t] = out_ref[t, k] - ratio * result[t]
            out_ref[t, k] = result[t]


def vertical_mix(values, wet_mask, diffusivity):
    tracer_count, level_count, row_count, col_count = values.shape
    rows = 16 if row_count % 16 == 0 else row_count
    return pl.pallas_call(
        mix_kernel,
        grid=(row_count // rows,),
        in_specs=[
            pl.BlockSpec((tracer_count, level_count, rows, col_count), lambda i: (0, 0, i, 0)),
            pl.BlockSpec((level_count, rows, col_count), lambda i: (0, i, 0)),
            pl.BlockSpec((level_count, rows, col_count), lambda i: (0, i, 0)),
        ],
        out_specs=pl.BlockSpec((tracer_count, level_count, rows, col_count), lambda i: (0, 0, i, 0)),
        out_shape=jax.ShapeDtypeStruct(values.shape, jnp.float32),
        scratch_shapes=[pltpu.VMEM((level_count - 1, rows, col_count), jnp.float32)],
    )(values, wet_mask, diffusivity)


def nine_point(padded, wet_surface, centre_weight):
    centre = window(padded, 1, 1)
    edges = (
        window(padded, 0, 1) + window(padded, 2, 1) + window(padded, 1, 0) + window(padded, 1, 2)
    )
    corners = (
        window(padded, 0, 0) + window(padded, 0, 2) + window(padded, 2, 0) + window(padded, 2, 2)
    )
    return wet_surface * (centre_weight * centre - edges - corner_weight * corners)


def wrapped_extend(stacked, fold_signs):
    rows, cols = stacked.shape[2], stacked.shape[3]
    height = -(-(rows + 4) // 8) * 8
    width = -(-(cols + 4) // 128) * 128
    lead = stacked.shape[:2]
    lon_count = lax.axis_size("lon")
    lat_count = lax.axis_size("lat")
    east_halo = lax.ppermute(
        stacked[..., :2], "lon", [(i, (i - 1) % lon_count) for i in range(lon_count)]
    )
    west_halo = lax.ppermute(
        stacked[..., cols - 2 :], "lon", [(i, (i + 1) % lon_count) for i in range(lon_count)]
    )
    widened = jnp.concatenate(
        [stacked, east_halo, jnp.zeros(lead + (rows, width - cols - 4), stacked.dtype), west_halo],
        axis=3,
    )
    north_rows = lax.ppermute(widened[:, :, :2], "lat", [(j, j - 1) for j in range(1, lat_count)])
    south_rows = lax.ppermute(
        widened[:, :, rows - 2 :], "lat", [(j, j + 1) for j in range(lat_count - 1)]
    )
    mirrored = lax.ppermute(
        widened[:, :, rows - 2 :], "lon", [(i, lon_count - 1 - i) for i in range(lon_count)]
    )
    folded = jnp.roll(jnp.flip(mirrored, axis=(2, 3)), cols - width, axis=3) * fold_signs
    at_top = lax.axis_index("lat") == lat_count - 1
    north = jnp.where(at_top, folded, north_rows)
    return jnp.concatenate(
        [widened, north, jnp.zeros(lead + (height - rows - 4, width), stacked.dtype), south_rows],
        axis=2,
    )


def clinic_extend(stacked, fold_signs):
    row_count = stacked.shape[2]
    widened = extended_2(stacked, (("lon", 3),), 2, True)
    extended = extended_2(widened, (("lat", 2),), 2, False)
    top_rows = widened[:, :, row_count - 2 :, :]
    for bit in range(lax.axis_size("lon").bit_length() - 1):
        top_rows = from_partner(top_rows, "lon", bit)
    northern = jnp.flip(top_rows, axis=(2, 3)) * fold_signs
    at_top = lax.axis_index("lat") == lax.axis_size("lat") - 1
    ghost_rows = jnp.where(at_top, northern, extended[:, :, row_count + 2 :, :])
    return jnp.concatenate([extended[:, :, : row_count + 2, :], ghost_rows], axis=2)


def strip_pad(surface_field):
    lon_index = lax.axis_index("lon")
    lon_count = lax.axis_size("lon")
    first_row = surface_field[0:1, :]
    last_row = surface_field[-1:, :]
    following = passed_along(first_row, "lon", -1)
    following_far = shifted(following, "lat", -1)
    preceding = passed_along(last_row, "lon", 1)
    preceding_far = shifted(preceding, "lat", 1)
    above_row = jnp.where(lon_index == lon_count - 1, following_far, following)
    below_row = jnp.where(lon_index == 0, preceding_far, preceding)
    top_strip = jnp.logical_and(
        lon_index == lon_count - 1, lax.axis_index("lat") == lax.axis_size("lat") - 1
    )
    above_row = jnp.where(top_strip, jnp.flip(last_row, axis=1), above_row)
    extended = jnp.concatenate([below_row, surface_field, above_row], axis=0)
    return jnp.concatenate([extended[:, -1:], extended, extended[:, :1]], axis=1)


def strip_pad_joined(surface_field):
    lon_count = lax.axis_size("lon")
    lat_count = lax.axis_size("lat")
    strip_count = lon_count * lat_count
    axes = ("lon", "lat")

    def device(strip):
        return (strip % lon_count) * lat_count + strip // lon_count

    first_row = surface_field[0:1, :]
    last_row = surface_field[-1:, :]
    above_row = lax.ppermute(
        first_row, axes, [(device(s + 1), device(s)) for s in range(strip_count - 1)]
    )
    below_row = lax.ppermute(
        last_row, axes, [(device(s - 1), device(s)) for s in range(1, strip_count)]
    )
    top_strip = jnp.logical_and(
        lax.axis_index("lon") == lon_count - 1, lax.axis_index("lat") == lat_count - 1
    )
    above_row = jnp.where(top_strip, jnp.flip(last_row, axis=1), above_row)
    extended = jnp.concatenate([below_row, surface_field, above_row], axis=0)
    return jnp.concatenate([extended[:, -1:], extended, extended[:, :1]], axis=1)


def butterfly_sum(value):
    for axis in ("lon", "lat"):
        count = lax.axis_size(axis)
        bit = 1
        while bit < count:
            value = value + lax.ppermute(value, axis, [(i, i ^ bit) for i in range(count)])
            bit <<= 1
    return value


def solve(surface_source, wet_surface, centre_weight, padder):

    def precondition(residual):
        return wet_surface * residual / centre_weight

    def apply_operator(field):
        return nine_point(padder(field), wet_surface, centre_weight)

    solution = jnp.zeros_like(surface_source)
    residual = surface_source
    precond = precondition(residual)
    direction = precond
    operator_image = apply_operator(direction)
    totals = butterfly_sum(
        jnp.stack([jnp.sum(residual * precond), jnp.sum(direction * operator_image)])
    )
    resid_dot, curvature = totals[0], totals[1]
    for iteration in range(ITERS):
        step_size = resid_dot / curvature
        solution = solution + step_size * direction
        if iteration + 1 < ITERS:
            residual = residual - step_size * operator_image
            precond = precondition(residual)
            precond_image = apply_operator(precond)
            totals = butterfly_sum(
                jnp.stack(
                    [
                        jnp.sum(residual * precond),
                        jnp.sum(precond * precond_image),
                        jnp.sum(precond * operator_image),
                    ]
                )
            )
            dot_next = totals[0]
            ratio = dot_next / resid_dot
            direction = precond + ratio * direction
            curvature = totals[1] + 2.0 * ratio * totals[2] + ratio * ratio * curvature
            operator_image = precond_image + ratio * operator_image
            resid_dot = dot_next
    return solution


def shards(
    tracers,
    east_velocity,
    north_velocity,
    vertical_diffusivity,
    depth_levels,
    ocean_blocks,
    forcing,
    surface_coupling,
):
    level_count = tracers.shape[1]
    row_count = tracers.shape[2]
    col_count = tracers.shape[3]
    ocean_cells = jnp.repeat(
        jnp.repeat(ocean_blocks, row_count // ocean_blocks.shape[0], axis=0),
        col_count // ocean_blocks.shape[1],
        axis=1,
    ).astype(jnp.float32)
    level_index = lax.broadcasted_iota(jnp.int32, (level_count, row_count, col_count), 0)
    wet_mask = jnp.where(
        level_index < depth_levels[None], ocean_cells[None], jnp.zeros_like(ocean_cells)[None]
    )
    east_float = east_velocity.astype(jnp.float32)
    north_float = north_velocity.astype(jnp.float32)
    stacked = jnp.concatenate(
        [tracers, wet_mask[None], east_float[None], north_float[None]], axis=0
    )
    fold_signs = jnp.array([1.0, 1.0, 1.0, -1.0, -1.0], jnp.float32).reshape(5, 1, 1, 1)
    provisional = stencil_call(wrapped_extend(stacked, fold_signs), row_count, col_count)
    new_tracers = vertical_mix(provisional, wet_mask, vertical_diffusivity)
    wet_surface = wet_mask[0]
    surface_source = wet_surface * (forcing + jnp.mean(new_tracers[0] - new_tracers[1], axis=0))
    centre_weight = 6.0 + surface_coupling
    relaid = lax.all_to_all(
        jnp.stack([surface_source, wet_surface, centre_weight]),
        "lon",
        split_axis=1,
        concat_axis=2,
        tiled=True,
    )
    strip_solution = solve(relaid[0], relaid[1], relaid[2], strip_pad_joined)
    solution = lax.all_to_all(strip_solution, "lon", split_axis=1, concat_axis=0, tiled=True)
    return (new_tracers, solution)


def solution(mesh):
    placed = (
        P(None, None, "lat", "lon"),
        P(None, "lat", "lon"),
        P(None, "lat", "lon"),
        P(None, "lat", "lon"),
        P("lat", "lon"),
        P("lat", "lon"),
        P("lat", "lon"),
        P("lat", "lon"),
    )
    return jax.shard_map(
        shards,
        mesh=mesh,
        in_specs=placed,
        out_specs=(P(None, None, "lat", "lon"), P("lat", "lon")),
        check_vma=False,
    )
```

```python
import jax
import jax.numpy as jnp
from jax import lax
from jax.sharding import PartitionSpec as P
from jax.experimental import pallas as pl
from jax.experimental.pallas import tpu as pltpu

ITERS = 3


advection_rate = 0.25
biharmonic_rate = 0.01
corner_weight = 0.5


def extended_2(block, sides, width, periodic):
    for axis, dim in sides:
        count = lax.axis_size(axis)
        forward = [(i, i + 1) for i in range(count - 1)]
        if periodic:
            forward.append((count - 1, 0))
        backward = [(target, source) for source, target in forward]
        low = lax.ppermute(
            lax.slice_in_dim(block, block.shape[dim] - width, None, axis=dim), axis, forward
        )
        high = lax.ppermute(lax.slice_in_dim(block, 0, width, axis=dim), axis, backward)
        block = jnp.concatenate([low, block, high], axis=dim)
    return block


def from_partner(block, axis, stride):
    count = lax.axis_size(axis)
    route = []
    for low in range(count):
        high = low | 1 << stride
        if high != low and high < count:
            route += [(low, high), (high, low)]
    return lax.ppermute(block, axis, route)


def passed_along(value, axis, steps):
    count = lax.axis_size(axis)
    pairs = [(source, (source + steps) % count) for source in range(count)]
    return lax.ppermute(value, axis, pairs)


def shifted(shard, axis, by):
    count = lax.axis_size(axis)
    pairs = [(i, i + by) for i in range(count) if 0 <= i + by < count]
    return lax.ppermute(shard, axis, pairs)


def window(array, shift_row, shift_col):
    inner_height = array.shape[-2] - 2
    inner_width = array.shape[-1] - 2
    return array[..., shift_row : shift_row + inner_height, shift_col : shift_col + inner_width]


def masked_laplacian(values, wet_mask):
    centre = window(values, 1, 1)
    running = jnp.zeros_like(centre)
    for shift_row, shift_col in ((0, 1), (2, 1), (1, 0), (1, 2)):
        running = running + window(wet_mask, shift_row, shift_col) * (
            window(values, shift_row, shift_col) - centre
        )
    return window(wet_mask, 1, 1) * running


def face_flux(speed_one, speed_two, tracer_one, tracer_two, wet_one, wet_two):
    return 0.5 * (speed_one + speed_two) * 0.5 * (tracer_one + tracer_two) * wet_one * wet_two


def baroclinic(padded):
    tracer = padded[0:2]
    wet_mask = padded[2]
    inner_tracer = tracer[..., 1:-1, 1:-1]
    inner_mask = wet_mask[..., 1:-1, 1:-1]
    east_speed = padded[3][..., 1:-1, 1:-1]
    north_speed = padded[4][..., 1:-1, 1:-1]
    lap_one = masked_laplacian(tracer, wet_mask)
    lap_two = masked_laplacian(lap_one, inner_mask)
    centre = window(inner_tracer, 1, 1)
    wet_centre = window(inner_mask, 1, 1)
    east_flux = face_flux(
        window(east_speed, 1, 1),
        window(east_speed, 1, 2),
        centre,
        window(inner_tracer, 1, 2),
        wet_centre,
        window(inner_mask, 1, 2),
    )
    west_flux = face_flux(
        window(east_speed, 1, 0),
        window(east_speed, 1, 1),
        window(inner_tracer, 1, 0),
        centre,
        window(inner_mask, 1, 0),
        wet_centre,
    )
    north_flux = face_flux(
        window(north_speed, 1, 1),
        window(north_speed, 2, 1),
        centre,
        window(inner_tracer, 2, 1),
        wet_centre,
        window(inner_mask, 2, 1),
    )
    south_flux = face_flux(
        window(north_speed, 0, 1),
        window(north_speed, 1, 1),
        window(inner_tracer, 0, 1),
        centre,
        window(inner_mask, 0, 1),
        wet_centre,
    )
    divergence = east_flux - west_flux + north_flux - south_flux
    return wet_centre * (centre - advection_rate * divergence - biharmonic_rate * lap_two)


def stencil_body(field, out_ref):
    height, width = field(2).shape
    row_count, col_count = out_ref.shape[2], out_ref.shape[3]

    def south(x):
        return pltpu.roll(x, 1, 0)

    def north(x):
        return pltpu.roll(x, height - 1, 0)

    def west(x):
        return pltpu.roll(x, 1, 1)

    def east(x):
        return pltpu.roll(x, width - 1, 1)

    shifts = (south, north, west, east)
    wet = field(2)
    wet_near = [shift(wet) for shift in shifts]

    def laplacian(values):
        running = None
        for shift, wet_n in zip(shifts, wet_near):
            term = wet_n * (shift(values) - values)
            running = term if running is None else running + term
        return wet * running

    east_speed = field(3)
    north_speed = field(4)
    east_mean = 0.5 * (east_speed + east(east_speed))
    north_mean = 0.5 * (north_speed + north(north_speed))
    for t in range(out_ref.shape[0]):
        tracer = field(t)
        lap_two = laplacian(laplacian(tracer))
        east_flux = east_mean * 0.5 * (tracer + east(tracer)) * wet * wet_near[3]
        north_flux = north_mean * 0.5 * (tracer + north(tracer)) * wet * wet_near[1]
        divergence = east_flux - west(east_flux) + north_flux - south(north_flux)
        result = wet * (tracer - advection_rate * divergence - biharmonic_rate * lap_two)
        out_ref[t, 0] = result[:row_count, :col_count]


def stencil_kernel(ext_ref, out_ref):
    stencil_body(lambda f: ext_ref[f, 0], out_ref)


def assembling_kernel(tracer_ref, wet_ref, east_ref, north_ref, cols_ref, rows_ref, out_ref, ext_ref):
    rows, cols = wet_ref.shape[1], wet_ref.shape[2]
    interiors = (
        tracer_ref[0, 0],
        tracer_ref[1, 0],
        wet_ref[0],
        east_ref[0].astype(jnp.float32),
        north_ref[0].astype(jnp.float32),
    )
    for f, interior in enumerate(interiors):
        ext_ref[f, 0:rows, 0:cols] = interior
        ext_ref[f, 0:rows, cols:] = cols_ref[f, 0]
        ext_ref[f, rows:, :] = rows_ref[f, 0]
    stencil_body(lambda f: ext_ref[f], out_ref)


def halo_pieces(tracers, wet_mask, east_velocity, north_velocity, fold_signs):
    rows, cols = wet_mask.shape[1], wet_mask.shape[2]
    width = -(-(cols + 4) // 128) * 128
    lead = wet_mask.shape[:1]
    lon_count = lax.axis_size("lon")
    lat_count = lax.axis_size("lat")

    def fields(index):
        return jnp.concatenate(
            [
                tracers[index],
                wet_mask[None][index],
                east_velocity[None][index].astype(jnp.float32),
                north_velocity[None][index].astype(jnp.float32),
            ],
            axis=0,
        )

    every = slice(None)
    east_halo = lax.ppermute(
        fields((every, every, every, slice(0, 2))),
        "lon",
        [(i, (i - 1) % lon_count) for i in range(lon_count)],
    )
    west_halo = lax.ppermute(
        fields((every, every, every, slice(cols - 2, cols))),
        "lon",
        [(i, (i + 1) % lon_count) for i in range(lon_count)],
    )
    halo_cols = jnp.concatenate(
        [east_halo, jnp.zeros((5,) + lead + (rows, width - cols - 4), jnp.float32), west_halo],
        axis=3,
    )

    def widened_rows(start):
        band = (every, every, slice(start, start + 2))
        return jnp.concatenate([fields(band), halo_cols[band]], axis=3)

    bottom = widened_rows(0)
    top = widened_rows(rows - 2)
    north_rows = lax.ppermute(bottom, "lat", [(j, j - 1) for j in range(1, lat_count)])
    south_rows = lax.ppermute(top, "lat", [(j, j + 1) for j in range(lat_count - 1)])
    mirrored = lax.ppermute(top, "lon", [(i, lon_count - 1 - i) for i in range(lon_count)])
    folded = jnp.roll(jnp.flip(mirrored, axis=(2, 3)), cols - width, axis=3) * fold_signs
    at_top = lax.axis_index("lat") == lat_count - 1
    north = jnp.where(at_top, folded, north_rows)
    halo_rows = jnp.concatenate(
        [north, jnp.zeros((5,) + lead + (4, width), jnp.float32), south_rows], axis=2
    )
    return halo_cols, halo_rows


def assembling_call(tracers, wet_mask, east_velocity, north_velocity, fold_signs):
    halo_cols, halo_rows = halo_pieces(tracers, wet_mask, east_velocity, north_velocity, fold_signs)
    tracer_count, level_count, rows, cols = tracers.shape
    width = cols + halo_cols.shape[3]
    height = rows + halo_rows.shape[2]
    level_block = pl.BlockSpec((1, rows, cols), lambda k: (k, 0, 0))
    return pl.pallas_call(
        assembling_kernel,
        grid=(level_count,),
        in_specs=[
            pl.BlockSpec((tracer_count, 1, rows, cols), lambda k: (0, k, 0, 0)),
            level_block,
            level_block,
            level_block,
            pl.BlockSpec((5, 1, rows, halo_cols.shape[3]), lambda k: (0, k, 0, 0)),
            pl.BlockSpec((5, 1, halo_rows.shape[2], width), lambda k: (0, k, 0, 0)),
        ],
        out_specs=pl.BlockSpec((tracer_count, 1, rows, cols), lambda k: (0, k, 0, 0)),
        out_shape=jax.ShapeDtypeStruct(tracers.shape, jnp.float32),
        scratch_shapes=[pltpu.VMEM((5, height, width), jnp.float32)],
    )(tracers, wet_mask, east_velocity, north_velocity, halo_cols, halo_rows)


def wrapped_layout(padded):
    rows = padded.shape[2] - 4
    cols = padded.shape[3] - 4
    height = -(-(rows + 4) // 8) * 8
    width = -(-(cols + 4) // 128) * 128
    lead = padded.shape[:2]
    by_rows = jnp.concatenate(
        [
            padded[:, :, 2 : rows + 4],
            jnp.zeros(lead + (height - rows - 4, padded.shape[3]), padded.dtype),
            padded[:, :, 0:2],
        ],
        axis=2,
    )
    return jnp.concatenate(
        [
            by_rows[..., 2 : cols + 4],
            jnp.zeros(lead + (height, width - cols - 4), padded.dtype),
            by_rows[..., 0:2],
        ],
        axis=3,
    )


def stencil_call(ext, rows, cols):
    tracer_count = 2
    level_count = ext.shape[1]
    height, width = ext.shape[2], ext.shape[3]
    return pl.pallas_call(
        stencil_kernel,
        grid=(level_count,),
        in_specs=[pl.BlockSpec((ext.shape[0], 1, height, width), lambda k: (0, k, 0, 0))],
        out_specs=pl.BlockSpec((tracer_count, 1, rows, cols), lambda k: (0, k, 0, 0)),
        out_shape=jax.ShapeDtypeStruct((tracer_count, level_count, rows, cols), jnp.float32),
    )(ext)


def mix_kernel(values_ref, wet_ref, diff_ref, out_ref, ratio_ref):
    level_count = wet_ref.shape[0]
    tracer_count = values_ref.shape[0]

    def coupling(k):
        return diff_ref[k].astype(jnp.float32) * wet_ref[k] * wet_ref[k - 1]

    below = coupling(1)
    upper = None
    reduced = [None] * tracer_count
    for k in range(level_count):
        above = below
        below = coupling(k + 1) if k + 1 < level_count else None
        if k == 0:
            diagonal = 1.0 + below
            divisor = diagonal
        elif below is None:
            diagonal = 1.0 + above
            divisor = diagonal + above * upper
        else:
            diagonal = 1.0 + above + below
            divisor = diagonal + above * upper
        if below is not None:
            upper = -below / divisor
            ratio_ref[k] = upper
        for t in range(tracer_count):
            if k == 0:
                source = values_ref[t, 0]
            else:
                source = values_ref[t, k] + above * reduced[t]
            reduced[t] = source / divisor
            out_ref[t, k] = reduced[t]
    result = reduced
    for k in range(level_count - 2, -1, -1):
        ratio = ratio_ref[k]
        for t in range(tracer_count):
            result[t] = out_ref[t, k] - ratio * result[t]
            out_ref[t, k] = result[t]


def vertical_mix(values, wet_mask, diffusivity):
    tracer_count, level_count, row_count, col_count = values.shape
    rows = 16 if row_count % 16 == 0 else row_count
    return pl.pallas_call(
        mix_kernel,
        grid=(row_count // rows,),
        in_specs=[
            pl.BlockSpec((tracer_count, level_count, rows, col_count), lambda i: (0, 0, i, 0)),
            pl.BlockSpec((level_count, rows, col_count), lambda i: (0, i, 0)),
            pl.BlockSpec((level_count, rows, col_count), lambda i: (0, i, 0)),
        ],
        out_specs=pl.BlockSpec((tracer_count, level_count, rows, col_count), lambda i: (0, 0, i, 0)),
        out_shape=jax.ShapeDtypeStruct(values.shape, jnp.float32),
        scratch_shapes=[pltpu.VMEM((level_count - 1, rows, col_count), jnp.float32)],
    )(values, wet_mask, diffusivity)


def nine_point(padded, wet_surface, centre_weight):
    centre = window(padded, 1, 1)
    edges = (
        window(padded, 0, 1) + window(padded, 2, 1) + window(padded, 1, 0) + window(padded, 1, 2)
    )
    corners = (
        window(padded, 0, 0) + window(padded, 0, 2) + window(padded, 2, 0) + window(padded, 2, 2)
    )
    return wet_surface * (centre_weight * centre - edges - corner_weight * corners)


def wrapped_extend(stacked, fold_signs):
    rows, cols = stacked.shape[2], stacked.shape[3]
    height = -(-(rows + 4) // 8) * 8
    width = -(-(cols + 4) // 128) * 128
    lead = stacked.shape[:2]
    lon_count = lax.axis_size("lon")
    lat_count = lax.axis_size("lat")
    east_halo = lax.ppermute(
        stacked[..., :2], "lon", [(i, (i - 1) % lon_count) for i in range(lon_count)]
    )
    west_halo = lax.ppermute(
        stacked[..., cols - 2 :], "lon", [(i, (i + 1) % lon_count) for i in range(lon_count)]
    )
    widened = jnp.concatenate(
        [stacked, east_halo, jnp.zeros(lead + (rows, width - cols - 4), stacked.dtype), west_halo],
        axis=3,
    )
    north_rows = lax.ppermute(widened[:, :, :2], "lat", [(j, j - 1) for j in range(1, lat_count)])
    south_rows = lax.ppermute(
        widened[:, :, rows - 2 :], "lat", [(j, j + 1) for j in range(lat_count - 1)]
    )
    mirrored = lax.ppermute(
        widened[:, :, rows - 2 :], "lon", [(i, lon_count - 1 - i) for i in range(lon_count)]
    )
    folded = jnp.roll(jnp.flip(mirrored, axis=(2, 3)), cols - width, axis=3) * fold_signs
    at_top = lax.axis_index("lat") == lat_count - 1
    north = jnp.where(at_top, folded, north_rows)
    return jnp.concatenate(
        [widened, north, jnp.zeros(lead + (height - rows - 4, width), stacked.dtype), south_rows],
        axis=2,
    )


def clinic_extend(stacked, fold_signs):
    row_count = stacked.shape[2]
    widened = extended_2(stacked, (("lon", 3),), 2, True)
    extended = extended_2(widened, (("lat", 2),), 2, False)
    top_rows = widened[:, :, row_count - 2 :, :]
    for bit in range(lax.axis_size("lon").bit_length() - 1):
        top_rows = from_partner(top_rows, "lon", bit)
    northern = jnp.flip(top_rows, axis=(2, 3)) * fold_signs
    at_top = lax.axis_index("lat") == lax.axis_size("lat") - 1
    ghost_rows = jnp.where(at_top, northern, extended[:, :, row_count + 2 :, :])
    return jnp.concatenate([extended[:, :, : row_count + 2, :], ghost_rows], axis=2)


def strip_pad(surface_field):
    lon_index = lax.axis_index("lon")
    lon_count = lax.axis_size("lon")
    first_row = surface_field[0:1, :]
    last_row = surface_field[-1:, :]
    following = passed_along(first_row, "lon", -1)
    following_far = shifted(following, "lat", -1)
    preceding = passed_along(last_row, "lon", 1)
    preceding_far = shifted(preceding, "lat", 1)
    above_row = jnp.where(lon_index == lon_count - 1, following_far, following)
    below_row = jnp.where(lon_index == 0, preceding_far, preceding)
    top_strip = jnp.logical_and(
        lon_index == lon_count - 1, lax.axis_index("lat") == lax.axis_size("lat") - 1
    )
    above_row = jnp.where(top_strip, jnp.flip(last_row, axis=1), above_row)
    extended = jnp.concatenate([below_row, surface_field, above_row], axis=0)
    return jnp.concatenate([extended[:, -1:], extended, extended[:, :1]], axis=1)


def strip_pad_joined(surface_field):
    lon_count = lax.axis_size("lon")
    lat_count = lax.axis_size("lat")
    strip_count = lon_count * lat_count
    axes = ("lon", "lat")

    def device(strip):
        return (strip % lon_count) * lat_count + strip // lon_count

    first_row = surface_field[0:1, :]
    last_row = surface_field[-1:, :]
    above_row = lax.ppermute(
        first_row, axes, [(device(s + 1), device(s)) for s in range(strip_count - 1)]
    )
    below_row = lax.ppermute(
        last_row, axes, [(device(s - 1), device(s)) for s in range(1, strip_count)]
    )
    top_strip = jnp.logical_and(
        lax.axis_index("lon") == lon_count - 1, lax.axis_index("lat") == lat_count - 1
    )
    above_row = jnp.where(top_strip, jnp.flip(last_row, axis=1), above_row)
    extended = jnp.concatenate([below_row, surface_field, above_row], axis=0)
    return jnp.concatenate([extended[:, -1:], extended, extended[:, :1]], axis=1)


def butterfly_sum(value):
    for axis in ("lon", "lat"):
        count = lax.axis_size(axis)
        bit = 1
        while bit < count:
            value = value + lax.ppermute(value, axis, [(i, i ^ bit) for i in range(count)])
            bit <<= 1
    return value


def solve(surface_source, wet_surface, centre_weight, padder):

    def precondition(residual):
        return wet_surface * residual / centre_weight

    def apply_operator(field):
        return nine_point(padder(field), wet_surface, centre_weight)

    solution = jnp.zeros_like(surface_source)
    residual = surface_source
    precond = precondition(residual)
    direction = precond
    operator_image = apply_operator(direction)
    totals = butterfly_sum(
        jnp.stack([jnp.sum(residual * precond), jnp.sum(direction * operator_image)])
    )
    resid_dot, curvature = totals[0], totals[1]
    for iteration in range(ITERS):
        step_size = resid_dot / curvature
        solution = solution + step_size * direction
        if iteration + 1 < ITERS:
            residual = residual - step_size * operator_image
            precond = precondition(residual)
            precond_image = apply_operator(precond)
            totals = butterfly_sum(
                jnp.stack(
                    [
                        jnp.sum(residual * precond),
                        jnp.sum(precond * precond_image),
                        jnp.sum(precond * operator_image),
                    ]
                )
            )
            dot_next = totals[0]
            ratio = dot_next / resid_dot
            direction = precond + ratio * direction
            curvature = totals[1] + 2.0 * ratio * totals[2] + ratio * ratio * curvature
            operator_image = precond_image + ratio * operator_image
            resid_dot = dot_next
    return solution


def shards(
    tracers,
    east_velocity,
    north_velocity,
    vertical_diffusivity,
    depth_levels,
    ocean_blocks,
    forcing,
    surface_coupling,
):
    level_count = tracers.shape[1]
    row_count = tracers.shape[2]
    col_count = tracers.shape[3]
    ocean_cells = jnp.repeat(
        jnp.repeat(ocean_blocks, row_count // ocean_blocks.shape[0], axis=0),
        col_count // ocean_blocks.shape[1],
        axis=1,
    ).astype(jnp.float32)
    level_index = lax.broadcasted_iota(jnp.int32, (level_count, row_count, col_count), 0)
    wet_mask = jnp.where(
        level_index < depth_levels[None], ocean_cells[None], jnp.zeros_like(ocean_cells)[None]
    )
    fold_signs = jnp.array([1.0, 1.0, 1.0, -1.0, -1.0], jnp.float32).reshape(5, 1, 1, 1)
    provisional = assembling_call(tracers, wet_mask, east_velocity, north_velocity, fold_signs)
    new_tracers = vertical_mix(provisional, wet_mask, vertical_diffusivity)
    wet_surface = wet_mask[0]
    surface_source = wet_surface * (forcing + jnp.mean(new_tracers[0] - new_tracers[1], axis=0))
    centre_weight = 6.0 + surface_coupling
    relaid = lax.all_to_all(
        jnp.stack([surface_source, wet_surface, centre_weight]),
        "lon",
        split_axis=1,
        concat_axis=2,
        tiled=True,
    )
    strip_solution = solve(relaid[0], relaid[1], relaid[2], strip_pad_joined)
    solution = lax.all_to_all(strip_solution, "lon", split_axis=1, concat_axis=0, tiled=True)
    return (new_tracers, solution)


def solution(mesh):
    placed = (
        P(None, None, "lat", "lon"),
        P(None, "lat", "lon"),
        P(None, "lat", "lon"),
        P(None, "lat", "lon"),
        P("lat", "lon"),
        P("lat", "lon"),
        P("lat", "lon"),
        P("lat", "lon"),
    )
    return jax.shard_map(
        shards,
        mesh=mesh,
        in_specs=placed,
        out_specs=(P(None, None, "lat", "lon"), P("lat", "lon")),
        check_vma=False,
    )
```

```python
import jax
import jax.numpy as jnp
from jax import lax
from jax.sharding import PartitionSpec as P
from jax.experimental import pallas as pl
from jax.experimental.pallas import tpu as pltpu

ITERS = 3


advection_rate = 0.25
biharmonic_rate = 0.01
corner_weight = 0.5


def extended_2(block, sides, width, periodic):
    for axis, dim in sides:
        count = lax.axis_size(axis)
        forward = [(i, i + 1) for i in range(count - 1)]
        if periodic:
            forward.append((count - 1, 0))
        backward = [(target, source) for source, target in forward]
        low = lax.ppermute(
            lax.slice_in_dim(block, block.shape[dim] - width, None, axis=dim), axis, forward
        )
        high = lax.ppermute(lax.slice_in_dim(block, 0, width, axis=dim), axis, backward)
        block = jnp.concatenate([low, block, high], axis=dim)
    return block


def from_partner(block, axis, stride):
    count = lax.axis_size(axis)
    route = []
    for low in range(count):
        high = low | 1 << stride
        if high != low and high < count:
            route += [(low, high), (high, low)]
    return lax.ppermute(block, axis, route)


def passed_along(value, axis, steps):
    count = lax.axis_size(axis)
    pairs = [(source, (source + steps) % count) for source in range(count)]
    return lax.ppermute(value, axis, pairs)


def shifted(shard, axis, by):
    count = lax.axis_size(axis)
    pairs = [(i, i + by) for i in range(count) if 0 <= i + by < count]
    return lax.ppermute(shard, axis, pairs)


def window(array, shift_row, shift_col):
    inner_height = array.shape[-2] - 2
    inner_width = array.shape[-1] - 2
    return array[..., shift_row : shift_row + inner_height, shift_col : shift_col + inner_width]


def masked_laplacian(values, wet_mask):
    centre = window(values, 1, 1)
    running = jnp.zeros_like(centre)
    for shift_row, shift_col in ((0, 1), (2, 1), (1, 0), (1, 2)):
        running = running + window(wet_mask, shift_row, shift_col) * (
            window(values, shift_row, shift_col) - centre
        )
    return window(wet_mask, 1, 1) * running


def face_flux(speed_one, speed_two, tracer_one, tracer_two, wet_one, wet_two):
    return 0.5 * (speed_one + speed_two) * 0.5 * (tracer_one + tracer_two) * wet_one * wet_two


def baroclinic(padded):
    tracer = padded[0:2]
    wet_mask = padded[2]
    inner_tracer = tracer[..., 1:-1, 1:-1]
    inner_mask = wet_mask[..., 1:-1, 1:-1]
    east_speed = padded[3][..., 1:-1, 1:-1]
    north_speed = padded[4][..., 1:-1, 1:-1]
    lap_one = masked_laplacian(tracer, wet_mask)
    lap_two = masked_laplacian(lap_one, inner_mask)
    centre = window(inner_tracer, 1, 1)
    wet_centre = window(inner_mask, 1, 1)
    east_flux = face_flux(
        window(east_speed, 1, 1),
        window(east_speed, 1, 2),
        centre,
        window(inner_tracer, 1, 2),
        wet_centre,
        window(inner_mask, 1, 2),
    )
    west_flux = face_flux(
        window(east_speed, 1, 0),
        window(east_speed, 1, 1),
        window(inner_tracer, 1, 0),
        centre,
        window(inner_mask, 1, 0),
        wet_centre,
    )
    north_flux = face_flux(
        window(north_speed, 1, 1),
        window(north_speed, 2, 1),
        centre,
        window(inner_tracer, 2, 1),
        wet_centre,
        window(inner_mask, 2, 1),
    )
    south_flux = face_flux(
        window(north_speed, 0, 1),
        window(north_speed, 1, 1),
        window(inner_tracer, 0, 1),
        centre,
        window(inner_mask, 0, 1),
        wet_centre,
    )
    divergence = east_flux - west_flux + north_flux - south_flux
    return wet_centre * (centre - advection_rate * divergence - biharmonic_rate * lap_two)


def stencil_body(field, out_ref):
    height, width = field(2).shape
    row_count, col_count = out_ref.shape[2], out_ref.shape[3]

    def south(x):
        return pltpu.roll(x, 1, 0)

    def north(x):
        return pltpu.roll(x, height - 1, 0)

    def west(x):
        return pltpu.roll(x, 1, 1)

    def east(x):
        return pltpu.roll(x, width - 1, 1)

    shifts = (south, north, west, east)
    wet = field(2)
    wet_near = [shift(wet) for shift in shifts]

    def laplacian(values):
        running = None
        for shift, wet_n in zip(shifts, wet_near):
            term = wet_n * (shift(values) - values)
            running = term if running is None else running + term
        return wet * running

    east_speed = field(3)
    north_speed = field(4)
    east_mean = 0.5 * (east_speed + east(east_speed))
    north_mean = 0.5 * (north_speed + north(north_speed))
    for t in range(out_ref.shape[0]):
        tracer = field(t)
        lap_two = laplacian(laplacian(tracer))
        east_flux = east_mean * 0.5 * (tracer + east(tracer)) * wet * wet_near[3]
        north_flux = north_mean * 0.5 * (tracer + north(tracer)) * wet * wet_near[1]
        divergence = east_flux - west(east_flux) + north_flux - south(north_flux)
        result = wet * (tracer - advection_rate * divergence - biharmonic_rate * lap_two)
        out_ref[t, 0] = result[:row_count, :col_count]


def stencil_kernel(ext_ref, out_ref):
    stencil_body(lambda f: ext_ref[f, 0], out_ref)


def assembling_kernel(tracer_ref, wet_ref, east_ref, north_ref, cols_ref, rows_ref, out_ref, ext_ref):
    rows, cols = wet_ref.shape[1], wet_ref.shape[2]
    interiors = (
        tracer_ref[0, 0],
        tracer_ref[1, 0],
        wet_ref[0],
        east_ref[0].astype(jnp.float32),
        north_ref[0].astype(jnp.float32),
    )
    for f, interior in enumerate(interiors):
        ext_ref[f, 0:rows, 0:cols] = interior
        ext_ref[f, 0:rows, cols:] = cols_ref[f, 0]
        ext_ref[f, rows:, :] = rows_ref[f, 0]
    stencil_body(lambda f: ext_ref[f], out_ref)


def halo_pieces(tracers, wet_mask, east_velocity, north_velocity, fold_signs):
    rows, cols = wet_mask.shape[1], wet_mask.shape[2]
    width = -(-(cols + 4) // 128) * 128
    lead = wet_mask.shape[:1]
    lon_count = lax.axis_size("lon")
    lat_count = lax.axis_size("lat")

    def fields(index):
        return jnp.concatenate(
            [
                tracers[index],
                wet_mask[None][index],
                east_velocity[None][index].astype(jnp.float32),
                north_velocity[None][index].astype(jnp.float32),
            ],
            axis=0,
        )

    every = slice(None)
    east_halo = lax.ppermute(
        fields((every, every, every, slice(0, 2))),
        "lon",
        [(i, (i - 1) % lon_count) for i in range(lon_count)],
    )
    west_halo = lax.ppermute(
        fields((every, every, every, slice(cols - 2, cols))),
        "lon",
        [(i, (i + 1) % lon_count) for i in range(lon_count)],
    )
    halo_cols = jnp.concatenate(
        [east_halo, jnp.zeros((5,) + lead + (rows, width - cols - 4), jnp.float32), west_halo],
        axis=3,
    )

    def widened_rows(start):
        band = (every, every, slice(start, start + 2))
        return jnp.concatenate([fields(band), halo_cols[band]], axis=3)

    bottom = widened_rows(0)
    top = widened_rows(rows - 2)
    north_rows = lax.ppermute(bottom, "lat", [(j, j - 1) for j in range(1, lat_count)])
    south_rows = lax.ppermute(top, "lat", [(j, j + 1) for j in range(lat_count - 1)])
    mirrored = lax.ppermute(top, "lon", [(i, lon_count - 1 - i) for i in range(lon_count)])
    folded = jnp.roll(jnp.flip(mirrored, axis=(2, 3)), cols - width, axis=3) * fold_signs
    at_top = lax.axis_index("lat") == lat_count - 1
    north = jnp.where(at_top, folded, north_rows)
    halo_rows = jnp.concatenate(
        [north, jnp.zeros((5,) + lead + (4, width), jnp.float32), south_rows], axis=2
    )
    return halo_cols, halo_rows


def assembling_call(tracers, wet_mask, east_velocity, north_velocity, fold_signs):
    halo_cols, halo_rows = halo_pieces(tracers, wet_mask, east_velocity, north_velocity, fold_signs)
    tracer_count, level_count, rows, cols = tracers.shape
    width = cols + halo_cols.shape[3]
    height = rows + halo_rows.shape[2]
    level_block = pl.BlockSpec((1, rows, cols), lambda k: (k, 0, 0))
    return pl.pallas_call(
        assembling_kernel,
        grid=(level_count,),
        in_specs=[
            pl.BlockSpec((tracer_count, 1, rows, cols), lambda k: (0, k, 0, 0)),
            level_block,
            level_block,
            level_block,
            pl.BlockSpec((5, 1, rows, halo_cols.shape[3]), lambda k: (0, k, 0, 0)),
            pl.BlockSpec((5, 1, halo_rows.shape[2], width), lambda k: (0, k, 0, 0)),
        ],
        out_specs=pl.BlockSpec((tracer_count, 1, rows, cols), lambda k: (0, k, 0, 0)),
        out_shape=jax.ShapeDtypeStruct(tracers.shape, jnp.float32),
        scratch_shapes=[pltpu.VMEM((5, height, width), jnp.float32)],
    )(tracers, wet_mask, east_velocity, north_velocity, halo_cols, halo_rows)


def wrapped_layout(padded):
    rows = padded.shape[2] - 4
    cols = padded.shape[3] - 4
    height = -(-(rows + 4) // 8) * 8
    width = -(-(cols + 4) // 128) * 128
    lead = padded.shape[:2]
    by_rows = jnp.concatenate(
        [
            padded[:, :, 2 : rows + 4],
            jnp.zeros(lead + (height - rows - 4, padded.shape[3]), padded.dtype),
            padded[:, :, 0:2],
        ],
        axis=2,
    )
    return jnp.concatenate(
        [
            by_rows[..., 2 : cols + 4],
            jnp.zeros(lead + (height, width - cols - 4), padded.dtype),
            by_rows[..., 0:2],
        ],
        axis=3,
    )


def stencil_call(ext, rows, cols):
    tracer_count = 2
    level_count = ext.shape[1]
    height, width = ext.shape[2], ext.shape[3]
    return pl.pallas_call(
        stencil_kernel,
        grid=(level_count,),
        in_specs=[pl.BlockSpec((ext.shape[0], 1, height, width), lambda k: (0, k, 0, 0))],
        out_specs=pl.BlockSpec((tracer_count, 1, rows, cols), lambda k: (0, k, 0, 0)),
        out_shape=jax.ShapeDtypeStruct((tracer_count, level_count, rows, cols), jnp.float32),
    )(ext)


def mix_kernel(values_ref, wet_ref, diff_ref, out_ref, ratio_ref):
    level_count = wet_ref.shape[0]
    tracer_count = values_ref.shape[0]

    def coupling(k):
        return diff_ref[k].astype(jnp.float32) * wet_ref[k] * wet_ref[k - 1]

    below = coupling(1)
    upper = None
    reduced = [None] * tracer_count
    for k in range(level_count):
        above = below
        below = coupling(k + 1) if k + 1 < level_count else None
        if k == 0:
            diagonal = 1.0 + below
            divisor = diagonal
        elif below is None:
            diagonal = 1.0 + above
            divisor = diagonal + above * upper
        else:
            diagonal = 1.0 + above + below
            divisor = diagonal + above * upper
        if below is not None:
            upper = -below / divisor
            ratio_ref[k] = upper
        for t in range(tracer_count):
            if k == 0:
                source = values_ref[t, 0]
            else:
                source = values_ref[t, k] + above * reduced[t]
            reduced[t] = source / divisor
            out_ref[t, k] = reduced[t]
    result = reduced
    for k in range(level_count - 2, -1, -1):
        ratio = ratio_ref[k]
        for t in range(tracer_count):
            result[t] = out_ref[t, k] - ratio * result[t]
            out_ref[t, k] = result[t]


def vertical_mix(values, wet_mask, diffusivity):
    tracer_count, level_count, row_count, col_count = values.shape
    rows = 16 if row_count % 16 == 0 else row_count
    return pl.pallas_call(
        mix_kernel,
        grid=(row_count // rows,),
        in_specs=[
            pl.BlockSpec((tracer_count, level_count, rows, col_count), lambda i: (0, 0, i, 0)),
            pl.BlockSpec((level_count, rows, col_count), lambda i: (0, i, 0)),
            pl.BlockSpec((level_count, rows, col_count), lambda i: (0, i, 0)),
        ],
        out_specs=pl.BlockSpec((tracer_count, level_count, rows, col_count), lambda i: (0, 0, i, 0)),
        out_shape=jax.ShapeDtypeStruct(values.shape, jnp.float32),
        scratch_shapes=[pltpu.VMEM((level_count - 1, rows, col_count), jnp.float32)],
    )(values, wet_mask, diffusivity)


def nine_point(padded, wet_surface, centre_weight):
    centre = window(padded, 1, 1)
    edges = (
        window(padded, 0, 1) + window(padded, 2, 1) + window(padded, 1, 0) + window(padded, 1, 2)
    )
    corners = (
        window(padded, 0, 0) + window(padded, 0, 2) + window(padded, 2, 0) + window(padded, 2, 2)
    )
    return wet_surface * (centre_weight * centre - edges - corner_weight * corners)


def wrapped_extend(stacked, fold_signs):
    rows, cols = stacked.shape[2], stacked.shape[3]
    height = -(-(rows + 4) // 8) * 8
    width = -(-(cols + 4) // 128) * 128
    lead = stacked.shape[:2]
    lon_count = lax.axis_size("lon")
    lat_count = lax.axis_size("lat")
    east_halo = lax.ppermute(
        stacked[..., :2], "lon", [(i, (i - 1) % lon_count) for i in range(lon_count)]
    )
    west_halo = lax.ppermute(
        stacked[..., cols - 2 :], "lon", [(i, (i + 1) % lon_count) for i in range(lon_count)]
    )
    widened = jnp.concatenate(
        [stacked, east_halo, jnp.zeros(lead + (rows, width - cols - 4), stacked.dtype), west_halo],
        axis=3,
    )
    north_rows = lax.ppermute(widened[:, :, :2], "lat", [(j, j - 1) for j in range(1, lat_count)])
    south_rows = lax.ppermute(
        widened[:, :, rows - 2 :], "lat", [(j, j + 1) for j in range(lat_count - 1)]
    )
    mirrored = lax.ppermute(
        widened[:, :, rows - 2 :], "lon", [(i, lon_count - 1 - i) for i in range(lon_count)]
    )
    folded = jnp.roll(jnp.flip(mirrored, axis=(2, 3)), cols - width, axis=3) * fold_signs
    at_top = lax.axis_index("lat") == lat_count - 1
    north = jnp.where(at_top, folded, north_rows)
    return jnp.concatenate(
        [widened, north, jnp.zeros(lead + (height - rows - 4, width), stacked.dtype), south_rows],
        axis=2,
    )


def clinic_extend(stacked, fold_signs):
    row_count = stacked.shape[2]
    widened = extended_2(stacked, (("lon", 3),), 2, True)
    extended = extended_2(widened, (("lat", 2),), 2, False)
    top_rows = widened[:, :, row_count - 2 :, :]
    for bit in range(lax.axis_size("lon").bit_length() - 1):
        top_rows = from_partner(top_rows, "lon", bit)
    northern = jnp.flip(top_rows, axis=(2, 3)) * fold_signs
    at_top = lax.axis_index("lat") == lax.axis_size("lat") - 1
    ghost_rows = jnp.where(at_top, northern, extended[:, :, row_count + 2 :, :])
    return jnp.concatenate([extended[:, :, : row_count + 2, :], ghost_rows], axis=2)


def strip_pad(surface_field):
    lon_index = lax.axis_index("lon")
    lon_count = lax.axis_size("lon")
    first_row = surface_field[0:1, :]
    last_row = surface_field[-1:, :]
    following = passed_along(first_row, "lon", -1)
    following_far = shifted(following, "lat", -1)
    preceding = passed_along(last_row, "lon", 1)
    preceding_far = shifted(preceding, "lat", 1)
    above_row = jnp.where(lon_index == lon_count - 1, following_far, following)
    below_row = jnp.where(lon_index == 0, preceding_far, preceding)
    top_strip = jnp.logical_and(
        lon_index == lon_count - 1, lax.axis_index("lat") == lax.axis_size("lat") - 1
    )
    above_row = jnp.where(top_strip, jnp.flip(last_row, axis=1), above_row)
    extended = jnp.concatenate([below_row, surface_field, above_row], axis=0)
    return jnp.concatenate([extended[:, -1:], extended, extended[:, :1]], axis=1)


def strip_pad_joined(surface_field):
    lon_count = lax.axis_size("lon")
    lat_count = lax.axis_size("lat")
    strip_count = lon_count * lat_count
    axes = ("lon", "lat")

    def device(strip):
        return (strip % lon_count) * lat_count + strip // lon_count

    first_row = surface_field[0:1, :]
    last_row = surface_field[-1:, :]
    above_row = lax.ppermute(
        first_row, axes, [(device(s + 1), device(s)) for s in range(strip_count - 1)]
    )
    below_row = lax.ppermute(
        last_row, axes, [(device(s - 1), device(s)) for s in range(1, strip_count)]
    )
    top_strip = jnp.logical_and(
        lax.axis_index("lon") == lon_count - 1, lax.axis_index("lat") == lat_count - 1
    )
    above_row = jnp.where(top_strip, jnp.flip(last_row, axis=1), above_row)
    extended = jnp.concatenate([below_row, surface_field, above_row], axis=0)
    return jnp.concatenate([extended[:, -1:], extended, extended[:, :1]], axis=1)


def butterfly_sum(value):
    for axis in ("lon", "lat"):
        count = lax.axis_size(axis)
        bit = 1
        while bit < count:
            value = value + lax.ppermute(value, axis, [(i, i ^ bit) for i in range(count)])
            bit <<= 1
    return value


def neighbour_rows(values):
    lon_count = lax.axis_size("lon")
    lat_count = lax.axis_size("lat")
    strip_count = lon_count * lat_count
    axes = ("lon", "lat")

    def device(strip):
        return (strip % lon_count) * lat_count + strip // lon_count

    above = lax.ppermute(
        values[:, 0:1, :], axes, [(device(s + 1), device(s)) for s in range(strip_count - 1)]
    )
    below = lax.ppermute(
        values[:, -1:, :], axes, [(device(s - 1), device(s)) for s in range(1, strip_count)]
    )
    return above, below


def strip_assemble(surface_field, above_row, below_row):
    top_strip = jnp.logical_and(
        lax.axis_index("lon") == lax.axis_size("lon") - 1,
        lax.axis_index("lat") == lax.axis_size("lat") - 1,
    )
    above_row = jnp.where(top_strip, jnp.flip(surface_field[-1:, :], axis=1), above_row)
    extended = jnp.concatenate([below_row, surface_field, above_row], axis=0)
    return jnp.concatenate([extended[:, -1:], extended, extended[:, :1]], axis=1)


def solve(surface_source, wet_surface, centre_weight):

    def precondition(residual, wet, weight):
        return wet * residual / weight

    def apply_operator(field, above, below):
        return nine_point(strip_assemble(field, above, below), wet_surface, centre_weight)

    rim_above, rim_below = neighbour_rows(jnp.stack([wet_surface, centre_weight, surface_source]))
    solution = jnp.zeros_like(surface_source)
    residual = surface_source
    resid_rims = [rim_above[2], rim_below[2]]
    weight_rims = [
        (rim[0], jnp.where(rim[1] == 0.0, 1.0, rim[1])) for rim in (rim_above, rim_below)
    ]
    precond = precondition(residual, wet_surface, centre_weight)
    direction = precond
    operator_image = apply_operator(
        direction,
        *[precondition(r, w, c) for r, (w, c) in zip(resid_rims, weight_rims)],
    )
    image_above, image_below = neighbour_rows(operator_image[None])
    image_rims = [image_above[0], image_below[0]]
    totals = butterfly_sum(
        jnp.stack([jnp.sum(residual * precond), jnp.sum(direction * operator_image)])
    )
    resid_dot, curvature = totals[0], totals[1]
    for iteration in range(ITERS):
        step_size = resid_dot / curvature
        solution = solution + step_size * direction
        if iteration + 1 < ITERS:
            residual = residual - step_size * operator_image
            resid_rims = [r - step_size * a for r, a in zip(resid_rims, image_rims)]
            precond = precondition(residual, wet_surface, centre_weight)
            precond_image = apply_operator(
                precond,
                *[precondition(r, w, c) for r, (w, c) in zip(resid_rims, weight_rims)],
            )
            if iteration + 2 < ITERS:
                fresh_above, fresh_below = neighbour_rows(precond_image[None])
                fresh_rims = [fresh_above[0], fresh_below[0]]
            totals = butterfly_sum(
                jnp.stack(
                    [
                        jnp.sum(residual * precond),
                        jnp.sum(precond * precond_image),
                        jnp.sum(precond * operator_image),
                    ]
                )
            )
            dot_next = totals[0]
            ratio = dot_next / resid_dot
            direction = precond + ratio * direction
            curvature = totals[1] + 2.0 * ratio * totals[2] + ratio * ratio * curvature
            operator_image = precond_image + ratio * operator_image
            if iteration + 2 < ITERS:
                image_rims = [f + ratio * a for f, a in zip(fresh_rims, image_rims)]
            resid_dot = dot_next
    return solution


def shards(
    tracers,
    east_velocity,
    north_velocity,
    vertical_diffusivity,
    depth_levels,
    ocean_blocks,
    forcing,
    surface_coupling,
):
    level_count = tracers.shape[1]
    row_count = tracers.shape[2]
    col_count = tracers.shape[3]
    ocean_cells = jnp.repeat(
        jnp.repeat(ocean_blocks, row_count // ocean_blocks.shape[0], axis=0),
        col_count // ocean_blocks.shape[1],
        axis=1,
    ).astype(jnp.float32)
    level_index = lax.broadcasted_iota(jnp.int32, (level_count, row_count, col_count), 0)
    wet_mask = jnp.where(
        level_index < depth_levels[None], ocean_cells[None], jnp.zeros_like(ocean_cells)[None]
    )
    fold_signs = jnp.array([1.0, 1.0, 1.0, -1.0, -1.0], jnp.float32).reshape(5, 1, 1, 1)
    provisional = assembling_call(tracers, wet_mask, east_velocity, north_velocity, fold_signs)
    new_tracers = vertical_mix(provisional, wet_mask, vertical_diffusivity)
    wet_surface = wet_mask[0]
    surface_source = wet_surface * (forcing + jnp.mean(new_tracers[0] - new_tracers[1], axis=0))
    centre_weight = 6.0 + surface_coupling
    relaid = lax.all_to_all(
        jnp.stack([surface_source, wet_surface, centre_weight]),
        "lon",
        split_axis=1,
        concat_axis=2,
        tiled=True,
    )
    strip_solution = solve(relaid[0], relaid[1], relaid[2])
    solution = lax.all_to_all(strip_solution, "lon", split_axis=1, concat_axis=0, tiled=True)
    return (new_tracers, solution)


def solution(mesh):
    placed = (
        P(None, None, "lat", "lon"),
        P(None, "lat", "lon"),
        P(None, "lat", "lon"),
        P(None, "lat", "lon"),
        P("lat", "lon"),
        P("lat", "lon"),
        P("lat", "lon"),
        P("lat", "lon"),
    )
    return jax.shard_map(
        shards,
        mesh=mesh,
        in_specs=placed,
        out_specs=(P(None, None, "lat", "lon"), P("lat", "lon")),
        check_vma=False,
    )
```

```python
import jax
import jax.numpy as jnp
from jax import lax
from jax.sharding import PartitionSpec as P
from jax.experimental import pallas as pl
from jax.experimental.pallas import tpu as pltpu

ITERS = 3


advection_rate = 0.25
biharmonic_rate = 0.01
corner_weight = 0.5


def extended_2(block, sides, width, periodic):
    for axis, dim in sides:
        count = lax.axis_size(axis)
        forward = [(i, i + 1) for i in range(count - 1)]
        if periodic:
            forward.append((count - 1, 0))
        backward = [(target, source) for source, target in forward]
        low = lax.ppermute(
            lax.slice_in_dim(block, block.shape[dim] - width, None, axis=dim), axis, forward
        )
        high = lax.ppermute(lax.slice_in_dim(block, 0, width, axis=dim), axis, backward)
        block = jnp.concatenate([low, block, high], axis=dim)
    return block


def from_partner(block, axis, stride):
    count = lax.axis_size(axis)
    route = []
    for low in range(count):
        high = low | 1 << stride
        if high != low and high < count:
            route += [(low, high), (high, low)]
    return lax.ppermute(block, axis, route)


def passed_along(value, axis, steps):
    count = lax.axis_size(axis)
    pairs = [(source, (source + steps) % count) for source in range(count)]
    return lax.ppermute(value, axis, pairs)


def shifted(shard, axis, by):
    count = lax.axis_size(axis)
    pairs = [(i, i + by) for i in range(count) if 0 <= i + by < count]
    return lax.ppermute(shard, axis, pairs)


def window(array, shift_row, shift_col):
    inner_height = array.shape[-2] - 2
    inner_width = array.shape[-1] - 2
    return array[..., shift_row : shift_row + inner_height, shift_col : shift_col + inner_width]


def masked_laplacian(values, wet_mask):
    centre = window(values, 1, 1)
    running = jnp.zeros_like(centre)
    for shift_row, shift_col in ((0, 1), (2, 1), (1, 0), (1, 2)):
        running = running + window(wet_mask, shift_row, shift_col) * (
            window(values, shift_row, shift_col) - centre
        )
    return window(wet_mask, 1, 1) * running


def face_flux(speed_one, speed_two, tracer_one, tracer_two, wet_one, wet_two):
    return 0.5 * (speed_one + speed_two) * 0.5 * (tracer_one + tracer_two) * wet_one * wet_two


def baroclinic(padded):
    tracer = padded[0:2]
    wet_mask = padded[2]
    inner_tracer = tracer[..., 1:-1, 1:-1]
    inner_mask = wet_mask[..., 1:-1, 1:-1]
    east_speed = padded[3][..., 1:-1, 1:-1]
    north_speed = padded[4][..., 1:-1, 1:-1]
    lap_one = masked_laplacian(tracer, wet_mask)
    lap_two = masked_laplacian(lap_one, inner_mask)
    centre = window(inner_tracer, 1, 1)
    wet_centre = window(inner_mask, 1, 1)
    east_flux = face_flux(
        window(east_speed, 1, 1),
        window(east_speed, 1, 2),
        centre,
        window(inner_tracer, 1, 2),
        wet_centre,
        window(inner_mask, 1, 2),
    )
    west_flux = face_flux(
        window(east_speed, 1, 0),
        window(east_speed, 1, 1),
        window(inner_tracer, 1, 0),
        centre,
        window(inner_mask, 1, 0),
        wet_centre,
    )
    north_flux = face_flux(
        window(north_speed, 1, 1),
        window(north_speed, 2, 1),
        centre,
        window(inner_tracer, 2, 1),
        wet_centre,
        window(inner_mask, 2, 1),
    )
    south_flux = face_flux(
        window(north_speed, 0, 1),
        window(north_speed, 1, 1),
        window(inner_tracer, 0, 1),
        centre,
        window(inner_mask, 0, 1),
        wet_centre,
    )
    divergence = east_flux - west_flux + north_flux - south_flux
    return wet_centre * (centre - advection_rate * divergence - biharmonic_rate * lap_two)


def stencil_body(field, out_ref):
    height, width = field(2).shape
    row_count, col_count = out_ref.shape[2], out_ref.shape[3]

    def south(x):
        return pltpu.roll(x, 1, 0)

    def north(x):
        return pltpu.roll(x, height - 1, 0)

    def west(x):
        return pltpu.roll(x, 1, 1)

    def east(x):
        return pltpu.roll(x, width - 1, 1)

    shifts = (south, north, west, east)
    wet = field(2)
    wet_near = [shift(wet) for shift in shifts]

    def laplacian(values):
        running = None
        for shift, wet_n in zip(shifts, wet_near):
            term = wet_n * (shift(values) - values)
            running = term if running is None else running + term
        return wet * running

    east_speed = field(3)
    north_speed = field(4)
    east_mean = 0.5 * (east_speed + east(east_speed))
    north_mean = 0.5 * (north_speed + north(north_speed))
    for t in range(out_ref.shape[0]):
        tracer = field(t)
        lap_two = laplacian(laplacian(tracer))
        east_flux = east_mean * 0.5 * (tracer + east(tracer)) * wet * wet_near[3]
        north_flux = north_mean * 0.5 * (tracer + north(tracer)) * wet * wet_near[1]
        divergence = east_flux - west(east_flux) + north_flux - south(north_flux)
        result = wet * (tracer - advection_rate * divergence - biharmonic_rate * lap_two)
        out_ref[t, 0] = result[:row_count, :col_count]


def stencil_kernel(ext_ref, out_ref):
    stencil_body(lambda f: ext_ref[f, 0], out_ref)


def assembling_kernel(tracer_ref, wet_ref, east_ref, north_ref, cols_ref, rows_ref, out_ref, ext_ref):
    rows, cols = wet_ref.shape[1], wet_ref.shape[2]
    interiors = (
        tracer_ref[0, 0],
        tracer_ref[1, 0],
        wet_ref[0],
        east_ref[0].astype(jnp.float32),
        north_ref[0].astype(jnp.float32),
    )
    for f, interior in enumerate(interiors):
        ext_ref[f, 0:rows, 0:cols] = interior
        ext_ref[f, 0:rows, cols:] = cols_ref[f, 0]
        ext_ref[f, rows:, :] = rows_ref[f, 0]
    stencil_body(lambda f: ext_ref[f], out_ref)


def halo_pieces(tracers, wet_mask, east_velocity, north_velocity, fold_signs):
    rows, cols = wet_mask.shape[1], wet_mask.shape[2]
    width = -(-(cols + 4) // 128) * 128
    lead = wet_mask.shape[:1]
    lon_count = lax.axis_size("lon")
    lat_count = lax.axis_size("lat")

    def fields(index):
        return jnp.concatenate(
            [
                tracers[index],
                wet_mask[None][index],
                east_velocity[None][index].astype(jnp.float32),
                north_velocity[None][index].astype(jnp.float32),
            ],
            axis=0,
        )

    every = slice(None)
    east_halo = lax.ppermute(
        fields((every, every, every, slice(0, 2))),
        "lon",
        [(i, (i - 1) % lon_count) for i in range(lon_count)],
    )
    west_halo = lax.ppermute(
        fields((every, every, every, slice(cols - 2, cols))),
        "lon",
        [(i, (i + 1) % lon_count) for i in range(lon_count)],
    )
    halo_cols = jnp.concatenate(
        [east_halo, jnp.zeros((5,) + lead + (rows, width - cols - 4), jnp.float32), west_halo],
        axis=3,
    )

    def widened_rows(start):
        band = (every, every, slice(start, start + 2))
        return jnp.concatenate([fields(band), halo_cols[band]], axis=3)

    bottom = widened_rows(0)
    top = widened_rows(rows - 2)
    north_rows = lax.ppermute(bottom, "lat", [(j, j - 1) for j in range(1, lat_count)])
    south_rows = lax.ppermute(top, "lat", [(j, j + 1) for j in range(lat_count - 1)])
    mirrored = lax.ppermute(top, "lon", [(i, lon_count - 1 - i) for i in range(lon_count)])
    folded = jnp.roll(jnp.flip(mirrored, axis=(2, 3)), cols - width, axis=3) * fold_signs
    at_top = lax.axis_index("lat") == lat_count - 1
    north = jnp.where(at_top, folded, north_rows)
    halo_rows = jnp.concatenate(
        [north, jnp.zeros((5,) + lead + (4, width), jnp.float32), south_rows], axis=2
    )
    return halo_cols, halo_rows


def assembling_call(tracers, wet_mask, east_velocity, north_velocity, fold_signs):
    halo_cols, halo_rows = halo_pieces(tracers, wet_mask, east_velocity, north_velocity, fold_signs)
    tracer_count, level_count, rows, cols = tracers.shape
    width = cols + halo_cols.shape[3]
    height = rows + halo_rows.shape[2]
    level_block = pl.BlockSpec((1, rows, cols), lambda k: (k, 0, 0))
    return pl.pallas_call(
        assembling_kernel,
        grid=(level_count,),
        in_specs=[
            pl.BlockSpec((tracer_count, 1, rows, cols), lambda k: (0, k, 0, 0)),
            level_block,
            level_block,
            level_block,
            pl.BlockSpec((5, 1, rows, halo_cols.shape[3]), lambda k: (0, k, 0, 0)),
            pl.BlockSpec((5, 1, halo_rows.shape[2], width), lambda k: (0, k, 0, 0)),
        ],
        out_specs=pl.BlockSpec((tracer_count, 1, rows, cols), lambda k: (0, k, 0, 0)),
        out_shape=jax.ShapeDtypeStruct(tracers.shape, jnp.float32),
        scratch_shapes=[pltpu.VMEM((5, height, width), jnp.float32)],
    )(tracers, wet_mask, east_velocity, north_velocity, halo_cols, halo_rows)


def wrapped_layout(padded):
    rows = padded.shape[2] - 4
    cols = padded.shape[3] - 4
    height = -(-(rows + 4) // 8) * 8
    width = -(-(cols + 4) // 128) * 128
    lead = padded.shape[:2]
    by_rows = jnp.concatenate(
        [
            padded[:, :, 2 : rows + 4],
            jnp.zeros(lead + (height - rows - 4, padded.shape[3]), padded.dtype),
            padded[:, :, 0:2],
        ],
        axis=2,
    )
    return jnp.concatenate(
        [
            by_rows[..., 2 : cols + 4],
            jnp.zeros(lead + (height, width - cols - 4), padded.dtype),
            by_rows[..., 0:2],
        ],
        axis=3,
    )


def stencil_call(ext, rows, cols):
    tracer_count = 2
    level_count = ext.shape[1]
    height, width = ext.shape[2], ext.shape[3]
    return pl.pallas_call(
        stencil_kernel,
        grid=(level_count,),
        in_specs=[pl.BlockSpec((ext.shape[0], 1, height, width), lambda k: (0, k, 0, 0))],
        out_specs=pl.BlockSpec((tracer_count, 1, rows, cols), lambda k: (0, k, 0, 0)),
        out_shape=jax.ShapeDtypeStruct((tracer_count, level_count, rows, cols), jnp.float32),
    )(ext)


def mix_kernel(values_ref, wet_ref, diff_ref, forcing_ref, out_ref, source_ref, ratio_ref):
    level_count = wet_ref.shape[0]
    tracer_count = values_ref.shape[0]

    def coupling(k):
        return diff_ref[k].astype(jnp.float32) * wet_ref[k] * wet_ref[k - 1]

    below = coupling(1)
    upper = None
    reduced = [None] * tracer_count
    for k in range(level_count):
        above = below
        below = coupling(k + 1) if k + 1 < level_count else None
        if k == 0:
            diagonal = 1.0 + below
            divisor = diagonal
        elif below is None:
            diagonal = 1.0 + above
            divisor = diagonal + above * upper
        else:
            diagonal = 1.0 + above + below
            divisor = diagonal + above * upper
        if below is not None:
            upper = -below / divisor
            ratio_ref[k] = upper
        for t in range(tracer_count):
            if k == 0:
                source = values_ref[t, 0]
            else:
                source = values_ref[t, k] + above * reduced[t]
            reduced[t] = source / divisor
            out_ref[t, k] = reduced[t]
    result = reduced
    contrast = result[0] - result[1]
    for k in range(level_count - 2, -1, -1):
        ratio = ratio_ref[k]
        for t in range(tracer_count):
            result[t] = out_ref[t, k] - ratio * result[t]
            out_ref[t, k] = result[t]
        contrast = contrast + (result[0] - result[1])
    source_ref[...] = wet_ref[0] * (forcing_ref[...] + contrast / level_count)


def vertical_mix(values, wet_mask, diffusivity, forcing):
    tracer_count, level_count, row_count, col_count = values.shape
    rows = 16 if row_count % 16 == 0 else row_count
    return pl.pallas_call(
        mix_kernel,
        grid=(row_count // rows,),
        in_specs=[
            pl.BlockSpec((tracer_count, level_count, rows, col_count), lambda i: (0, 0, i, 0)),
            pl.BlockSpec((level_count, rows, col_count), lambda i: (0, i, 0)),
            pl.BlockSpec((level_count, rows, col_count), lambda i: (0, i, 0)),
            pl.BlockSpec((rows, col_count), lambda i: (i, 0)),
        ],
        out_specs=[
            pl.BlockSpec((tracer_count, level_count, rows, col_count), lambda i: (0, 0, i, 0)),
            pl.BlockSpec((rows, col_count), lambda i: (i, 0)),
        ],
        out_shape=[
            jax.ShapeDtypeStruct(values.shape, jnp.float32),
            jax.ShapeDtypeStruct((row_count, col_count), jnp.float32),
        ],
        scratch_shapes=[pltpu.VMEM((level_count - 1, rows, col_count), jnp.float32)],
    )(values, wet_mask, diffusivity, forcing)


def nine_point(padded, wet_surface, centre_weight):
    centre = window(padded, 1, 1)
    edges = (
        window(padded, 0, 1) + window(padded, 2, 1) + window(padded, 1, 0) + window(padded, 1, 2)
    )
    corners = (
        window(padded, 0, 0) + window(padded, 0, 2) + window(padded, 2, 0) + window(padded, 2, 2)
    )
    return wet_surface * (centre_weight * centre - edges - corner_weight * corners)


def wrapped_extend(stacked, fold_signs):
    rows, cols = stacked.shape[2], stacked.shape[3]
    height = -(-(rows + 4) // 8) * 8
    width = -(-(cols + 4) // 128) * 128
    lead = stacked.shape[:2]
    lon_count = lax.axis_size("lon")
    lat_count = lax.axis_size("lat")
    east_halo = lax.ppermute(
        stacked[..., :2], "lon", [(i, (i - 1) % lon_count) for i in range(lon_count)]
    )
    west_halo = lax.ppermute(
        stacked[..., cols - 2 :], "lon", [(i, (i + 1) % lon_count) for i in range(lon_count)]
    )
    widened = jnp.concatenate(
        [stacked, east_halo, jnp.zeros(lead + (rows, width - cols - 4), stacked.dtype), west_halo],
        axis=3,
    )
    north_rows = lax.ppermute(widened[:, :, :2], "lat", [(j, j - 1) for j in range(1, lat_count)])
    south_rows = lax.ppermute(
        widened[:, :, rows - 2 :], "lat", [(j, j + 1) for j in range(lat_count - 1)]
    )
    mirrored = lax.ppermute(
        widened[:, :, rows - 2 :], "lon", [(i, lon_count - 1 - i) for i in range(lon_count)]
    )
    folded = jnp.roll(jnp.flip(mirrored, axis=(2, 3)), cols - width, axis=3) * fold_signs
    at_top = lax.axis_index("lat") == lat_count - 1
    north = jnp.where(at_top, folded, north_rows)
    return jnp.concatenate(
        [widened, north, jnp.zeros(lead + (height - rows - 4, width), stacked.dtype), south_rows],
        axis=2,
    )


def clinic_extend(stacked, fold_signs):
    row_count = stacked.shape[2]
    widened = extended_2(stacked, (("lon", 3),), 2, True)
    extended = extended_2(widened, (("lat", 2),), 2, False)
    top_rows = widened[:, :, row_count - 2 :, :]
    for bit in range(lax.axis_size("lon").bit_length() - 1):
        top_rows = from_partner(top_rows, "lon", bit)
    northern = jnp.flip(top_rows, axis=(2, 3)) * fold_signs
    at_top = lax.axis_index("lat") == lax.axis_size("lat") - 1
    ghost_rows = jnp.where(at_top, northern, extended[:, :, row_count + 2 :, :])
    return jnp.concatenate([extended[:, :, : row_count + 2, :], ghost_rows], axis=2)


def strip_pad(surface_field):
    lon_index = lax.axis_index("lon")
    lon_count = lax.axis_size("lon")
    first_row = surface_field[0:1, :]
    last_row = surface_field[-1:, :]
    following = passed_along(first_row, "lon", -1)
    following_far = shifted(following, "lat", -1)
    preceding = passed_along(last_row, "lon", 1)
    preceding_far = shifted(preceding, "lat", 1)
    above_row = jnp.where(lon_index == lon_count - 1, following_far, following)
    below_row = jnp.where(lon_index == 0, preceding_far, preceding)
    top_strip = jnp.logical_and(
        lon_index == lon_count - 1, lax.axis_index("lat") == lax.axis_size("lat") - 1
    )
    above_row = jnp.where(top_strip, jnp.flip(last_row, axis=1), above_row)
    extended = jnp.concatenate([below_row, surface_field, above_row], axis=0)
    return jnp.concatenate([extended[:, -1:], extended, extended[:, :1]], axis=1)


def strip_pad_joined(surface_field):
    lon_count = lax.axis_size("lon")
    lat_count = lax.axis_size("lat")
    strip_count = lon_count * lat_count
    axes = ("lon", "lat")

    def device(strip):
        return (strip % lon_count) * lat_count + strip // lon_count

    first_row = surface_field[0:1, :]
    last_row = surface_field[-1:, :]
    above_row = lax.ppermute(
        first_row, axes, [(device(s + 1), device(s)) for s in range(strip_count - 1)]
    )
    below_row = lax.ppermute(
        last_row, axes, [(device(s - 1), device(s)) for s in range(1, strip_count)]
    )
    top_strip = jnp.logical_and(
        lax.axis_index("lon") == lon_count - 1, lax.axis_index("lat") == lat_count - 1
    )
    above_row = jnp.where(top_strip, jnp.flip(last_row, axis=1), above_row)
    extended = jnp.concatenate([below_row, surface_field, above_row], axis=0)
    return jnp.concatenate([extended[:, -1:], extended, extended[:, :1]], axis=1)


def butterfly_sum(value):
    for axis in ("lon", "lat"):
        count = lax.axis_size(axis)
        bit = 1
        while bit < count:
            value = value + lax.ppermute(value, axis, [(i, i ^ bit) for i in range(count)])
            bit <<= 1
    return value


def neighbour_rows(values):
    lon_count = lax.axis_size("lon")
    lat_count = lax.axis_size("lat")
    strip_count = lon_count * lat_count
    axes = ("lon", "lat")

    def device(strip):
        return (strip % lon_count) * lat_count + strip // lon_count

    above = lax.ppermute(
        values[:, 0:1, :], axes, [(device(s + 1), device(s)) for s in range(strip_count - 1)]
    )
    below = lax.ppermute(
        values[:, -1:, :], axes, [(device(s - 1), device(s)) for s in range(1, strip_count)]
    )
    return above, below


def strip_assemble(surface_field, above_row, below_row):
    top_strip = jnp.logical_and(
        lax.axis_index("lon") == lax.axis_size("lon") - 1,
        lax.axis_index("lat") == lax.axis_size("lat") - 1,
    )
    above_row = jnp.where(top_strip, jnp.flip(surface_field[-1:, :], axis=1), above_row)
    extended = jnp.concatenate([below_row, surface_field, above_row], axis=0)
    return jnp.concatenate([extended[:, -1:], extended, extended[:, :1]], axis=1)


def solve(surface_source, wet_surface, centre_weight):

    def precondition(residual, wet, weight):
        return wet * residual / weight

    def apply_operator(field, above, below):
        return nine_point(strip_assemble(field, above, below), wet_surface, centre_weight)

    rim_above, rim_below = neighbour_rows(jnp.stack([wet_surface, centre_weight, surface_source]))
    solution = jnp.zeros_like(surface_source)
    residual = surface_source
    resid_rims = [rim_above[2], rim_below[2]]
    weight_rims = [
        (rim[0], jnp.where(rim[1] == 0.0, 1.0, rim[1])) for rim in (rim_above, rim_below)
    ]
    precond = precondition(residual, wet_surface, centre_weight)
    direction = precond
    operator_image = apply_operator(
        direction,
        *[precondition(r, w, c) for r, (w, c) in zip(resid_rims, weight_rims)],
    )
    image_above, image_below = neighbour_rows(operator_image[None])
    image_rims = [image_above[0], image_below[0]]
    totals = butterfly_sum(
        jnp.stack([jnp.sum(residual * precond), jnp.sum(direction * operator_image)])
    )
    resid_dot, curvature = totals[0], totals[1]
    for iteration in range(ITERS):
        step_size = resid_dot / curvature
        solution = solution + step_size * direction
        if iteration + 1 < ITERS:
            residual = residual - step_size * operator_image
            resid_rims = [r - step_size * a for r, a in zip(resid_rims, image_rims)]
            precond = precondition(residual, wet_surface, centre_weight)
            precond_image = apply_operator(
                precond,
                *[precondition(r, w, c) for r, (w, c) in zip(resid_rims, weight_rims)],
            )
            if iteration + 2 < ITERS:
                fresh_above, fresh_below = neighbour_rows(precond_image[None])
                fresh_rims = [fresh_above[0], fresh_below[0]]
            totals = butterfly_sum(
                jnp.stack(
                    [
                        jnp.sum(residual * precond),
                        jnp.sum(precond * precond_image),
                        jnp.sum(precond * operator_image),
                    ]
                )
            )
            dot_next = totals[0]
            ratio = dot_next / resid_dot
            direction = precond + ratio * direction
            curvature = totals[1] + 2.0 * ratio * totals[2] + ratio * ratio * curvature
            operator_image = precond_image + ratio * operator_image
            if iteration + 2 < ITERS:
                image_rims = [f + ratio * a for f, a in zip(fresh_rims, image_rims)]
            resid_dot = dot_next
    return solution


def shards(
    tracers,
    east_velocity,
    north_velocity,
    vertical_diffusivity,
    depth_levels,
    ocean_blocks,
    forcing,
    surface_coupling,
):
    level_count = tracers.shape[1]
    row_count = tracers.shape[2]
    col_count = tracers.shape[3]
    ocean_cells = jnp.repeat(
        jnp.repeat(ocean_blocks, row_count // ocean_blocks.shape[0], axis=0),
        col_count // ocean_blocks.shape[1],
        axis=1,
    ).astype(jnp.float32)
    level_index = lax.broadcasted_iota(jnp.int32, (level_count, row_count, col_count), 0)
    wet_mask = jnp.where(
        level_index < depth_levels[None], ocean_cells[None], jnp.zeros_like(ocean_cells)[None]
    )
    relaid = lax.all_to_all(
        jnp.stack([wet_mask[0], 6.0 + surface_coupling]),
        "lon",
        split_axis=1,
        concat_axis=2,
        tiled=True,
    )
    fold_signs = jnp.array([1.0, 1.0, 1.0, -1.0, -1.0], jnp.float32).reshape(5, 1, 1, 1)
    provisional = assembling_call(tracers, wet_mask, east_velocity, north_velocity, fold_signs)
    new_tracers, surface_source = vertical_mix(
        provisional, wet_mask, vertical_diffusivity, forcing
    )
    wet_surface = wet_mask[0]
    centre_weight = 6.0 + surface_coupling
    strip_source = lax.all_to_all(surface_source, "lon", split_axis=0, concat_axis=1, tiled=True)
    strip_solution = solve(strip_source, relaid[0], relaid[1])
    solution = lax.all_to_all(strip_solution, "lon", split_axis=1, concat_axis=0, tiled=True)
    return (new_tracers, solution)


def solution(mesh):
    placed = (
        P(None, None, "lat", "lon"),
        P(None, "lat", "lon"),
        P(None, "lat", "lon"),
        P(None, "lat", "lon"),
        P("lat", "lon"),
        P("lat", "lon"),
        P("lat", "lon"),
        P("lat", "lon"),
    )
    return jax.shard_map(
        shards,
        mesh=mesh,
        in_specs=placed,
        out_specs=(P(None, None, "lat", "lon"), P("lat", "lon")),
        check_vma=False,
    )
```

```python
import jax
import jax.numpy as jnp
from jax import lax
from jax.sharding import PartitionSpec as P
from jax.experimental import pallas as pl
from jax.experimental.pallas import tpu as pltpu

ITERS = 3


advection_rate = 0.25
biharmonic_rate = 0.01
corner_weight = 0.5


def extended_2(block, sides, width, periodic):
    for axis, dim in sides:
        count = lax.axis_size(axis)
        forward = [(i, i + 1) for i in range(count - 1)]
        if periodic:
            forward.append((count - 1, 0))
        backward = [(target, source) for source, target in forward]
        low = lax.ppermute(
            lax.slice_in_dim(block, block.shape[dim] - width, None, axis=dim), axis, forward
        )
        high = lax.ppermute(lax.slice_in_dim(block, 0, width, axis=dim), axis, backward)
        block = jnp.concatenate([low, block, high], axis=dim)
    return block


def from_partner(block, axis, stride):
    count = lax.axis_size(axis)
    route = []
    for low in range(count):
        high = low | 1 << stride
        if high != low and high < count:
            route += [(low, high), (high, low)]
    return lax.ppermute(block, axis, route)


def passed_along(value, axis, steps):
    count = lax.axis_size(axis)
    pairs = [(source, (source + steps) % count) for source in range(count)]
    return lax.ppermute(value, axis, pairs)


def shifted(shard, axis, by):
    count = lax.axis_size(axis)
    pairs = [(i, i + by) for i in range(count) if 0 <= i + by < count]
    return lax.ppermute(shard, axis, pairs)


def window(array, shift_row, shift_col):
    inner_height = array.shape[-2] - 2
    inner_width = array.shape[-1] - 2
    return array[..., shift_row : shift_row + inner_height, shift_col : shift_col + inner_width]


def masked_laplacian(values, wet_mask):
    centre = window(values, 1, 1)
    running = jnp.zeros_like(centre)
    for shift_row, shift_col in ((0, 1), (2, 1), (1, 0), (1, 2)):
        running = running + window(wet_mask, shift_row, shift_col) * (
            window(values, shift_row, shift_col) - centre
        )
    return window(wet_mask, 1, 1) * running


def face_flux(speed_one, speed_two, tracer_one, tracer_two, wet_one, wet_two):
    return 0.5 * (speed_one + speed_two) * 0.5 * (tracer_one + tracer_two) * wet_one * wet_two


def baroclinic(padded):
    tracer = padded[0:2]
    wet_mask = padded[2]
    inner_tracer = tracer[..., 1:-1, 1:-1]
    inner_mask = wet_mask[..., 1:-1, 1:-1]
    east_speed = padded[3][..., 1:-1, 1:-1]
    north_speed = padded[4][..., 1:-1, 1:-1]
    lap_one = masked_laplacian(tracer, wet_mask)
    lap_two = masked_laplacian(lap_one, inner_mask)
    centre = window(inner_tracer, 1, 1)
    wet_centre = window(inner_mask, 1, 1)
    east_flux = face_flux(
        window(east_speed, 1, 1),
        window(east_speed, 1, 2),
        centre,
        window(inner_tracer, 1, 2),
        wet_centre,
        window(inner_mask, 1, 2),
    )
    west_flux = face_flux(
        window(east_speed, 1, 0),
        window(east_speed, 1, 1),
        window(inner_tracer, 1, 0),
        centre,
        window(inner_mask, 1, 0),
        wet_centre,
    )
    north_flux = face_flux(
        window(north_speed, 1, 1),
        window(north_speed, 2, 1),
        centre,
        window(inner_tracer, 2, 1),
        wet_centre,
        window(inner_mask, 2, 1),
    )
    south_flux = face_flux(
        window(north_speed, 0, 1),
        window(north_speed, 1, 1),
        window(inner_tracer, 0, 1),
        centre,
        window(inner_mask, 0, 1),
        wet_centre,
    )
    divergence = east_flux - west_flux + north_flux - south_flux
    return wet_centre * (centre - advection_rate * divergence - biharmonic_rate * lap_two)


def stencil_body(field, out_ref):
    height, width = field(2).shape
    row_count, col_count = out_ref.shape[2], out_ref.shape[3]

    def south(x):
        return pltpu.roll(x, 1, 0)

    def north(x):
        return pltpu.roll(x, height - 1, 0)

    def west(x):
        return pltpu.roll(x, 1, 1)

    def east(x):
        return pltpu.roll(x, width - 1, 1)

    shifts = (south, north, west, east)
    wet = field(2)
    wet_near = [shift(wet) for shift in shifts]

    def laplacian(values):
        running = None
        for shift, wet_n in zip(shifts, wet_near):
            term = wet_n * (shift(values) - values)
            running = term if running is None else running + term
        return wet * running

    east_speed = field(3)
    north_speed = field(4)
    east_mean = 0.5 * (east_speed + east(east_speed))
    north_mean = 0.5 * (north_speed + north(north_speed))
    for t in range(out_ref.shape[0]):
        tracer = field(t)
        lap_two = laplacian(laplacian(tracer))
        east_flux = east_mean * 0.5 * (tracer + east(tracer)) * wet * wet_near[3]
        north_flux = north_mean * 0.5 * (tracer + north(tracer)) * wet * wet_near[1]
        divergence = east_flux - west(east_flux) + north_flux - south(north_flux)
        result = wet * (tracer - advection_rate * divergence - biharmonic_rate * lap_two)
        out_ref[t, 0] = result[:row_count, :col_count]


def stencil_kernel(ext_ref, out_ref):
    stencil_body(lambda f: ext_ref[f, 0], out_ref)


def assembling_kernel(tracer_ref, wet_ref, east_ref, north_ref, cols_ref, rows_ref, out_ref, ext_ref):
    rows, cols = wet_ref.shape[1], wet_ref.shape[2]
    interiors = (
        tracer_ref[0, 0],
        tracer_ref[1, 0],
        wet_ref[0],
        east_ref[0].astype(jnp.float32),
        north_ref[0].astype(jnp.float32),
    )
    for f, interior in enumerate(interiors):
        ext_ref[f, 0:rows, 0:cols] = interior
        ext_ref[f, 0:rows, cols:] = cols_ref[f, 0]
        ext_ref[f, rows:, :] = rows_ref[f, 0]
    stencil_body(lambda f: ext_ref[f], out_ref)


def halo_pieces(tracers, wet_mask, east_velocity, north_velocity, fold_signs):
    rows, cols = wet_mask.shape[1], wet_mask.shape[2]
    width = -(-(cols + 4) // 128) * 128
    lead = wet_mask.shape[:1]
    lon_count = lax.axis_size("lon")
    lat_count = lax.axis_size("lat")

    def fields(index):
        return jnp.concatenate(
            [
                tracers[index],
                wet_mask[None][index],
                east_velocity[None][index].astype(jnp.float32),
                north_velocity[None][index].astype(jnp.float32),
            ],
            axis=0,
        )

    every = slice(None)
    east_halo = lax.ppermute(
        fields((every, every, every, slice(0, 2))),
        "lon",
        [(i, (i - 1) % lon_count) for i in range(lon_count)],
    )
    west_halo = lax.ppermute(
        fields((every, every, every, slice(cols - 2, cols))),
        "lon",
        [(i, (i + 1) % lon_count) for i in range(lon_count)],
    )
    halo_cols = jnp.concatenate(
        [east_halo, jnp.zeros((5,) + lead + (rows, width - cols - 4), jnp.float32), west_halo],
        axis=3,
    )

    def widened_rows(start):
        band = (every, every, slice(start, start + 2))
        return jnp.concatenate([fields(band), halo_cols[band]], axis=3)

    bottom = widened_rows(0)
    top = widened_rows(rows - 2)
    north_rows = lax.ppermute(bottom, "lat", [(j, j - 1) for j in range(1, lat_count)])
    south_rows = lax.ppermute(top, "lat", [(j, j + 1) for j in range(lat_count - 1)])
    mirrored = lax.ppermute(top, "lon", [(i, lon_count - 1 - i) for i in range(lon_count)])
    folded = jnp.roll(jnp.flip(mirrored, axis=(2, 3)), cols - width, axis=3) * fold_signs
    at_top = lax.axis_index("lat") == lat_count - 1
    north = jnp.where(at_top, folded, north_rows)
    halo_rows = jnp.concatenate(
        [north, jnp.zeros((5,) + lead + (4, width), jnp.float32), south_rows], axis=2
    )
    return halo_cols, halo_rows


def assembling_call(tracers, wet_mask, east_velocity, north_velocity, fold_signs):
    halo_cols, halo_rows = halo_pieces(tracers, wet_mask, east_velocity, north_velocity, fold_signs)
    tracer_count, level_count, rows, cols = tracers.shape
    width = cols + halo_cols.shape[3]
    height = rows + halo_rows.shape[2]
    level_block = pl.BlockSpec((1, rows, cols), lambda k: (k, 0, 0))
    return pl.pallas_call(
        assembling_kernel,
        grid=(level_count,),
        in_specs=[
            pl.BlockSpec((tracer_count, 1, rows, cols), lambda k: (0, k, 0, 0)),
            level_block,
            level_block,
            level_block,
            pl.BlockSpec((5, 1, rows, halo_cols.shape[3]), lambda k: (0, k, 0, 0)),
            pl.BlockSpec((5, 1, halo_rows.shape[2], width), lambda k: (0, k, 0, 0)),
        ],
        out_specs=pl.BlockSpec((tracer_count, 1, rows, cols), lambda k: (0, k, 0, 0)),
        out_shape=jax.ShapeDtypeStruct(tracers.shape, jnp.float32),
        scratch_shapes=[pltpu.VMEM((5, height, width), jnp.float32)],
    )(tracers, wet_mask, east_velocity, north_velocity, halo_cols, halo_rows)


def wrapped_layout(padded):
    rows = padded.shape[2] - 4
    cols = padded.shape[3] - 4
    height = -(-(rows + 4) // 8) * 8
    width = -(-(cols + 4) // 128) * 128
    lead = padded.shape[:2]
    by_rows = jnp.concatenate(
        [
            padded[:, :, 2 : rows + 4],
            jnp.zeros(lead + (height - rows - 4, padded.shape[3]), padded.dtype),
            padded[:, :, 0:2],
        ],
        axis=2,
    )
    return jnp.concatenate(
        [
            by_rows[..., 2 : cols + 4],
            jnp.zeros(lead + (height, width - cols - 4), padded.dtype),
            by_rows[..., 0:2],
        ],
        axis=3,
    )


def stencil_call(ext, rows, cols):
    tracer_count = 2
    level_count = ext.shape[1]
    height, width = ext.shape[2], ext.shape[3]
    return pl.pallas_call(
        stencil_kernel,
        grid=(level_count,),
        in_specs=[pl.BlockSpec((ext.shape[0], 1, height, width), lambda k: (0, k, 0, 0))],
        out_specs=pl.BlockSpec((tracer_count, 1, rows, cols), lambda k: (0, k, 0, 0)),
        out_shape=jax.ShapeDtypeStruct((tracer_count, level_count, rows, cols), jnp.float32),
    )(ext)


def mix_kernel(values_ref, wet_ref, diff_ref, forcing_ref, out_ref, source_ref, ratio_ref):
    level_count = wet_ref.shape[0]
    tracer_count = values_ref.shape[0]

    def coupling(k):
        return diff_ref[k].astype(jnp.float32) * wet_ref[k] * wet_ref[k - 1]

    below = coupling(1)
    upper = None
    reduced = [None] * tracer_count
    for k in range(level_count):
        above = below
        below = coupling(k + 1) if k + 1 < level_count else None
        if k == 0:
            diagonal = 1.0 + below
            divisor = diagonal
        elif below is None:
            diagonal = 1.0 + above
            divisor = diagonal + above * upper
        else:
            diagonal = 1.0 + above + below
            divisor = diagonal + above * upper
        if below is not None:
            upper = -below / divisor
            ratio_ref[k] = upper
        for t in range(tracer_count):
            if k == 0:
                source = values_ref[t, 0]
            else:
                source = values_ref[t, k] + above * reduced[t]
            reduced[t] = source / divisor
            out_ref[t, k] = reduced[t]
    result = reduced
    contrast = result[0] - result[1]
    for k in range(level_count - 2, -1, -1):
        ratio = ratio_ref[k]
        for t in range(tracer_count):
            result[t] = out_ref[t, k] - ratio * result[t]
            out_ref[t, k] = result[t]
        contrast = contrast + (result[0] - result[1])
    source_ref[...] = wet_ref[0] * (forcing_ref[...] + contrast / level_count)


def vertical_mix(values, wet_mask, diffusivity, forcing):
    tracer_count, level_count, row_count, col_count = values.shape
    rows = 16 if row_count % 16 == 0 else row_count
    return pl.pallas_call(
        mix_kernel,
        grid=(row_count // rows,),
        in_specs=[
            pl.BlockSpec((tracer_count, level_count, rows, col_count), lambda i: (0, 0, i, 0)),
            pl.BlockSpec((level_count, rows, col_count), lambda i: (0, i, 0)),
            pl.BlockSpec((level_count, rows, col_count), lambda i: (0, i, 0)),
            pl.BlockSpec((rows, col_count), lambda i: (i, 0)),
        ],
        out_specs=[
            pl.BlockSpec((tracer_count, level_count, rows, col_count), lambda i: (0, 0, i, 0)),
            pl.BlockSpec((rows, col_count), lambda i: (i, 0)),
        ],
        out_shape=[
            jax.ShapeDtypeStruct(values.shape, jnp.float32),
            jax.ShapeDtypeStruct((row_count, col_count), jnp.float32),
        ],
        scratch_shapes=[pltpu.VMEM((level_count - 1, rows, col_count), jnp.float32)],
    )(values, wet_mask, diffusivity, forcing)


def nine_point(padded, wet_surface, centre_weight):
    centre = window(padded, 1, 1)
    edges = (
        window(padded, 0, 1) + window(padded, 2, 1) + window(padded, 1, 0) + window(padded, 1, 2)
    )
    corners = (
        window(padded, 0, 0) + window(padded, 0, 2) + window(padded, 2, 0) + window(padded, 2, 2)
    )
    return wet_surface * (centre_weight * centre - edges - corner_weight * corners)


def wrapped_extend(stacked, fold_signs):
    rows, cols = stacked.shape[2], stacked.shape[3]
    height = -(-(rows + 4) // 8) * 8
    width = -(-(cols + 4) // 128) * 128
    lead = stacked.shape[:2]
    lon_count = lax.axis_size("lon")
    lat_count = lax.axis_size("lat")
    east_halo = lax.ppermute(
        stacked[..., :2], "lon", [(i, (i - 1) % lon_count) for i in range(lon_count)]
    )
    west_halo = lax.ppermute(
        stacked[..., cols - 2 :], "lon", [(i, (i + 1) % lon_count) for i in range(lon_count)]
    )
    widened = jnp.concatenate(
        [stacked, east_halo, jnp.zeros(lead + (rows, width - cols - 4), stacked.dtype), west_halo],
        axis=3,
    )
    north_rows = lax.ppermute(widened[:, :, :2], "lat", [(j, j - 1) for j in range(1, lat_count)])
    south_rows = lax.ppermute(
        widened[:, :, rows - 2 :], "lat", [(j, j + 1) for j in range(lat_count - 1)]
    )
    mirrored = lax.ppermute(
        widened[:, :, rows - 2 :], "lon", [(i, lon_count - 1 - i) for i in range(lon_count)]
    )
    folded = jnp.roll(jnp.flip(mirrored, axis=(2, 3)), cols - width, axis=3) * fold_signs
    at_top = lax.axis_index("lat") == lat_count - 1
    north = jnp.where(at_top, folded, north_rows)
    return jnp.concatenate(
        [widened, north, jnp.zeros(lead + (height - rows - 4, width), stacked.dtype), south_rows],
        axis=2,
    )


def clinic_extend(stacked, fold_signs):
    row_count = stacked.shape[2]
    widened = extended_2(stacked, (("lon", 3),), 2, True)
    extended = extended_2(widened, (("lat", 2),), 2, False)
    top_rows = widened[:, :, row_count - 2 :, :]
    for bit in range(lax.axis_size("lon").bit_length() - 1):
        top_rows = from_partner(top_rows, "lon", bit)
    northern = jnp.flip(top_rows, axis=(2, 3)) * fold_signs
    at_top = lax.axis_index("lat") == lax.axis_size("lat") - 1
    ghost_rows = jnp.where(at_top, northern, extended[:, :, row_count + 2 :, :])
    return jnp.concatenate([extended[:, :, : row_count + 2, :], ghost_rows], axis=2)


def strip_pad(surface_field):
    lon_index = lax.axis_index("lon")
    lon_count = lax.axis_size("lon")
    first_row = surface_field[0:1, :]
    last_row = surface_field[-1:, :]
    following = passed_along(first_row, "lon", -1)
    following_far = shifted(following, "lat", -1)
    preceding = passed_along(last_row, "lon", 1)
    preceding_far = shifted(preceding, "lat", 1)
    above_row = jnp.where(lon_index == lon_count - 1, following_far, following)
    below_row = jnp.where(lon_index == 0, preceding_far, preceding)
    top_strip = jnp.logical_and(
        lon_index == lon_count - 1, lax.axis_index("lat") == lax.axis_size("lat") - 1
    )
    above_row = jnp.where(top_strip, jnp.flip(last_row, axis=1), above_row)
    extended = jnp.concatenate([below_row, surface_field, above_row], axis=0)
    return jnp.concatenate([extended[:, -1:], extended, extended[:, :1]], axis=1)


def strip_pad_joined(surface_field):
    lon_count = lax.axis_size("lon")
    lat_count = lax.axis_size("lat")
    strip_count = lon_count * lat_count
    axes = ("lon", "lat")

    def device(strip):
        return (strip % lon_count) * lat_count + strip // lon_count

    first_row = surface_field[0:1, :]
    last_row = surface_field[-1:, :]
    above_row = lax.ppermute(
        first_row, axes, [(device(s + 1), device(s)) for s in range(strip_count - 1)]
    )
    below_row = lax.ppermute(
        last_row, axes, [(device(s - 1), device(s)) for s in range(1, strip_count)]
    )
    top_strip = jnp.logical_and(
        lax.axis_index("lon") == lon_count - 1, lax.axis_index("lat") == lat_count - 1
    )
    above_row = jnp.where(top_strip, jnp.flip(last_row, axis=1), above_row)
    extended = jnp.concatenate([below_row, surface_field, above_row], axis=0)
    return jnp.concatenate([extended[:, -1:], extended, extended[:, :1]], axis=1)


def butterfly_sum(value):
    for axis in ("lon", "lat"):
        count = lax.axis_size(axis)
        bit = 1
        while bit < count:
            value = value + lax.ppermute(value, axis, [(i, i ^ bit) for i in range(count)])
            bit <<= 1
    return value


def neighbour_rows(values):
    lon_count = lax.axis_size("lon")
    lat_count = lax.axis_size("lat")
    strip_count = lon_count * lat_count
    axes = ("lon", "lat")

    def device(strip):
        return (strip % lon_count) * lat_count + strip // lon_count

    above = lax.ppermute(
        values[:, 0:1, :], axes, [(device(s + 1), device(s)) for s in range(strip_count - 1)]
    )
    below = lax.ppermute(
        values[:, -1:, :], axes, [(device(s - 1), device(s)) for s in range(1, strip_count)]
    )
    return above, below


def last_flipped(surface_field):
    return jnp.flip(surface_field[-1:, :], axis=1)


def strip_assemble(surface_field, above_row, below_row, folded_row):
    top_strip = jnp.logical_and(
        lax.axis_index("lon") == lax.axis_size("lon") - 1,
        lax.axis_index("lat") == lax.axis_size("lat") - 1,
    )
    above_row = jnp.where(top_strip, folded_row, above_row)
    extended = jnp.concatenate([below_row, surface_field, above_row], axis=0)
    return jnp.concatenate([extended[:, -1:], extended, extended[:, :1]], axis=1)


def solve(surface_source, wet_surface, centre_weight):

    def precondition(residual, wet, weight):
        return wet * residual / weight

    def apply_operator(field, above, below, folded):
        return nine_point(strip_assemble(field, above, below, folded), wet_surface, centre_weight)

    fold_wet = last_flipped(wet_surface)
    fold_weight = last_flipped(centre_weight)
    fold_resid = last_flipped(surface_source)

    rim_above, rim_below = neighbour_rows(jnp.stack([wet_surface, centre_weight, surface_source]))
    solution = jnp.zeros_like(surface_source)
    residual = surface_source
    resid_rims = [rim_above[2], rim_below[2]]
    weight_rims = [
        (rim[0], jnp.where(rim[1] == 0.0, 1.0, rim[1])) for rim in (rim_above, rim_below)
    ]
    precond = precondition(residual, wet_surface, centre_weight)
    direction = precond
    operator_image = apply_operator(
        direction,
        *[precondition(r, w, c) for r, (w, c) in zip(resid_rims, weight_rims)],
        precondition(fold_resid, fold_wet, fold_weight),
    )
    fold_image = last_flipped(operator_image)
    image_above, image_below = neighbour_rows(operator_image[None])
    image_rims = [image_above[0], image_below[0]]
    totals = butterfly_sum(
        jnp.stack([jnp.sum(residual * precond), jnp.sum(direction * operator_image)])
    )
    resid_dot, curvature = totals[0], totals[1]
    for iteration in range(ITERS):
        step_size = resid_dot / curvature
        solution = solution + step_size * direction
        if iteration + 1 < ITERS:
            residual = residual - step_size * operator_image
            resid_rims = [r - step_size * a for r, a in zip(resid_rims, image_rims)]
            fold_resid = fold_resid - step_size * fold_image
            precond = precondition(residual, wet_surface, centre_weight)
            precond_image = apply_operator(
                precond,
                *[precondition(r, w, c) for r, (w, c) in zip(resid_rims, weight_rims)],
                precondition(fold_resid, fold_wet, fold_weight),
            )
            if iteration + 2 < ITERS:
                fresh_above, fresh_below = neighbour_rows(precond_image[None])
                fresh_rims = [fresh_above[0], fresh_below[0]]
                fresh_fold = last_flipped(precond_image)
            totals = butterfly_sum(
                jnp.stack(
                    [
                        jnp.sum(residual * precond),
                        jnp.sum(precond * precond_image),
                        jnp.sum(precond * operator_image),
                    ]
                )
            )
            dot_next = totals[0]
            ratio = dot_next / resid_dot
            direction = precond + ratio * direction
            curvature = totals[1] + 2.0 * ratio * totals[2] + ratio * ratio * curvature
            operator_image = precond_image + ratio * operator_image
            if iteration + 2 < ITERS:
                image_rims = [f + ratio * a for f, a in zip(fresh_rims, image_rims)]
                fold_image = fresh_fold + ratio * fold_image
            resid_dot = dot_next
    return solution


def shards(
    tracers,
    east_velocity,
    north_velocity,
    vertical_diffusivity,
    depth_levels,
    ocean_blocks,
    forcing,
    surface_coupling,
):
    level_count = tracers.shape[1]
    row_count = tracers.shape[2]
    col_count = tracers.shape[3]
    ocean_cells = jnp.repeat(
        jnp.repeat(ocean_blocks, row_count // ocean_blocks.shape[0], axis=0),
        col_count // ocean_blocks.shape[1],
        axis=1,
    ).astype(jnp.float32)
    level_index = lax.broadcasted_iota(jnp.int32, (level_count, row_count, col_count), 0)
    wet_mask = jnp.where(
        level_index < depth_levels[None], ocean_cells[None], jnp.zeros_like(ocean_cells)[None]
    )
    relaid = lax.all_to_all(
        jnp.stack([wet_mask[0], 6.0 + surface_coupling]),
        "lon",
        split_axis=1,
        concat_axis=2,
        tiled=True,
    )
    fold_signs = jnp.array([1.0, 1.0, 1.0, -1.0, -1.0], jnp.float32).reshape(5, 1, 1, 1)
    provisional = assembling_call(tracers, wet_mask, east_velocity, north_velocity, fold_signs)
    new_tracers, surface_source = vertical_mix(
        provisional, wet_mask, vertical_diffusivity, forcing
    )
    wet_surface = wet_mask[0]
    centre_weight = 6.0 + surface_coupling
    strip_source = lax.all_to_all(surface_source, "lon", split_axis=0, concat_axis=1, tiled=True)
    strip_solution = solve(strip_source, relaid[0], relaid[1])
    solution = lax.all_to_all(strip_solution, "lon", split_axis=1, concat_axis=0, tiled=True)
    return (new_tracers, solution)


def solution(mesh):
    placed = (
        P(None, None, "lat", "lon"),
        P(None, "lat", "lon"),
        P(None, "lat", "lon"),
        P(None, "lat", "lon"),
        P("lat", "lon"),
        P("lat", "lon"),
        P("lat", "lon"),
        P("lat", "lon"),
    )
    return jax.shard_map(
        shards,
        mesh=mesh,
        in_specs=placed,
        out_specs=(P(None, None, "lat", "lon"), P("lat", "lon")),
        check_vma=False,
    )
```

```python
import jax
import jax.numpy as jnp
from jax import lax
from jax.sharding import PartitionSpec as P
from jax.experimental import pallas as pl
from jax.experimental.pallas import tpu as pltpu

ITERS = 3


advection_rate = 0.25
biharmonic_rate = 0.01
corner_weight = 0.5


def extended_2(block, sides, width, periodic):
    for axis, dim in sides:
        count = lax.axis_size(axis)
        forward = [(i, i + 1) for i in range(count - 1)]
        if periodic:
            forward.append((count - 1, 0))
        backward = [(target, source) for source, target in forward]
        low = lax.ppermute(
            lax.slice_in_dim(block, block.shape[dim] - width, None, axis=dim), axis, forward
        )
        high = lax.ppermute(lax.slice_in_dim(block, 0, width, axis=dim), axis, backward)
        block = jnp.concatenate([low, block, high], axis=dim)
    return block


def from_partner(block, axis, stride):
    count = lax.axis_size(axis)
    route = []
    for low in range(count):
        high = low | 1 << stride
        if high != low and high < count:
            route += [(low, high), (high, low)]
    return lax.ppermute(block, axis, route)


def passed_along(value, axis, steps):
    count = lax.axis_size(axis)
    pairs = [(source, (source + steps) % count) for source in range(count)]
    return lax.ppermute(value, axis, pairs)


def shifted(shard, axis, by):
    count = lax.axis_size(axis)
    pairs = [(i, i + by) for i in range(count) if 0 <= i + by < count]
    return lax.ppermute(shard, axis, pairs)


def window(array, shift_row, shift_col):
    inner_height = array.shape[-2] - 2
    inner_width = array.shape[-1] - 2
    return array[..., shift_row : shift_row + inner_height, shift_col : shift_col + inner_width]


def masked_laplacian(values, wet_mask):
    centre = window(values, 1, 1)
    running = jnp.zeros_like(centre)
    for shift_row, shift_col in ((0, 1), (2, 1), (1, 0), (1, 2)):
        running = running + window(wet_mask, shift_row, shift_col) * (
            window(values, shift_row, shift_col) - centre
        )
    return window(wet_mask, 1, 1) * running


def face_flux(speed_one, speed_two, tracer_one, tracer_two, wet_one, wet_two):
    return 0.5 * (speed_one + speed_two) * 0.5 * (tracer_one + tracer_two) * wet_one * wet_two


def baroclinic(padded):
    tracer = padded[0:2]
    wet_mask = padded[2]
    inner_tracer = tracer[..., 1:-1, 1:-1]
    inner_mask = wet_mask[..., 1:-1, 1:-1]
    east_speed = padded[3][..., 1:-1, 1:-1]
    north_speed = padded[4][..., 1:-1, 1:-1]
    lap_one = masked_laplacian(tracer, wet_mask)
    lap_two = masked_laplacian(lap_one, inner_mask)
    centre = window(inner_tracer, 1, 1)
    wet_centre = window(inner_mask, 1, 1)
    east_flux = face_flux(
        window(east_speed, 1, 1),
        window(east_speed, 1, 2),
        centre,
        window(inner_tracer, 1, 2),
        wet_centre,
        window(inner_mask, 1, 2),
    )
    west_flux = face_flux(
        window(east_speed, 1, 0),
        window(east_speed, 1, 1),
        window(inner_tracer, 1, 0),
        centre,
        window(inner_mask, 1, 0),
        wet_centre,
    )
    north_flux = face_flux(
        window(north_speed, 1, 1),
        window(north_speed, 2, 1),
        centre,
        window(inner_tracer, 2, 1),
        wet_centre,
        window(inner_mask, 2, 1),
    )
    south_flux = face_flux(
        window(north_speed, 0, 1),
        window(north_speed, 1, 1),
        window(inner_tracer, 0, 1),
        centre,
        window(inner_mask, 0, 1),
        wet_centre,
    )
    divergence = east_flux - west_flux + north_flux - south_flux
    return wet_centre * (centre - advection_rate * divergence - biharmonic_rate * lap_two)


def stencil_body(field, out_ref):
    height, width = field(2).shape
    row_count, col_count = out_ref.shape[2], out_ref.shape[3]

    def south(x):
        return pltpu.roll(x, 1, 0)

    def north(x):
        return pltpu.roll(x, height - 1, 0)

    def west(x):
        return pltpu.roll(x, 1, 1)

    def east(x):
        return pltpu.roll(x, width - 1, 1)

    shifts = (south, north, west, east)
    wet = field(2)
    wet_near = [shift(wet) for shift in shifts]

    def laplacian(values):
        running = None
        for shift, wet_n in zip(shifts, wet_near):
            term = wet_n * (shift(values) - values)
            running = term if running is None else running + term
        return wet * running

    east_speed = field(3)
    north_speed = field(4)
    east_mean = 0.5 * (east_speed + east(east_speed)) * 0.5
    north_mean = 0.5 * (north_speed + north(north_speed)) * 0.5
    east_pair = wet * wet_near[3]
    north_pair = wet * wet_near[1]
    for t in range(out_ref.shape[0]):
        tracer = field(t)
        lap_two = laplacian(laplacian(tracer))
        east_flux = east_mean * (tracer + east(tracer)) * east_pair
        north_flux = north_mean * (tracer + north(tracer)) * north_pair
        divergence = east_flux - west(east_flux) + north_flux - south(north_flux)
        result = wet * (tracer - advection_rate * divergence - biharmonic_rate * lap_two)
        out_ref[t, 0] = result[:row_count, :col_count]


def stencil_kernel(ext_ref, out_ref):
    stencil_body(lambda f: ext_ref[f, 0], out_ref)


def assembling_kernel(tracer_ref, wet_ref, east_ref, north_ref, cols_ref, rows_ref, out_ref, ext_ref):
    rows, cols = wet_ref.shape[1], wet_ref.shape[2]
    interiors = (
        tracer_ref[0, 0],
        tracer_ref[1, 0],
        wet_ref[0],
        east_ref[0].astype(jnp.float32),
        north_ref[0].astype(jnp.float32),
    )
    for f, interior in enumerate(interiors):
        ext_ref[f, 0:rows, 0:cols] = interior
        ext_ref[f, 0:rows, cols:] = cols_ref[f, 0]
        ext_ref[f, rows:, :] = rows_ref[f, 0]
    stencil_body(lambda f: ext_ref[f], out_ref)


def halo_pieces(tracers, wet_mask, east_velocity, north_velocity, fold_signs):
    rows, cols = wet_mask.shape[1], wet_mask.shape[2]
    width = -(-(cols + 4) // 128) * 128
    lead = wet_mask.shape[:1]
    lon_count = lax.axis_size("lon")
    lat_count = lax.axis_size("lat")

    def fields(index):
        return jnp.concatenate(
            [
                tracers[index],
                wet_mask[None][index],
                east_velocity[None][index].astype(jnp.float32),
                north_velocity[None][index].astype(jnp.float32),
            ],
            axis=0,
        )

    every = slice(None)
    east_halo = lax.ppermute(
        fields((every, every, every, slice(0, 2))),
        "lon",
        [(i, (i - 1) % lon_count) for i in range(lon_count)],
    )
    west_halo = lax.ppermute(
        fields((every, every, every, slice(cols - 2, cols))),
        "lon",
        [(i, (i + 1) % lon_count) for i in range(lon_count)],
    )
    halo_cols = jnp.concatenate(
        [east_halo, jnp.zeros((5,) + lead + (rows, width - cols - 4), jnp.float32), west_halo],
        axis=3,
    )

    def widened_rows(start):
        band = (every, every, slice(start, start + 2))
        return jnp.concatenate([fields(band), halo_cols[band]], axis=3)

    bottom = widened_rows(0)
    top = widened_rows(rows - 2)
    north_rows = lax.ppermute(bottom, "lat", [(j, j - 1) for j in range(1, lat_count)])
    south_rows = lax.ppermute(top, "lat", [(j, j + 1) for j in range(lat_count - 1)])
    mirrored = lax.ppermute(top, "lon", [(i, lon_count - 1 - i) for i in range(lon_count)])
    folded = jnp.roll(jnp.flip(mirrored, axis=(2, 3)), cols - width, axis=3) * fold_signs
    at_top = lax.axis_index("lat") == lat_count - 1
    north = jnp.where(at_top, folded, north_rows)
    halo_rows = jnp.concatenate(
        [north, jnp.zeros((5,) + lead + (4, width), jnp.float32), south_rows], axis=2
    )
    return halo_cols, halo_rows


def assembling_call(tracers, wet_mask, east_velocity, north_velocity, fold_signs):
    halo_cols, halo_rows = halo_pieces(tracers, wet_mask, east_velocity, north_velocity, fold_signs)
    tracer_count, level_count, rows, cols = tracers.shape
    width = cols + halo_cols.shape[3]
    height = rows + halo_rows.shape[2]
    level_block = pl.BlockSpec((1, rows, cols), lambda k: (k, 0, 0))
    return pl.pallas_call(
        assembling_kernel,
        grid=(level_count,),
        in_specs=[
            pl.BlockSpec((tracer_count, 1, rows, cols), lambda k: (0, k, 0, 0)),
            level_block,
            level_block,
            level_block,
            pl.BlockSpec((5, 1, rows, halo_cols.shape[3]), lambda k: (0, k, 0, 0)),
            pl.BlockSpec((5, 1, halo_rows.shape[2], width), lambda k: (0, k, 0, 0)),
        ],
        out_specs=pl.BlockSpec((tracer_count, 1, rows, cols), lambda k: (0, k, 0, 0)),
        out_shape=jax.ShapeDtypeStruct(tracers.shape, jnp.float32),
        scratch_shapes=[pltpu.VMEM((5, height, width), jnp.float32)],
    )(tracers, wet_mask, east_velocity, north_velocity, halo_cols, halo_rows)


def wrapped_layout(padded):
    rows = padded.shape[2] - 4
    cols = padded.shape[3] - 4
    height = -(-(rows + 4) // 8) * 8
    width = -(-(cols + 4) // 128) * 128
    lead = padded.shape[:2]
    by_rows = jnp.concatenate(
        [
            padded[:, :, 2 : rows + 4],
            jnp.zeros(lead + (height - rows - 4, padded.shape[3]), padded.dtype),
            padded[:, :, 0:2],
        ],
        axis=2,
    )
    return jnp.concatenate(
        [
            by_rows[..., 2 : cols + 4],
            jnp.zeros(lead + (height, width - cols - 4), padded.dtype),
            by_rows[..., 0:2],
        ],
        axis=3,
    )


def stencil_call(ext, rows, cols):
    tracer_count = 2
    level_count = ext.shape[1]
    height, width = ext.shape[2], ext.shape[3]
    return pl.pallas_call(
        stencil_kernel,
        grid=(level_count,),
        in_specs=[pl.BlockSpec((ext.shape[0], 1, height, width), lambda k: (0, k, 0, 0))],
        out_specs=pl.BlockSpec((tracer_count, 1, rows, cols), lambda k: (0, k, 0, 0)),
        out_shape=jax.ShapeDtypeStruct((tracer_count, level_count, rows, cols), jnp.float32),
    )(ext)


def mix_kernel(values_ref, wet_ref, diff_ref, forcing_ref, out_ref, source_ref, ratio_ref):
    level_count = wet_ref.shape[0]
    tracer_count = values_ref.shape[0]

    def coupling(k):
        return diff_ref[k].astype(jnp.float32) * wet_ref[k] * wet_ref[k - 1]

    below = coupling(1)
    upper = None
    reduced = [None] * tracer_count
    for k in range(level_count):
        above = below
        below = coupling(k + 1) if k + 1 < level_count else None
        if k == 0:
            diagonal = 1.0 + below
            divisor = diagonal
        elif below is None:
            diagonal = 1.0 + above
            divisor = diagonal + above * upper
        else:
            diagonal = 1.0 + above + below
            divisor = diagonal + above * upper
        if below is not None:
            upper = -below / divisor
            ratio_ref[k] = upper
        for t in range(tracer_count):
            if k == 0:
                source = values_ref[t, 0]
            else:
                source = values_ref[t, k] + above * reduced[t]
            reduced[t] = source / divisor
            out_ref[t, k] = reduced[t]
    result = reduced
    contrast = result[0] - result[1]
    for k in range(level_count - 2, -1, -1):
        ratio = ratio_ref[k]
        for t in range(tracer_count):
            result[t] = out_ref[t, k] - ratio * result[t]
            out_ref[t, k] = result[t]
        contrast = contrast + (result[0] - result[1])
    source_ref[...] = wet_ref[0] * (forcing_ref[...] + contrast / level_count)


def vertical_mix(values, wet_mask, diffusivity, forcing):
    tracer_count, level_count, row_count, col_count = values.shape
    rows = 16 if row_count % 16 == 0 else row_count
    return pl.pallas_call(
        mix_kernel,
        grid=(row_count // rows,),
        in_specs=[
            pl.BlockSpec((tracer_count, level_count, rows, col_count), lambda i: (0, 0, i, 0)),
            pl.BlockSpec((level_count, rows, col_count), lambda i: (0, i, 0)),
            pl.BlockSpec((level_count, rows, col_count), lambda i: (0, i, 0)),
            pl.BlockSpec((rows, col_count), lambda i: (i, 0)),
        ],
        out_specs=[
            pl.BlockSpec((tracer_count, level_count, rows, col_count), lambda i: (0, 0, i, 0)),
            pl.BlockSpec((rows, col_count), lambda i: (i, 0)),
        ],
        out_shape=[
            jax.ShapeDtypeStruct(values.shape, jnp.float32),
            jax.ShapeDtypeStruct((row_count, col_count), jnp.float32),
        ],
        scratch_shapes=[pltpu.VMEM((level_count - 1, rows, col_count), jnp.float32)],
    )(values, wet_mask, diffusivity, forcing)


def nine_point(padded, wet_surface, centre_weight):
    centre = window(padded, 1, 1)
    edges = (
        window(padded, 0, 1) + window(padded, 2, 1) + window(padded, 1, 0) + window(padded, 1, 2)
    )
    corners = (
        window(padded, 0, 0) + window(padded, 0, 2) + window(padded, 2, 0) + window(padded, 2, 2)
    )
    return wet_surface * (centre_weight * centre - edges - corner_weight * corners)


def wrapped_extend(stacked, fold_signs):
    rows, cols = stacked.shape[2], stacked.shape[3]
    height = -(-(rows + 4) // 8) * 8
    width = -(-(cols + 4) // 128) * 128
    lead = stacked.shape[:2]
    lon_count = lax.axis_size("lon")
    lat_count = lax.axis_size("lat")
    east_halo = lax.ppermute(
        stacked[..., :2], "lon", [(i, (i - 1) % lon_count) for i in range(lon_count)]
    )
    west_halo = lax.ppermute(
        stacked[..., cols - 2 :], "lon", [(i, (i + 1) % lon_count) for i in range(lon_count)]
    )
    widened = jnp.concatenate(
        [stacked, east_halo, jnp.zeros(lead + (rows, width - cols - 4), stacked.dtype), west_halo],
        axis=3,
    )
    north_rows = lax.ppermute(widened[:, :, :2], "lat", [(j, j - 1) for j in range(1, lat_count)])
    south_rows = lax.ppermute(
        widened[:, :, rows - 2 :], "lat", [(j, j + 1) for j in range(lat_count - 1)]
    )
    mirrored = lax.ppermute(
        widened[:, :, rows - 2 :], "lon", [(i, lon_count - 1 - i) for i in range(lon_count)]
    )
    folded = jnp.roll(jnp.flip(mirrored, axis=(2, 3)), cols - width, axis=3) * fold_signs
    at_top = lax.axis_index("lat") == lat_count - 1
    north = jnp.where(at_top, folded, north_rows)
    return jnp.concatenate(
        [widened, north, jnp.zeros(lead + (height - rows - 4, width), stacked.dtype), south_rows],
        axis=2,
    )


def clinic_extend(stacked, fold_signs):
    row_count = stacked.shape[2]
    widened = extended_2(stacked, (("lon", 3),), 2, True)
    extended = extended_2(widened, (("lat", 2),), 2, False)
    top_rows = widened[:, :, row_count - 2 :, :]
    for bit in range(lax.axis_size("lon").bit_length() - 1):
        top_rows = from_partner(top_rows, "lon", bit)
    northern = jnp.flip(top_rows, axis=(2, 3)) * fold_signs
    at_top = lax.axis_index("lat") == lax.axis_size("lat") - 1
    ghost_rows = jnp.where(at_top, northern, extended[:, :, row_count + 2 :, :])
    return jnp.concatenate([extended[:, :, : row_count + 2, :], ghost_rows], axis=2)


def strip_pad(surface_field):
    lon_index = lax.axis_index("lon")
    lon_count = lax.axis_size("lon")
    first_row = surface_field[0:1, :]
    last_row = surface_field[-1:, :]
    following = passed_along(first_row, "lon", -1)
    following_far = shifted(following, "lat", -1)
    preceding = passed_along(last_row, "lon", 1)
    preceding_far = shifted(preceding, "lat", 1)
    above_row = jnp.where(lon_index == lon_count - 1, following_far, following)
    below_row = jnp.where(lon_index == 0, preceding_far, preceding)
    top_strip = jnp.logical_and(
        lon_index == lon_count - 1, lax.axis_index("lat") == lax.axis_size("lat") - 1
    )
    above_row = jnp.where(top_strip, jnp.flip(last_row, axis=1), above_row)
    extended = jnp.concatenate([below_row, surface_field, above_row], axis=0)
    return jnp.concatenate([extended[:, -1:], extended, extended[:, :1]], axis=1)


def strip_pad_joined(surface_field):
    lon_count = lax.axis_size("lon")
    lat_count = lax.axis_size("lat")
    strip_count = lon_count * lat_count
    axes = ("lon", "lat")

    def device(strip):
        return (strip % lon_count) * lat_count + strip // lon_count

    first_row = surface_field[0:1, :]
    last_row = surface_field[-1:, :]
    above_row = lax.ppermute(
        first_row, axes, [(device(s + 1), device(s)) for s in range(strip_count - 1)]
    )
    below_row = lax.ppermute(
        last_row, axes, [(device(s - 1), device(s)) for s in range(1, strip_count)]
    )
    top_strip = jnp.logical_and(
        lax.axis_index("lon") == lon_count - 1, lax.axis_index("lat") == lat_count - 1
    )
    above_row = jnp.where(top_strip, jnp.flip(last_row, axis=1), above_row)
    extended = jnp.concatenate([below_row, surface_field, above_row], axis=0)
    return jnp.concatenate([extended[:, -1:], extended, extended[:, :1]], axis=1)


def butterfly_sum(value):
    for axis in ("lon", "lat"):
        count = lax.axis_size(axis)
        bit = 1
        while bit < count:
            value = value + lax.ppermute(value, axis, [(i, i ^ bit) for i in range(count)])
            bit <<= 1
    return value


def neighbour_rows(values):
    lon_count = lax.axis_size("lon")
    lat_count = lax.axis_size("lat")
    strip_count = lon_count * lat_count
    axes = ("lon", "lat")

    def device(strip):
        return (strip % lon_count) * lat_count + strip // lon_count

    above = lax.ppermute(
        values[:, 0:1, :], axes, [(device(s + 1), device(s)) for s in range(strip_count - 1)]
    )
    below = lax.ppermute(
        values[:, -1:, :], axes, [(device(s - 1), device(s)) for s in range(1, strip_count)]
    )
    return above, below


def strip_assemble(surface_field, above_row, below_row):
    top_strip = jnp.logical_and(
        lax.axis_index("lon") == lax.axis_size("lon") - 1,
        lax.axis_index("lat") == lax.axis_size("lat") - 1,
    )
    above_row = jnp.where(top_strip, jnp.flip(surface_field[-1:, :], axis=1), above_row)
    extended = jnp.concatenate([below_row, surface_field, above_row], axis=0)
    return jnp.concatenate([extended[:, -1:], extended, extended[:, :1]], axis=1)


def solve(surface_source, wet_surface, centre_weight):

    def precondition(residual, wet, weight):
        return wet * residual / weight

    def apply_operator(field, above, below):
        return nine_point(strip_assemble(field, above, below), wet_surface, centre_weight)

    rim_above, rim_below = neighbour_rows(jnp.stack([wet_surface, centre_weight, surface_source]))
    solution = jnp.zeros_like(surface_source)
    residual = surface_source
    resid_rims = [rim_above[2], rim_below[2]]
    weight_rims = [
        (rim[0], jnp.where(rim[1] == 0.0, 1.0, rim[1])) for rim in (rim_above, rim_below)
    ]
    precond = precondition(residual, wet_surface, centre_weight)
    direction = precond
    operator_image = apply_operator(
        direction,
        *[precondition(r, w, c) for r, (w, c) in zip(resid_rims, weight_rims)],
    )
    image_above, image_below = neighbour_rows(operator_image[None])
    image_rims = [image_above[0], image_below[0]]
    totals = butterfly_sum(
        jnp.stack([jnp.sum(residual * precond), jnp.sum(direction * operator_image)])
    )
    resid_dot, curvature = totals[0], totals[1]
    for iteration in range(ITERS):
        step_size = resid_dot / curvature
        solution = solution + step_size * direction
        if iteration + 1 < ITERS:
            residual = residual - step_size * operator_image
            resid_rims = [r - step_size * a for r, a in zip(resid_rims, image_rims)]
            precond = precondition(residual, wet_surface, centre_weight)
            precond_image = apply_operator(
                precond,
                *[precondition(r, w, c) for r, (w, c) in zip(resid_rims, weight_rims)],
            )
            if iteration + 2 < ITERS:
                fresh_above, fresh_below = neighbour_rows(precond_image[None])
                fresh_rims = [fresh_above[0], fresh_below[0]]
            totals = butterfly_sum(
                jnp.stack(
                    [
                        jnp.sum(residual * precond),
                        jnp.sum(precond * precond_image),
                        jnp.sum(precond * operator_image),
                    ]
                )
            )
            dot_next = totals[0]
            ratio = dot_next / resid_dot
            direction = precond + ratio * direction
            curvature = totals[1] + 2.0 * ratio * totals[2] + ratio * ratio * curvature
            operator_image = precond_image + ratio * operator_image
            if iteration + 2 < ITERS:
                image_rims = [f + ratio * a for f, a in zip(fresh_rims, image_rims)]
            resid_dot = dot_next
    return solution


def shards(
    tracers,
    east_velocity,
    north_velocity,
    vertical_diffusivity,
    depth_levels,
    ocean_blocks,
    forcing,
    surface_coupling,
):
    level_count = tracers.shape[1]
    row_count = tracers.shape[2]
    col_count = tracers.shape[3]
    ocean_cells = jnp.repeat(
        jnp.repeat(ocean_blocks, row_count // ocean_blocks.shape[0], axis=0),
        col_count // ocean_blocks.shape[1],
        axis=1,
    ).astype(jnp.float32)
    level_index = lax.broadcasted_iota(jnp.int32, (level_count, row_count, col_count), 0)
    wet_mask = jnp.where(
        level_index < depth_levels[None], ocean_cells[None], jnp.zeros_like(ocean_cells)[None]
    )
    relaid = lax.all_to_all(
        jnp.stack([wet_mask[0], 6.0 + surface_coupling]),
        "lon",
        split_axis=1,
        concat_axis=2,
        tiled=True,
    )
    fold_signs = jnp.array([1.0, 1.0, 1.0, -1.0, -1.0], jnp.float32).reshape(5, 1, 1, 1)
    provisional = assembling_call(tracers, wet_mask, east_velocity, north_velocity, fold_signs)
    new_tracers, surface_source = vertical_mix(
        provisional, wet_mask, vertical_diffusivity, forcing
    )
    wet_surface = wet_mask[0]
    centre_weight = 6.0 + surface_coupling
    strip_source = lax.all_to_all(surface_source, "lon", split_axis=0, concat_axis=1, tiled=True)
    strip_solution = solve(strip_source, relaid[0], relaid[1])
    solution = lax.all_to_all(strip_solution, "lon", split_axis=1, concat_axis=0, tiled=True)
    return (new_tracers, solution)


def solution(mesh):
    placed = (
        P(None, None, "lat", "lon"),
        P(None, "lat", "lon"),
        P(None, "lat", "lon"),
        P(None, "lat", "lon"),
        P("lat", "lon"),
        P("lat", "lon"),
        P("lat", "lon"),
        P("lat", "lon"),
    )
    return jax.shard_map(
        shards,
        mesh=mesh,
        in_specs=placed,
        out_specs=(P(None, None, "lat", "lon"), P("lat", "lon")),
        check_vma=False,
    )
```

```python
import jax
import jax.numpy as jnp
from jax import lax
from jax.sharding import PartitionSpec as P
from jax.experimental import pallas as pl
from jax.experimental.pallas import tpu as pltpu

ITERS = 3


advection_rate = 0.25
biharmonic_rate = 0.01
corner_weight = 0.5


def extended_2(block, sides, width, periodic):
    for axis, dim in sides:
        count = lax.axis_size(axis)
        forward = [(i, i + 1) for i in range(count - 1)]
        if periodic:
            forward.append((count - 1, 0))
        backward = [(target, source) for source, target in forward]
        low = lax.ppermute(
            lax.slice_in_dim(block, block.shape[dim] - width, None, axis=dim), axis, forward
        )
        high = lax.ppermute(lax.slice_in_dim(block, 0, width, axis=dim), axis, backward)
        block = jnp.concatenate([low, block, high], axis=dim)
    return block


def from_partner(block, axis, stride):
    count = lax.axis_size(axis)
    route = []
    for low in range(count):
        high = low | 1 << stride
        if high != low and high < count:
            route += [(low, high), (high, low)]
    return lax.ppermute(block, axis, route)


def passed_along(value, axis, steps):
    count = lax.axis_size(axis)
    pairs = [(source, (source + steps) % count) for source in range(count)]
    return lax.ppermute(value, axis, pairs)


def shifted(shard, axis, by):
    count = lax.axis_size(axis)
    pairs = [(i, i + by) for i in range(count) if 0 <= i + by < count]
    return lax.ppermute(shard, axis, pairs)


def window(array, shift_row, shift_col):
    inner_height = array.shape[-2] - 2
    inner_width = array.shape[-1] - 2
    return array[..., shift_row : shift_row + inner_height, shift_col : shift_col + inner_width]


def masked_laplacian(values, wet_mask):
    centre = window(values, 1, 1)
    running = jnp.zeros_like(centre)
    for shift_row, shift_col in ((0, 1), (2, 1), (1, 0), (1, 2)):
        running = running + window(wet_mask, shift_row, shift_col) * (
            window(values, shift_row, shift_col) - centre
        )
    return window(wet_mask, 1, 1) * running


def face_flux(speed_one, speed_two, tracer_one, tracer_two, wet_one, wet_two):
    return 0.5 * (speed_one + speed_two) * 0.5 * (tracer_one + tracer_two) * wet_one * wet_two


def baroclinic(padded):
    tracer = padded[0:2]
    wet_mask = padded[2]
    inner_tracer = tracer[..., 1:-1, 1:-1]
    inner_mask = wet_mask[..., 1:-1, 1:-1]
    east_speed = padded[3][..., 1:-1, 1:-1]
    north_speed = padded[4][..., 1:-1, 1:-1]
    lap_one = masked_laplacian(tracer, wet_mask)
    lap_two = masked_laplacian(lap_one, inner_mask)
    centre = window(inner_tracer, 1, 1)
    wet_centre = window(inner_mask, 1, 1)
    east_flux = face_flux(
        window(east_speed, 1, 1),
        window(east_speed, 1, 2),
        centre,
        window(inner_tracer, 1, 2),
        wet_centre,
        window(inner_mask, 1, 2),
    )
    west_flux = face_flux(
        window(east_speed, 1, 0),
        window(east_speed, 1, 1),
        window(inner_tracer, 1, 0),
        centre,
        window(inner_mask, 1, 0),
        wet_centre,
    )
    north_flux = face_flux(
        window(north_speed, 1, 1),
        window(north_speed, 2, 1),
        centre,
        window(inner_tracer, 2, 1),
        wet_centre,
        window(inner_mask, 2, 1),
    )
    south_flux = face_flux(
        window(north_speed, 0, 1),
        window(north_speed, 1, 1),
        window(inner_tracer, 0, 1),
        centre,
        window(inner_mask, 0, 1),
        wet_centre,
    )
    divergence = east_flux - west_flux + north_flux - south_flux
    return wet_centre * (centre - advection_rate * divergence - biharmonic_rate * lap_two)


def stencil_body(field, out_ref):
    height, width = field(2).shape
    row_count, col_count = out_ref.shape[2], out_ref.shape[3]

    def south(x):
        return pltpu.roll(x, 1, 0)

    def north(x):
        return pltpu.roll(x, height - 1, 0)

    def west(x):
        return pltpu.roll(x, 1, 1)

    def east(x):
        return pltpu.roll(x, width - 1, 1)

    shifts = (south, north, west, east)
    wet = field(2)
    wet_near = [shift(wet) for shift in shifts]

    def laplacian(values):
        running = None
        for shift, wet_n in zip(shifts, wet_near):
            term = wet_n * (shift(values) - values)
            running = term if running is None else running + term
        return wet * running

    east_speed = field(3)
    north_speed = field(4)
    east_mean = 0.5 * (east_speed + east(east_speed))
    north_mean = 0.5 * (north_speed + north(north_speed))
    for t in range(out_ref.shape[0]):
        tracer = field(t)
        lap_two = laplacian(laplacian(tracer))
        east_flux = east_mean * 0.5 * (tracer + east(tracer)) * wet * wet_near[3]
        north_flux = north_mean * 0.5 * (tracer + north(tracer)) * wet * wet_near[1]
        divergence = east_flux - west(east_flux) + north_flux - south(north_flux)
        result = wet * (tracer - advection_rate * divergence - biharmonic_rate * lap_two)
        out_ref[t, 0] = result[:row_count, :col_count]


def stencil_kernel(ext_ref, out_ref):
    stencil_body(lambda f: ext_ref[f, 0], out_ref)


def assembling_kernel(tracer_ref, wet_ref, east_ref, north_ref, cols_ref, rows_ref, out_ref, ext_ref):
    rows, cols = wet_ref.shape[1], wet_ref.shape[2]
    interiors = (
        tracer_ref[0, 0],
        tracer_ref[1, 0],
        wet_ref[0],
        east_ref[0].astype(jnp.float32),
        north_ref[0].astype(jnp.float32),
    )
    for f, interior in enumerate(interiors):
        ext_ref[f, 0:rows, 0:cols] = interior
        ext_ref[f, 0:rows, cols:] = cols_ref[f, 0]
        ext_ref[f, rows:, :] = rows_ref[f, 0]
    stencil_body(lambda f: ext_ref[f], out_ref)


def halo_pieces(tracers, wet_mask, east_velocity, north_velocity, fold_signs):
    rows, cols = wet_mask.shape[1], wet_mask.shape[2]
    width = -(-(cols + 4) // 128) * 128
    lead = wet_mask.shape[:1]
    lon_count = lax.axis_size("lon")
    lat_count = lax.axis_size("lat")

    def fields(index):
        return jnp.concatenate(
            [
                tracers[index],
                wet_mask[None][index],
                east_velocity[None][index].astype(jnp.float32),
                north_velocity[None][index].astype(jnp.float32),
            ],
            axis=0,
        )

    every = slice(None)
    east_halo = lax.ppermute(
        fields((every, every, every, slice(0, 2))),
        "lon",
        [(i, (i - 1) % lon_count) for i in range(lon_count)],
    )
    west_halo = lax.ppermute(
        fields((every, every, every, slice(cols - 2, cols))),
        "lon",
        [(i, (i + 1) % lon_count) for i in range(lon_count)],
    )
    halo_cols = jnp.concatenate(
        [east_halo, jnp.zeros((5,) + lead + (rows, width - cols - 4), jnp.float32), west_halo],
        axis=3,
    )

    def widened_rows(start):
        band = (every, every, slice(start, start + 2))
        return jnp.concatenate([fields(band), halo_cols[band]], axis=3)

    bottom = widened_rows(0)
    top = widened_rows(rows - 2)
    north_rows = lax.ppermute(bottom, "lat", [(j, j - 1) for j in range(1, lat_count)])
    south_rows = lax.ppermute(top, "lat", [(j, j + 1) for j in range(lat_count - 1)])
    mirrored = lax.ppermute(top, "lon", [(i, lon_count - 1 - i) for i in range(lon_count)])
    folded = jnp.roll(jnp.flip(mirrored, axis=(2, 3)), cols - width, axis=3) * fold_signs
    at_top = lax.axis_index("lat") == lat_count - 1
    north = jnp.where(at_top, folded, north_rows)
    halo_rows = jnp.concatenate(
        [north, jnp.zeros((5,) + lead + (4, width), jnp.float32), south_rows], axis=2
    )
    return halo_cols, halo_rows


def assembling_call(tracers, wet_mask, east_velocity, north_velocity, fold_signs):
    halo_cols, halo_rows = halo_pieces(tracers, wet_mask, east_velocity, north_velocity, fold_signs)
    tracer_count, level_count, rows, cols = tracers.shape
    width = cols + halo_cols.shape[3]
    height = rows + halo_rows.shape[2]
    level_block = pl.BlockSpec((1, rows, cols), lambda k: (k, 0, 0))
    return pl.pallas_call(
        assembling_kernel,
        grid=(level_count,),
        in_specs=[
            pl.BlockSpec((tracer_count, 1, rows, cols), lambda k: (0, k, 0, 0)),
            level_block,
            level_block,
            level_block,
            pl.BlockSpec((5, 1, rows, halo_cols.shape[3]), lambda k: (0, k, 0, 0)),
            pl.BlockSpec((5, 1, halo_rows.shape[2], width), lambda k: (0, k, 0, 0)),
        ],
        out_specs=pl.BlockSpec((tracer_count, 1, rows, cols), lambda k: (0, k, 0, 0)),
        out_shape=jax.ShapeDtypeStruct(tracers.shape, jnp.float32),
        scratch_shapes=[pltpu.VMEM((5, height, width), jnp.float32)],
    )(tracers, wet_mask, east_velocity, north_velocity, halo_cols, halo_rows)


def wrapped_layout(padded):
    rows = padded.shape[2] - 4
    cols = padded.shape[3] - 4
    height = -(-(rows + 4) // 8) * 8
    width = -(-(cols + 4) // 128) * 128
    lead = padded.shape[:2]
    by_rows = jnp.concatenate(
        [
            padded[:, :, 2 : rows + 4],
            jnp.zeros(lead + (height - rows - 4, padded.shape[3]), padded.dtype),
            padded[:, :, 0:2],
        ],
        axis=2,
    )
    return jnp.concatenate(
        [
            by_rows[..., 2 : cols + 4],
            jnp.zeros(lead + (height, width - cols - 4), padded.dtype),
            by_rows[..., 0:2],
        ],
        axis=3,
    )


def stencil_call(ext, rows, cols):
    tracer_count = 2
    level_count = ext.shape[1]
    height, width = ext.shape[2], ext.shape[3]
    return pl.pallas_call(
        stencil_kernel,
        grid=(level_count,),
        in_specs=[pl.BlockSpec((ext.shape[0], 1, height, width), lambda k: (0, k, 0, 0))],
        out_specs=pl.BlockSpec((tracer_count, 1, rows, cols), lambda k: (0, k, 0, 0)),
        out_shape=jax.ShapeDtypeStruct((tracer_count, level_count, rows, cols), jnp.float32),
    )(ext)


def mix_kernel(values_ref, wet_ref, diff_ref, forcing_ref, out_ref, source_ref, ratio_ref):
    level_count = wet_ref.shape[0]
    tracer_count = values_ref.shape[0]

    def coupling(k):
        return diff_ref[k].astype(jnp.float32) * wet_ref[k] * wet_ref[k - 1]

    below = coupling(1)
    upper = None
    reduced = [None] * tracer_count
    for k in range(level_count):
        above = below
        below = coupling(k + 1) if k + 1 < level_count else None
        if k == 0:
            diagonal = 1.0 + below
            divisor = diagonal
        elif below is None:
            diagonal = 1.0 + above
            divisor = diagonal + above * upper
        else:
            diagonal = 1.0 + above + below
            divisor = diagonal + above * upper
        if below is not None:
            upper = -below / divisor
            ratio_ref[k] = upper
        for t in range(tracer_count):
            if k == 0:
                source = values_ref[t, 0]
            else:
                source = values_ref[t, k] + above * reduced[t]
            reduced[t] = source / divisor
            out_ref[t, k] = reduced[t]
    result = reduced
    contrast = result[0] - result[1]
    for k in range(level_count - 2, -1, -1):
        ratio = ratio_ref[k]
        for t in range(tracer_count):
            result[t] = out_ref[t, k] - ratio * result[t]
            out_ref[t, k] = result[t]
        contrast = contrast + (result[0] - result[1])
    source_ref[...] = wet_ref[0] * (forcing_ref[...] + contrast / level_count)


def vertical_mix(values, wet_mask, diffusivity, forcing):
    tracer_count, level_count, row_count, col_count = values.shape
    rows = 32 if row_count % 32 == 0 else row_count
    return pl.pallas_call(
        mix_kernel,
        grid=(row_count // rows,),
        in_specs=[
            pl.BlockSpec((tracer_count, level_count, rows, col_count), lambda i: (0, 0, i, 0)),
            pl.BlockSpec((level_count, rows, col_count), lambda i: (0, i, 0)),
            pl.BlockSpec((level_count, rows, col_count), lambda i: (0, i, 0)),
            pl.BlockSpec((rows, col_count), lambda i: (i, 0)),
        ],
        out_specs=[
            pl.BlockSpec((tracer_count, level_count, rows, col_count), lambda i: (0, 0, i, 0)),
            pl.BlockSpec((rows, col_count), lambda i: (i, 0)),
        ],
        out_shape=[
            jax.ShapeDtypeStruct(values.shape, jnp.float32),
            jax.ShapeDtypeStruct((row_count, col_count), jnp.float32),
        ],
        scratch_shapes=[pltpu.VMEM((level_count - 1, rows, col_count), jnp.float32)],
    )(values, wet_mask, diffusivity, forcing)


def nine_point(padded, wet_surface, centre_weight):
    centre = window(padded, 1, 1)
    edges = (
        window(padded, 0, 1) + window(padded, 2, 1) + window(padded, 1, 0) + window(padded, 1, 2)
    )
    corners = (
        window(padded, 0, 0) + window(padded, 0, 2) + window(padded, 2, 0) + window(padded, 2, 2)
    )
    return wet_surface * (centre_weight * centre - edges - corner_weight * corners)


def wrapped_extend(stacked, fold_signs):
    rows, cols = stacked.shape[2], stacked.shape[3]
    height = -(-(rows + 4) // 8) * 8
    width = -(-(cols + 4) // 128) * 128
    lead = stacked.shape[:2]
    lon_count = lax.axis_size("lon")
    lat_count = lax.axis_size("lat")
    east_halo = lax.ppermute(
        stacked[..., :2], "lon", [(i, (i - 1) % lon_count) for i in range(lon_count)]
    )
    west_halo = lax.ppermute(
        stacked[..., cols - 2 :], "lon", [(i, (i + 1) % lon_count) for i in range(lon_count)]
    )
    widened = jnp.concatenate(
        [stacked, east_halo, jnp.zeros(lead + (rows, width - cols - 4), stacked.dtype), west_halo],
        axis=3,
    )
    north_rows = lax.ppermute(widened[:, :, :2], "lat", [(j, j - 1) for j in range(1, lat_count)])
    south_rows = lax.ppermute(
        widened[:, :, rows - 2 :], "lat", [(j, j + 1) for j in range(lat_count - 1)]
    )
    mirrored = lax.ppermute(
        widened[:, :, rows - 2 :], "lon", [(i, lon_count - 1 - i) for i in range(lon_count)]
    )
    folded = jnp.roll(jnp.flip(mirrored, axis=(2, 3)), cols - width, axis=3) * fold_signs
    at_top = lax.axis_index("lat") == lat_count - 1
    north = jnp.where(at_top, folded, north_rows)
    return jnp.concatenate(
        [widened, north, jnp.zeros(lead + (height - rows - 4, width), stacked.dtype), south_rows],
        axis=2,
    )


def clinic_extend(stacked, fold_signs):
    row_count = stacked.shape[2]
    widened = extended_2(stacked, (("lon", 3),), 2, True)
    extended = extended_2(widened, (("lat", 2),), 2, False)
    top_rows = widened[:, :, row_count - 2 :, :]
    for bit in range(lax.axis_size("lon").bit_length() - 1):
        top_rows = from_partner(top_rows, "lon", bit)
    northern = jnp.flip(top_rows, axis=(2, 3)) * fold_signs
    at_top = lax.axis_index("lat") == lax.axis_size("lat") - 1
    ghost_rows = jnp.where(at_top, northern, extended[:, :, row_count + 2 :, :])
    return jnp.concatenate([extended[:, :, : row_count + 2, :], ghost_rows], axis=2)


def strip_pad(surface_field):
    lon_index = lax.axis_index("lon")
    lon_count = lax.axis_size("lon")
    first_row = surface_field[0:1, :]
    last_row = surface_field[-1:, :]
    following = passed_along(first_row, "lon", -1)
    following_far = shifted(following, "lat", -1)
    preceding = passed_along(last_row, "lon", 1)
    preceding_far = shifted(preceding, "lat", 1)
    above_row = jnp.where(lon_index == lon_count - 1, following_far, following)
    below_row = jnp.where(lon_index == 0, preceding_far, preceding)
    top_strip = jnp.logical_and(
        lon_index == lon_count - 1, lax.axis_index("lat") == lax.axis_size("lat") - 1
    )
    above_row = jnp.where(top_strip, jnp.flip(last_row, axis=1), above_row)
    extended = jnp.concatenate([below_row, surface_field, above_row], axis=0)
    return jnp.concatenate([extended[:, -1:], extended, extended[:, :1]], axis=1)


def strip_pad_joined(surface_field):
    lon_count = lax.axis_size("lon")
    lat_count = lax.axis_size("lat")
    strip_count = lon_count * lat_count
    axes = ("lon", "lat")

    def device(strip):
        return (strip % lon_count) * lat_count + strip // lon_count

    first_row = surface_field[0:1, :]
    last_row = surface_field[-1:, :]
    above_row = lax.ppermute(
        first_row, axes, [(device(s + 1), device(s)) for s in range(strip_count - 1)]
    )
    below_row = lax.ppermute(
        last_row, axes, [(device(s - 1), device(s)) for s in range(1, strip_count)]
    )
    top_strip = jnp.logical_and(
        lax.axis_index("lon") == lon_count - 1, lax.axis_index("lat") == lat_count - 1
    )
    above_row = jnp.where(top_strip, jnp.flip(last_row, axis=1), above_row)
    extended = jnp.concatenate([below_row, surface_field, above_row], axis=0)
    return jnp.concatenate([extended[:, -1:], extended, extended[:, :1]], axis=1)


def butterfly_sum(value):
    for axis in ("lon", "lat"):
        count = lax.axis_size(axis)
        bit = 1
        while bit < count:
            value = value + lax.ppermute(value, axis, [(i, i ^ bit) for i in range(count)])
            bit <<= 1
    return value


def neighbour_rows(values):
    lon_count = lax.axis_size("lon")
    lat_count = lax.axis_size("lat")
    strip_count = lon_count * lat_count
    axes = ("lon", "lat")

    def device(strip):
        return (strip % lon_count) * lat_count + strip // lon_count

    above = lax.ppermute(
        values[:, 0:1, :], axes, [(device(s + 1), device(s)) for s in range(strip_count - 1)]
    )
    below = lax.ppermute(
        values[:, -1:, :], axes, [(device(s - 1), device(s)) for s in range(1, strip_count)]
    )
    return above, below


def strip_assemble(surface_field, above_row, below_row):
    top_strip = jnp.logical_and(
        lax.axis_index("lon") == lax.axis_size("lon") - 1,
        lax.axis_index("lat") == lax.axis_size("lat") - 1,
    )
    above_row = jnp.where(top_strip, jnp.flip(surface_field[-1:, :], axis=1), above_row)
    extended = jnp.concatenate([below_row, surface_field, above_row], axis=0)
    return jnp.concatenate([extended[:, -1:], extended, extended[:, :1]], axis=1)


def solve(surface_source, wet_surface, centre_weight):

    def precondition(residual, wet, weight):
        return wet * residual / weight

    def apply_operator(field, above, below):
        return nine_point(strip_assemble(field, above, below), wet_surface, centre_weight)

    rim_above, rim_below = neighbour_rows(jnp.stack([wet_surface, centre_weight, surface_source]))
    solution = jnp.zeros_like(surface_source)
    residual = surface_source
    resid_rims = [rim_above[2], rim_below[2]]
    weight_rims = [
        (rim[0], jnp.where(rim[1] == 0.0, 1.0, rim[1])) for rim in (rim_above, rim_below)
    ]
    precond = precondition(residual, wet_surface, centre_weight)
    direction = precond
    operator_image = apply_operator(
        direction,
        *[precondition(r, w, c) for r, (w, c) in zip(resid_rims, weight_rims)],
    )
    image_above, image_below = neighbour_rows(operator_image[None])
    image_rims = [image_above[0], image_below[0]]
    totals = butterfly_sum(
        jnp.stack([jnp.sum(residual * precond), jnp.sum(direction * operator_image)])
    )
    resid_dot, curvature = totals[0], totals[1]
    for iteration in range(ITERS):
        step_size = resid_dot / curvature
        solution = solution + step_size * direction
        if iteration + 1 < ITERS:
            residual = residual - step_size * operator_image
            resid_rims = [r - step_size * a for r, a in zip(resid_rims, image_rims)]
            precond = precondition(residual, wet_surface, centre_weight)
            precond_image = apply_operator(
                precond,
                *[precondition(r, w, c) for r, (w, c) in zip(resid_rims, weight_rims)],
            )
            if iteration + 2 < ITERS:
                fresh_above, fresh_below = neighbour_rows(precond_image[None])
                fresh_rims = [fresh_above[0], fresh_below[0]]
            totals = butterfly_sum(
                jnp.stack(
                    [
                        jnp.sum(residual * precond),
                        jnp.sum(precond * precond_image),
                        jnp.sum(precond * operator_image),
                    ]
                )
            )
            dot_next = totals[0]
            ratio = dot_next / resid_dot
            direction = precond + ratio * direction
            curvature = totals[1] + 2.0 * ratio * totals[2] + ratio * ratio * curvature
            operator_image = precond_image + ratio * operator_image
            if iteration + 2 < ITERS:
                image_rims = [f + ratio * a for f, a in zip(fresh_rims, image_rims)]
            resid_dot = dot_next
    return solution


def shards(
    tracers,
    east_velocity,
    north_velocity,
    vertical_diffusivity,
    depth_levels,
    ocean_blocks,
    forcing,
    surface_coupling,
):
    level_count = tracers.shape[1]
    row_count = tracers.shape[2]
    col_count = tracers.shape[3]
    ocean_cells = jnp.repeat(
        jnp.repeat(ocean_blocks, row_count // ocean_blocks.shape[0], axis=0),
        col_count // ocean_blocks.shape[1],
        axis=1,
    ).astype(jnp.float32)
    level_index = lax.broadcasted_iota(jnp.int32, (level_count, row_count, col_count), 0)
    wet_mask = jnp.where(
        level_index < depth_levels[None], ocean_cells[None], jnp.zeros_like(ocean_cells)[None]
    )
    relaid = lax.all_to_all(
        jnp.stack([wet_mask[0], 6.0 + surface_coupling]),
        "lon",
        split_axis=1,
        concat_axis=2,
        tiled=True,
    )
    fold_signs = jnp.array([1.0, 1.0, 1.0, -1.0, -1.0], jnp.float32).reshape(5, 1, 1, 1)
    provisional = assembling_call(tracers, wet_mask, east_velocity, north_velocity, fold_signs)
    new_tracers, surface_source = vertical_mix(
        provisional, wet_mask, vertical_diffusivity, forcing
    )
    wet_surface = wet_mask[0]
    centre_weight = 6.0 + surface_coupling
    strip_source = lax.all_to_all(surface_source, "lon", split_axis=0, concat_axis=1, tiled=True)
    strip_solution = solve(strip_source, relaid[0], relaid[1])
    solution = lax.all_to_all(strip_solution, "lon", split_axis=1, concat_axis=0, tiled=True)
    return (new_tracers, solution)


def solution(mesh):
    placed = (
        P(None, None, "lat", "lon"),
        P(None, "lat", "lon"),
        P(None, "lat", "lon"),
        P(None, "lat", "lon"),
        P("lat", "lon"),
        P("lat", "lon"),
        P("lat", "lon"),
        P("lat", "lon"),
    )
    return jax.shard_map(
        shards,
        mesh=mesh,
        in_specs=placed,
        out_specs=(P(None, None, "lat", "lon"), P("lat", "lon")),
        check_vma=False,
    )
```
